32 devices in a mesh: cells: 8 (over z, y), slab: 4 (over x, core).
Axes of the slice: x: 2, y: 2, z: 4, core: 2. Of those that a mesh axis runs over, the one named last changes fastest.
Arguments:
- grad: float32 [2, 2, 64, 8192], P(None, None, 'slab', 'cells'), may hold values from -6 to 6
- acc_block: float32 [2, 4, 64, 8192], P(None, None, 'slab', 'cells')
- mobility: float32 [2, 2, 64, 8192], P(None, None, 'slab', 'cells'), may hold values from 0.2 to 1.5
- store: float32 [2, 2, 64, 8192], P(None, None, 'slab', 'cells'), may hold values from 0.1 to 0.5
- trans_h: float32 [64, 8192], P('slab', 'cells'), may hold values from 0.3 to 3
- trans_v: float32 [64, 8192], P('slab', 'cells'), may hold values from 0.3 to 3
- fault_near: int32 [4, 16384], P('slab', 'cells'), may hold values from 0 to 16383
- fault_far: int32 [4, 16384], P('slab', 'cells'), may hold values from 0 to 16383
- fault_trans: float32 [4, 16384], P('slab', 'cells'), may hold values from 0.3 to 3
- fault_count: int32 [4, 8], P('slab', 'cells'), may hold values from 256 to 2048, as said below
- compl_cell: int32 [4, 1024], P('slab', 'cells'), may hold values from 0 to 16383
- compl_well: int32 [4, 1024], P('slab', 'cells'), may hold values from 0 to 15, as said below
- compl_wi: float32 [4, 1024], P('slab', 'cells'), may hold values from 0.5 to 5
Outputs:
- adjoint: float32 [2, 2, 64, 8192], P(None, None, 'slab', 'cells')
- res_history: float32 [2, 2], replicated
The draws below stay inside these ranges and needn't reach their ends.
Inputs may be any that keep to these rules, and one draw needn't show every extreme that they name: `fault_count`: slots past a pair's count are padding; in every draw some pair of column blocks c, c+1 with c < 7 holds exactly 2048 live slots; the count of the last column block is unused. `compl_well`: every well of a group has at least one completion on the group's device of slab 0.
All inputs are finite; a program needn't handle non-finite values.
Results may differ from the reference program's by a relative error of at most 0.0001.
Values sent between devices are 32-bit elements; how exact they have to be, the bound alone decides.
No kernel may reach another device: no remote copies, remote signals or barrier semaphores. Data moves between devices by JAX's collectives and lax.ppermute only.
A program may use at most 128 MiB of HBM per device.

```python
import math
import jax
import jax.numpy as jnp
from jax import lax

LAY_DEV = 16
COL_DEV = 1024
FAULTS = 2048
COMPL = 128
WELLS = 16
NSTEPS = 2
ITERS = 1
LAYERS = 64
COLS = 8192
FAULT_SLOTS = 16384
COMPL_SLOTS = 1024
N_CELLS = 8
N_SLAB = 4


def draw_acc_block(key, part):
    subkeys = jax.random.split(key, 4)
    shape_main = (NSTEPS, LAYERS, COLS)
    diag_first = jnp.exp(jax.random.uniform(subkeys[0], shape_main, jnp.float32, math.log(0.02), math.log(0.2)))
    diag_second = jnp.exp(jax.random.uniform(subkeys[1], shape_main, jnp.float32, math.log(0.02), math.log(0.2)))
    cross_first = jax.random.uniform(subkeys[2], shape_main, jnp.float32, -0.5, 0.5) * diag_first
    cross_second = jax.random.uniform(subkeys[3], shape_main, jnp.float32, -0.5, 0.5) * diag_second
    return jnp.stack([diag_first, cross_first, cross_second, diag_second], axis=1)


def draw_fault_count(key, part):
    subkeys = jax.random.split(key, 5)
    lowest = max(1, FAULTS // 8)
    first = jax.random.randint(subkeys[0], (N_SLAB, N_CELLS), lowest, FAULTS + 1)
    second = jax.random.randint(subkeys[1], (N_SLAB, N_CELLS), lowest, FAULTS + 1)
    third = jax.random.randint(subkeys[2], (N_SLAB, N_CELLS), lowest, FAULTS + 1)
    counts = jnp.minimum(jnp.minimum(first, second), third)
    spot_slab = jax.random.randint(subkeys[3], (), 0, N_SLAB)
    spot_block = jax.random.randint(subkeys[4], (), 0, N_CELLS - 1)
    slab_ids = jnp.arange(N_SLAB, dtype=jnp.int32)[:, None]
    block_ids = jnp.arange(N_CELLS, dtype=jnp.int32)[None, :]
    chosen = (slab_ids == spot_slab) & (block_ids == spot_block)
    return jnp.where(chosen, FAULTS, counts).astype(jnp.int32)


def draw_compl_well(key, part):
    numbers = jax.random.randint(key, (N_SLAB, N_CELLS, COMPL), 0, WELLS)
    slot_ids = jnp.arange(COMPL, dtype=jnp.int32)[None, None, :]
    slab_ids = jnp.arange(N_SLAB, dtype=jnp.int32)[:, None, None]
    numbers = jnp.where((slab_ids == 0) & (slot_ids < WELLS), slot_ids, numbers)
    return numbers.reshape(N_SLAB, N_CELLS * COMPL).astype(jnp.int32)


def with_ends(values, own_key, low, high):
    longest = values.shape.index(max(values.shape))
    spots = []
    for shift in (0, 1):
        where = [jax.random.randint(jax.random.fold_in(own_key, axis), (), 0, length) for axis, length in enumerate(values.shape)]
        where[longest] = (where[longest] + shift) % values.shape[longest]
        spots.append(tuple(where))
    return values.at[spots[0]].set(low).at[spots[1]].set(high)


def level_of(stream_key, extent, shards, low, high):
    factor_of, own = 1.0, jax.random.fold_in(stream_key, 6)
    for dim, parts in shards:
        steps = jnp.exp(jax.random.uniform(jax.random.fold_in(own, dim), (parts,), jnp.float32, low / len(shards), high / len(shards)))
        factor_of = factor_of * jnp.repeat(steps, extent[dim] // parts).reshape([-1 if axis == dim else 1 for axis in range(len(extent))])
    return factor_of


def centred(key, dims, deviation, bound, cuts=(), kind=jnp.bfloat16):
    array = deviation * jax.random.normal(key, dims, jnp.float32)
    if cuts:
        array = array * level_of(key, dims, cuts, -0.22, 0.18)
    return jnp.clip(array, -bound, bound).astype(kind)


def setup_inputs(seed: int = 0) -> dict:
    streams_of = jax.random.split(jax.random.key(seed), 14)
    return {
        "grad": centred(streams_of[0], (NSTEPS, 2, LAYERS, COLS), 1.0, 6.0, ((2, 4), (3, 8)), jnp.float32),
        "acc_block": draw_acc_block(jax.random.fold_in(streams_of[13], 71), 0),
        "mobility": jnp.clip(jnp.exp(math.log(1.5) - 2.014903 * jax.random.uniform(streams_of[2], (NSTEPS, 2, LAYERS, COLS), jnp.float32) ** level_of(streams_of[2], (NSTEPS, 2, LAYERS, COLS), ((2, 4), (3, 8)), -0.2, 0.2)), 0.2, 1.5),
        "store": jnp.clip(jnp.exp(math.log(0.5) - 1.609438 * jax.random.uniform(streams_of[3], (NSTEPS, 2, LAYERS, COLS), jnp.float32) ** level_of(streams_of[3], (NSTEPS, 2, LAYERS, COLS), ((2, 4), (3, 8)), -0.2, 0.2)), 0.1, 0.5),
        "trans_h": jnp.clip(jnp.exp(math.log(3.0) - 2.3025851 * jax.random.uniform(streams_of[4], (LAYERS, COLS), jnp.float32) ** level_of(streams_of[4], (LAYERS, COLS), ((0, 4), (1, 8)), -0.2, 0.2)), 0.3, 3.0),
        "trans_v": jnp.clip(jnp.exp(math.log(3.0) - 2.3025851 * jax.random.uniform(streams_of[5], (LAYERS, COLS), jnp.float32) ** level_of(streams_of[5], (LAYERS, COLS), ((0, 4), (1, 8)), -0.2, 0.2)), 0.3, 3.0),
        "fault_near": with_ends(jax.random.randint(streams_of[6], (N_SLAB, FAULT_SLOTS), 0, LAY_DEV * COL_DEV), jax.random.fold_in(streams_of[6], 1), 0, (LAY_DEV * COL_DEV) - 1).astype(jnp.int32),
        "fault_far": with_ends(jax.random.randint(streams_of[7], (N_SLAB, FAULT_SLOTS), 0, LAY_DEV * COL_DEV), jax.random.fold_in(streams_of[7], 1), 0, (LAY_DEV * COL_DEV) - 1).astype(jnp.int32),
        "fault_trans": jnp.clip(jnp.exp(math.log(3.0) - 2.3025851 * jax.random.uniform(streams_of[8], (N_SLAB, FAULT_SLOTS), jnp.float32) ** level_of(streams_of[8], (N_SLAB, FAULT_SLOTS), ((0, 4), (1, 8)), -0.2, 0.2)), 0.3, 3.0),
        "fault_count": draw_fault_count(jax.random.fold_in(streams_of[13], 71), 0),
        "compl_cell": with_ends(jax.random.randint(streams_of[10], (N_SLAB, COMPL_SLOTS), 0, LAY_DEV * COL_DEV), jax.random.fold_in(streams_of[10], 1), 0, (LAY_DEV * COL_DEV) - 1).astype(jnp.int32),
        "compl_well": draw_compl_well(jax.random.fold_in(streams_of[13], 71), 0),
        "compl_wi": jnp.clip(jnp.exp(math.log(5.0) - 2.3025851 * jax.random.uniform(streams_of[12], (N_SLAB, COMPL_SLOTS), jnp.float32) ** level_of(streams_of[12], (N_SLAB, COMPL_SLOTS), ((0, 4), (1, 8)), -0.2, 0.2)), 0.5, 5.0),
    }


def global_index(local_index, slab_ids, block_ids):
    layer_local = local_index // COL_DEV
    column_local = local_index % COL_DEV
    return ((slab_ids * LAY_DEV + layer_local) * COLS + block_ids * COL_DEV + column_local).astype(jnp.int32)

def reference(grad, acc_block, mobility, store, trans_h, trans_v, fault_near, fault_far, fault_trans, fault_count, compl_cell, compl_well, compl_wi):
    highest = lax.Precision.HIGHEST
    column_ids = lax.broadcasted_iota(jnp.int32, (LAYERS, COLS), 1)
    layer_ids = lax.broadcasted_iota(jnp.int32, (LAYERS, COLS), 0)
    zero_value = jnp.zeros((), trans_h.dtype)
    trans_east = jnp.where(column_ids == COLS - 1, zero_value, trans_h)
    trans_down = jnp.where(layer_ids == LAYERS - 1, zero_value, trans_v)
    trans_west = jnp.pad(trans_east[:, :-1], ((0, 0), (1, 0)))
    trans_up = jnp.pad(trans_down[:-1, :], ((1, 0), (0, 0)))
    face_total = trans_east + trans_west + trans_down + trans_up
    slab_ids = jnp.arange(N_SLAB, dtype=jnp.int32)[:, None, None]
    block_ids = jnp.arange(N_CELLS, dtype=jnp.int32)[None, :, None]
    near_global = global_index(fault_near.reshape(N_SLAB, N_CELLS, FAULTS), slab_ids, block_ids)[:, :-1].reshape(-1)
    far_global = global_index(fault_far.reshape(N_SLAB, N_CELLS, FAULTS), slab_ids, block_ids)[:, 1:].reshape(-1)
    slot_live = jnp.arange(FAULTS, dtype=jnp.int32)[None, None, :] < fault_count[:, :, None]
    fault_weight = jnp.where(slot_live, fault_trans.reshape(N_SLAB, N_CELLS, FAULTS), zero_value)[:, :-1].reshape(-1)
    well_cells = global_index(compl_cell.reshape(N_SLAB, N_CELLS, COMPL), slab_ids, block_ids)
    well_onehot = (compl_well.reshape(N_SLAB, N_CELLS, COMPL)[..., None] == jnp.arange(WELLS, dtype=jnp.int32)).astype(trans_h.dtype)
    well_index = compl_wi.reshape(N_SLAB, N_CELLS, COMPL)
    well_totals = jnp.einsum('sckw,sck->cw', well_onehot, well_index, precision=highest)

    def apply_operator(field, mobile, block):
        scaled = mobile * field
        east = jnp.pad(scaled[:, :, 1:], ((0, 0), (0, 0), (0, 1)))
        west = jnp.pad(scaled[:, :, :-1], ((0, 0), (0, 0), (1, 0)))
        below = jnp.pad(scaled[:, 1:, :], ((0, 0), (0, 1), (0, 0)))
        above = jnp.pad(scaled[:, :-1, :], ((0, 0), (1, 0), (0, 0)))
        laplace = trans_east * (scaled - east) + trans_west * (scaled - west) + trans_down * (scaled - below) + trans_up * (scaled - above)
        flat = scaled.reshape(2, -1)
        flux = fault_weight * (flat[:, near_global] - flat[:, far_global])
        fault_term = jnp.zeros_like(flat).at[:, near_global].add(flux).at[:, far_global].add(-flux).reshape(2, LAYERS, COLS)
        pressure = field[0].reshape(-1)
        values = pressure[well_cells]
        rates = jnp.einsum('sckw,sck->cw', well_onehot, well_index * values, precision=highest)
        back = jnp.einsum('sckw,cw->sck', well_onehot, rates / well_totals, precision=highest)
        well_term = jnp.zeros_like(pressure).at[well_cells.reshape(-1)].add((well_index * (values - back)).reshape(-1)).reshape(LAYERS, COLS)
        first = block[0] * field[0] + block[1] * field[1] + laplace[0] + fault_term[0] + well_term
        second = block[2] * field[0] + block[3] * field[1] + laplace[1] + fault_term[1]
        return jnp.stack([first, second])
    solutions = [None] * NSTEPS
    histories = [None] * NSTEPS
    adjoint_next = jnp.zeros((2, LAYERS, COLS), grad.dtype)
    for newton in range(NSTEPS - 1, -1, -1):
        block = acc_block[newton]
        mobile = mobility[newton]
        diag_first = block[0] + mobile[0] * face_total
        diag_second = block[3] + mobile[1] * face_total
        determinant = diag_first * diag_second - block[1] * block[2]
        inverse_aa = diag_second / determinant
        inverse_ab = -block[1] / determinant
        inverse_ba = -block[2] / determinant
        inverse_bb = diag_first / determinant
        residual = grad[newton] + store[newton] * adjoint_next
        solution = jnp.zeros_like(residual)
        history = []
        for sweep_index in range(ITERS):
            history.append(jnp.sqrt(jnp.sum(residual * residual)))
            precond = jnp.stack([inverse_aa * residual[0] + inverse_ab * residual[1], inverse_ba * residual[0] + inverse_bb * residual[1]])
            image = apply_operator(precond, mobile, block)
            alpha = jnp.sum(residual * image) / jnp.sum(image * image)
            solution = solution + alpha * precond
            residual = residual - alpha * image
        history.append(jnp.sqrt(jnp.sum(residual * residual)))
        solutions[newton] = solution
        histories[newton] = jnp.stack(history)
        adjoint_next = solution
    return (jnp.stack(solutions), jnp.stack(histories))
```

```python
import jax
import jax.numpy as jnp
from jax import lax
from jax.sharding import PartitionSpec as P

WELLS = 16
NSTEPS = 2


def shifted(value, axis, by):
    length = lax.axis_size(axis)
    pairs = [(i, i + by) for i in range(length) if 0 <= i + by < length]
    return lax.ppermute(value, axis, pairs)


def extended(block, sides, width):
    for axis, dim in sides:
        count = lax.axis_size(axis)
        forward = [(i, i + 1) for i in range(count - 1)]
        backward = [(target, source) for source, target in forward]
        low = lax.ppermute(
            lax.slice_in_dim(block, block.shape[dim] - width, None, axis=dim), axis, forward
        )
        high = lax.ppermute(lax.slice_in_dim(block, 0, width, axis=dim), axis, backward)
        block = jnp.concatenate([low, block, high], axis=dim)
    return block


def global_sum(values):
    stacked = lax.psum(jnp.stack(values), "slab")
    count = lax.axis_size("cells")
    if count & (count - 1):
        stacked = lax.psum(stacked, "cells")
    else:
        step = 1
        while step < count:
            stacked = stacked + lax.ppermute(
                stacked, "cells", [(i, i ^ step) for i in range(count)]
            )
            step *= 2
    return [stacked[i] for i in range(len(values))]


def split3(value):
    high = value.astype(jnp.bfloat16)
    rest = value - high.astype(value.dtype)
    middle = rest.astype(jnp.bfloat16)
    low = (rest - middle.astype(value.dtype)).astype(jnp.bfloat16)
    return high, middle, low


def onehot_dot(value, onehot, dims):
    total = None
    for piece in split3(value):
        part = lax.dot_general(
            piece, onehot, (dims, ((), ())), preferred_element_type=jnp.float32
        )
        total = part if total is None else total + part
    return total


def per_device(
    grad,
    acc_block,
    mobility,
    store,
    trans_h,
    trans_v,
    fault_near,
    fault_far,
    fault_trans,
    fault_count,
    compl_cell,
    compl_well,
    compl_wi,
):
    highest = lax.Precision.HIGHEST
    layer_count, column_count = trans_h.shape
    cells_size = lax.axis_size("cells")
    slab_size = lax.axis_size("slab")
    cells_place = lax.axis_index("cells")
    slab_place = lax.axis_index("slab")
    column_ids = lax.broadcasted_iota(jnp.int32, (layer_count, column_count), 1)
    layer_ids = lax.broadcasted_iota(jnp.int32, (layer_count, column_count), 0)
    zero_value = jnp.zeros((), trans_h.dtype)
    trans_east = jnp.where(
        (cells_place == cells_size - 1) & (column_ids == column_count - 1), zero_value, trans_h
    )
    trans_down = jnp.where(
        (slab_place == slab_size - 1) & (layer_ids == layer_count - 1), zero_value, trans_v
    )
    east_edge = shifted(trans_east[:, -1], "cells", 1)
    down_edge = shifted(trans_down[-1, :], "slab", 1)
    trans_west = jnp.concatenate([east_edge[:, None], trans_east[:, :-1]], axis=1)
    trans_up = jnp.concatenate([down_edge[None, :], trans_down[:-1, :]], axis=0)
    face_total = trans_east + trans_west + trans_down + trans_up

    column_iota = jnp.arange(column_count, dtype=jnp.int32)
    layer_iota = jnp.arange(layer_count, dtype=jnp.int32)

    def locate(cells):
        cells = cells.reshape(-1)
        onehot = (cells % column_count)[:, None] == column_iota[None, :]
        rows = (layer_iota[:, None] == (cells // column_count)[None, :]).astype(jnp.float32)
        return onehot.astype(jnp.bfloat16), rows

    def gather(field, where):
        onehot, rows = where
        parts = field.shape[0]
        flat = field.reshape(parts * layer_count, column_count)
        picked = onehot_dot(flat, onehot, ((1,), (1,)))
        picked = picked.reshape(parts, layer_count, -1) * rows[None]
        return jnp.sum(picked, axis=1)

    def scatter(values, where):
        onehot, rows = where
        parts = values.shape[0]
        spread = (values[:, None, :] * rows[None]).reshape(parts * layer_count, -1)
        placed = onehot_dot(spread, onehot, ((1,), (0,)))
        return placed.reshape(parts, layer_count, column_count)

    near_at = locate(fault_near)
    far_at = locate(fault_far)
    slot_count = fault_near.size
    slot_live = (jnp.arange(slot_count, dtype=jnp.int32) < fault_count.reshape(())) & (
        cells_place < cells_size - 1
    )
    weight_here = jnp.where(slot_live, fault_trans.reshape(-1), zero_value)
    weight_left = shifted(weight_here, "cells", 1)
    well_at = locate(compl_cell)
    well_index = compl_wi.reshape(-1)
    well_onehot = (
        compl_well.reshape(-1)[:, None] == jnp.arange(WELLS, dtype=jnp.int32)[None, :]
    ).astype(trans_h.dtype)
    well_totals = lax.psum(jnp.dot(well_index, well_onehot, precision=highest), "slab")
    solutions = [None] * NSTEPS
    histories = [None] * NSTEPS
    adjoint_next = jnp.zeros(grad.shape[1:], grad.dtype)
    for newton in range(NSTEPS - 1, -1, -1):
        block = acc_block[newton]
        mobile = mobility[newton]
        diag_first = block[0] + mobile[0] * face_total
        diag_second = block[3] + mobile[1] * face_total
        determinant = diag_first * diag_second - block[1] * block[2]
        inverse_aa = diag_second / determinant
        inverse_ab = -block[1] / determinant
        inverse_ba = -block[2] / determinant
        inverse_bb = diag_first / determinant
        residual = grad[newton] + store[newton] * adjoint_next
        history = []
        norm_square = jnp.sum(residual * residual)
        precond = jnp.stack(
            [
                inverse_aa * residual[0] + inverse_ab * residual[1],
                inverse_ba * residual[0] + inverse_bb * residual[1],
            ]
        )
        scaled = mobile * precond
        picks_near = gather(scaled, near_at)
        picks_far = gather(scaled, far_at)
        padded = extended(scaled, (("cells", 2), ("slab", 1)), 1)
        east = padded[:, 1:-1, 2:]
        west = padded[:, 1:-1, :-2]
        below = padded[:, 2:, 1:-1]
        above = padded[:, :-2, 1:-1]
        from_left = shifted(picks_near, "cells", 1)
        from_right = shifted(picks_far, "cells", -1)
        laplace = (
            trans_east * (scaled - east)
            + trans_west * (scaled - west)
            + trans_down * (scaled - below)
            + trans_up * (scaled - above)
        )
        flux_right = weight_here * (picks_near - from_right)
        flux_left = weight_left * (from_left - picks_far)
        fault_term = scatter(flux_right, near_at) - scatter(flux_left, far_at)
        pressure = precond[0]
        values = gather(pressure[None], well_at)[0]
        rates = lax.psum(jnp.dot(well_index * values, well_onehot, precision=highest), "slab")
        back = jnp.dot(well_onehot, rates / well_totals, precision=highest)
        well_term = scatter((well_index * (values - back))[None], well_at)[0]
        first = (
            block[0] * precond[0] + block[1] * precond[1] + laplace[0] + fault_term[0] + well_term
        )
        second = block[2] * precond[0] + block[3] * precond[1] + laplace[1] + fault_term[1]
        image = jnp.stack([first, second])
        along, energy = global_sum([jnp.sum(residual * image), jnp.sum(image * image)])
        alpha = along / energy
        solution = alpha * precond
        residual = residual - alpha * image
        closing = jnp.sum(residual * residual)
        history.append(norm_square)
        history.append(closing)
        solutions[newton] = solution
        histories[newton] = history
        adjoint_next = solution
    norms = global_sum([value for history in histories for value in history])
    norms = jnp.sqrt(jnp.stack(norms)).reshape(NSTEPS, 2)
    return (jnp.stack(solutions), norms)


def solution(mesh):
    placed = (
        P(None, None, "slab", "cells"),
        P(None, None, "slab", "cells"),
        P(None, None, "slab", "cells"),
        P(None, None, "slab", "cells"),
        P("slab", "cells"),
        P("slab", "cells"),
        P("slab", "cells"),
        P("slab", "cells"),
        P("slab", "cells"),
        P("slab", "cells"),
        P("slab", "cells"),
        P("slab", "cells"),
        P("slab", "cells"),
    )
    return jax.shard_map(
        per_device,
        mesh=mesh,
        in_specs=placed,
        out_specs=(P(None, None, "slab", "cells"), P()),
        check_vma=False,
    )
```

```python
import jax
import jax.numpy as jnp
from jax import lax
from jax.sharding import PartitionSpec as P

WELLS = 16
NSTEPS = 2


def shifted(value, axis, by):
    length = lax.axis_size(axis)
    pairs = [(i, i + by) for i in range(length) if 0 <= i + by < length]
    return lax.ppermute(value, axis, pairs)


def global_sum(values):
    stacked = lax.psum(jnp.stack(values), "slab")
    count = lax.axis_size("cells")
    if count & (count - 1):
        stacked = lax.psum(stacked, "cells")
    else:
        step = 1
        while step < count:
            stacked = stacked + lax.ppermute(
                stacked, "cells", [(i, i ^ step) for i in range(count)]
            )
            step *= 2
    return [stacked[i] for i in range(len(values))]


def split3(value):
    high = value.astype(jnp.bfloat16)
    rest = value - high.astype(value.dtype)
    middle = rest.astype(jnp.bfloat16)
    low = (rest - middle.astype(value.dtype)).astype(jnp.bfloat16)
    return high, middle, low


def onehot_dot(value, onehot, dims):
    total = None
    for piece in split3(value):
        part = lax.dot_general(
            piece, onehot, (dims, ((), ())), preferred_element_type=jnp.float32
        )
        total = part if total is None else total + part
    return total


def per_device(
    grad,
    acc_block,
    mobility,
    store,
    trans_h,
    trans_v,
    fault_near,
    fault_far,
    fault_trans,
    fault_count,
    compl_cell,
    compl_well,
    compl_wi,
):
    highest = lax.Precision.HIGHEST
    layer_count, column_count = trans_h.shape
    cells_size = lax.axis_size("cells")
    slab_size = lax.axis_size("slab")
    cells_place = lax.axis_index("cells")
    slab_place = lax.axis_index("slab")
    column_ids = lax.broadcasted_iota(jnp.int32, (layer_count, column_count), 1)
    layer_ids = lax.broadcasted_iota(jnp.int32, (layer_count, column_count), 0)
    zero_value = jnp.zeros((), trans_h.dtype)
    trans_east = jnp.where(
        (cells_place == cells_size - 1) & (column_ids == column_count - 1), zero_value, trans_h
    )
    trans_down = jnp.where(
        (slab_place == slab_size - 1) & (layer_ids == layer_count - 1), zero_value, trans_v
    )
    slot_count = fault_near.size
    slot_live = (jnp.arange(slot_count, dtype=jnp.int32) < fault_count.reshape(())) & (
        cells_place < cells_size - 1
    )
    weight_here = jnp.where(slot_live, fault_trans.reshape(-1), zero_value)
    from_left_setup = shifted(jnp.concatenate([trans_east[:, -1], weight_here]), "cells", 1)
    east_edge = from_left_setup[:layer_count]
    weight_left = from_left_setup[layer_count:]
    down_edge = shifted(trans_down[-1, :], "slab", 1)
    trans_west = jnp.concatenate([east_edge[:, None], trans_east[:, :-1]], axis=1)
    trans_up = jnp.concatenate([down_edge[None, :], trans_down[:-1, :]], axis=0)
    face_total = trans_east + trans_west + trans_down + trans_up

    column_iota = jnp.arange(column_count, dtype=jnp.int32)
    layer_iota = jnp.arange(layer_count, dtype=jnp.int32)

    def locate(cells):
        cells = cells.reshape(-1)
        onehot = (cells % column_count)[:, None] == column_iota[None, :]
        rows = (layer_iota[:, None] == (cells // column_count)[None, :]).astype(jnp.float32)
        return onehot.astype(jnp.bfloat16), rows

    def gather(field, where):
        onehot, rows = where
        parts = field.shape[0]
        flat = field.reshape(parts * layer_count, column_count)
        picked = onehot_dot(flat, onehot, ((1,), (1,)))
        picked = picked.reshape(parts, layer_count, -1) * rows[None]
        return jnp.sum(picked, axis=1)

    def scatter(values, where):
        onehot, rows = where
        parts = values.shape[0]
        spread = (values[:, None, :] * rows[None]).reshape(parts * layer_count, -1)
        placed = onehot_dot(spread, onehot, ((1,), (0,)))
        return placed.reshape(parts, layer_count, column_count)

    near_at = locate(fault_near)
    far_at = locate(fault_far)
    well_at = locate(compl_cell)
    well_index = compl_wi.reshape(-1)
    well_onehot = (
        compl_well.reshape(-1)[:, None] == jnp.arange(WELLS, dtype=jnp.int32)[None, :]
    ).astype(trans_h.dtype)

    def inverse_of(newton):
        block = acc_block[newton]
        mobile = mobility[newton]
        diag_first = block[0] + mobile[0] * face_total
        diag_second = block[3] + mobile[1] * face_total
        determinant = diag_first * diag_second - block[1] * block[2]
        return (
            diag_second / determinant,
            -block[1] / determinant,
            -block[2] / determinant,
            diag_first / determinant,
        )

    def precondition(inverse, residual):
        inverse_aa, inverse_ab, inverse_ba, inverse_bb = inverse
        return jnp.stack(
            [
                inverse_aa * residual[0] + inverse_ab * residual[1],
                inverse_ba * residual[0] + inverse_bb * residual[1],
            ]
        )

    def operator(fields, mobile, block):
        count = fields.shape[0]
        scaled = (mobile * fields).reshape(count * 2, layer_count, column_count)
        picks_near = gather(scaled, near_at)
        picks_far = gather(scaled, far_at)
        from_left = shifted(jnp.concatenate([scaled[:, :, -1], picks_near], axis=1), "cells", 1)
        from_right = shifted(jnp.concatenate([scaled[:, :, 0], picks_far], axis=1), "cells", -1)
        from_above = shifted(scaled[:, -1, :], "slab", 1)
        from_below = shifted(scaled[:, 0, :], "slab", -1)
        west = jnp.concatenate([from_left[:, :layer_count, None], scaled[:, :, :-1]], axis=2)
        east = jnp.concatenate([scaled[:, :, 1:], from_right[:, :layer_count, None]], axis=2)
        above = jnp.concatenate([from_above[:, None, :], scaled[:, :-1, :]], axis=1)
        below = jnp.concatenate([scaled[:, 1:, :], from_below[:, None, :]], axis=1)
        laplace = (
            trans_east * (scaled - east)
            + trans_west * (scaled - west)
            + trans_down * (scaled - below)
            + trans_up * (scaled - above)
        )
        flux_right = weight_here * (picks_near - from_right[:, layer_count:])
        flux_left = weight_left * (from_left[:, layer_count:] - picks_far)
        fault_term = scatter(flux_right, near_at) - scatter(flux_left, far_at)
        laplace = (laplace + fault_term).reshape(count, 2, layer_count, column_count)
        pressure = fields[:, 0]
        values = gather(pressure, well_at)
        local = jnp.concatenate(
            [
                jnp.dot(well_index, well_onehot, precision=highest)[None],
                jnp.dot(well_index * values, well_onehot, precision=highest),
            ]
        )
        summed = lax.psum(local, "slab")
        back = jnp.dot(summed[1:] / summed[0], well_onehot.T, precision=highest)
        well_term = scatter(well_index * (values - back), well_at)
        first = (
            block[:, 0] * fields[:, 0]
            + block[:, 1] * fields[:, 1]
            + laplace[:, 0]
            + well_term
        )
        second = block[:, 2] * fields[:, 0] + block[:, 3] * fields[:, 1] + laplace[:, 1]
        return jnp.stack([first, second], axis=1)

    inverse_last = inverse_of(1)
    inverse_first = inverse_of(0)
    grad_last = grad[1]
    grad_first = grad[0]
    z_last = precondition(inverse_last, grad_last)
    carried = store[0] * z_last
    fields = jnp.stack(
        [z_last, precondition(inverse_first, grad_first), precondition(inverse_first, carried)]
    )
    mobile = jnp.stack([mobility[1], mobility[0], mobility[0]])
    block = jnp.stack([acc_block[1], acc_block[0], acc_block[0]])
    images = operator(fields, mobile, block)
    image_last, direct, coupled = images[0], images[1], images[2]
    (
        along_last,
        energy_last,
        norm_last,
        grad_direct,
        grad_coupled,
        carried_direct,
        carried_coupled,
        direct_direct,
        direct_coupled,
        coupled_coupled,
    ) = global_sum(
        [
            jnp.sum(grad_last * image_last),
            jnp.sum(image_last * image_last),
            jnp.sum(grad_last * grad_last),
            jnp.sum(grad_first * direct),
            jnp.sum(grad_first * coupled),
            jnp.sum(carried * direct),
            jnp.sum(carried * coupled),
            jnp.sum(direct * direct),
            jnp.sum(direct * coupled),
            jnp.sum(coupled * coupled),
        ]
    )
    alpha_last = along_last / energy_last
    along_first = grad_direct + alpha_last * (grad_coupled + carried_direct) + (
        alpha_last * alpha_last
    ) * carried_coupled
    energy_first = direct_direct + (2.0 * alpha_last) * direct_coupled + (
        alpha_last * alpha_last
    ) * coupled_coupled
    alpha_first = along_first / energy_first
    solution_last = alpha_last * z_last
    residual_last = grad_last - alpha_last * image_last
    residual_first = grad_first + store[0] * solution_last
    solution_first = alpha_first * precondition(inverse_first, residual_first)
    image_first = direct + alpha_last * coupled
    closing_first = residual_first - alpha_first * image_first
    norm_first, end_first, end_last = global_sum(
        [
            jnp.sum(residual_first * residual_first),
            jnp.sum(closing_first * closing_first),
            jnp.sum(residual_last * residual_last),
        ]
    )
    norms = jnp.sqrt(jnp.stack([norm_first, end_first, norm_last, end_last])).reshape(2, 2)
    return (jnp.stack([solution_first, solution_last]), norms)


def solution(mesh):
    placed = (
        P(None, None, "slab", "cells"),
        P(None, None, "slab", "cells"),
        P(None, None, "slab", "cells"),
        P(None, None, "slab", "cells"),
        P("slab", "cells"),
        P("slab", "cells"),
        P("slab", "cells"),
        P("slab", "cells"),
        P("slab", "cells"),
        P("slab", "cells"),
        P("slab", "cells"),
        P("slab", "cells"),
        P("slab", "cells"),
    )
    return jax.shard_map(
        per_device,
        mesh=mesh,
        in_specs=placed,
        out_specs=(P(None, None, "slab", "cells"), P()),
        check_vma=False,
    )
```

```python
import jax
import jax.numpy as jnp
from jax import lax
from jax.sharding import PartitionSpec as P

WELLS = 16
NSTEPS = 2


def shifted(value, axis, by):
    length = lax.axis_size(axis)
    pairs = [(i, i + by) for i in range(length) if 0 <= i + by < length]
    return lax.ppermute(value, axis, pairs)


def stacked_sums(pairs):
    products = jnp.stack([(left * right).reshape(-1) for left, right in pairs])
    return jnp.sum(products, axis=1)


def global_sum(values):
    stacked = lax.psum(values, "slab")
    count = lax.axis_size("cells")
    if count & (count - 1):
        stacked = lax.psum(stacked, "cells")
    else:
        step = 1
        while step < count:
            stacked = stacked + lax.ppermute(
                stacked, "cells", [(i, i ^ step) for i in range(count)]
            )
            step *= 2
    return [stacked[i] for i in range(values.shape[0])]


def split3(value):
    high = value.astype(jnp.bfloat16)
    rest = value - high.astype(value.dtype)
    middle = rest.astype(jnp.bfloat16)
    low = (rest - middle.astype(value.dtype)).astype(jnp.bfloat16)
    return high, middle, low


def onehot_dot(value, onehot, dims):
    rows = value.shape[0]
    pieces = jnp.concatenate(split3(value), axis=0)
    part = lax.dot_general(
        pieces, onehot, (dims, ((), ())), preferred_element_type=jnp.float32
    )
    return (part[:rows] + part[rows : 2 * rows]) + part[2 * rows :]


def per_device(
    grad,
    acc_block,
    mobility,
    store,
    trans_h,
    trans_v,
    fault_near,
    fault_far,
    fault_trans,
    fault_count,
    compl_cell,
    compl_well,
    compl_wi,
):
    highest = lax.Precision.HIGHEST
    layer_count, column_count = trans_h.shape
    cells_size = lax.axis_size("cells")
    slab_size = lax.axis_size("slab")
    cells_place = lax.axis_index("cells")
    slab_place = lax.axis_index("slab")
    column_ids = lax.broadcasted_iota(jnp.int32, (layer_count, column_count), 1)
    layer_ids = lax.broadcasted_iota(jnp.int32, (layer_count, column_count), 0)
    zero_value = jnp.zeros((), trans_h.dtype)
    trans_east = jnp.where(
        (cells_place == cells_size - 1) & (column_ids == column_count - 1), zero_value, trans_h
    )
    trans_down = jnp.where(
        (slab_place == slab_size - 1) & (layer_ids == layer_count - 1), zero_value, trans_v
    )
    slot_count = fault_near.size
    slot_live = (jnp.arange(slot_count, dtype=jnp.int32) < fault_count.reshape(())) & (
        cells_place < cells_size - 1
    )
    weight_here = jnp.where(slot_live, fault_trans.reshape(-1), zero_value)
    from_left_setup = shifted(jnp.concatenate([trans_east[:, -1], weight_here]), "cells", 1)
    east_edge = from_left_setup[:layer_count]
    weight_left = from_left_setup[layer_count:]
    down_edge = shifted(trans_down[-1, :], "slab", 1)
    trans_west = jnp.concatenate([east_edge[:, None], trans_east[:, :-1]], axis=1)
    trans_up = jnp.concatenate([down_edge[None, :], trans_down[:-1, :]], axis=0)
    face_total = trans_east + trans_west + trans_down + trans_up

    column_iota = jnp.arange(column_count, dtype=jnp.int32)
    layer_iota = jnp.arange(layer_count, dtype=jnp.int32)

    def locate(cells):
        cells = cells.reshape(-1)
        onehot = (cells % column_count)[:, None] == column_iota[None, :]
        rows = (layer_iota[:, None] == (cells // column_count)[None, :]).astype(jnp.float32)
        return onehot.astype(jnp.bfloat16), rows

    def gather(field, where):
        onehot, rows = where
        parts = field.shape[0]
        flat = field.reshape(parts * layer_count, column_count)
        picked = onehot_dot(flat, onehot, ((1,), (1,)))
        picked = picked.reshape(parts, layer_count, -1) * rows[None]
        return jnp.sum(picked, axis=1)

    def scatter(values, where):
        onehot, rows = where
        parts = values.shape[0]
        spread = (values[:, None, :] * rows[None]).reshape(parts * layer_count, -1)
        placed = onehot_dot(spread, onehot, ((1,), (0,)))
        return placed.reshape(parts, layer_count, column_count)

    near_at = locate(fault_near)
    far_at = locate(fault_far)
    well_at = locate(compl_cell)
    well_index = compl_wi.reshape(-1)
    well_onehot = (
        compl_well.reshape(-1)[:, None] == jnp.arange(WELLS, dtype=jnp.int32)[None, :]
    ).astype(trans_h.dtype)

    def inverse_of(newton):
        block = acc_block[newton]
        mobile = mobility[newton]
        diag_first = block[0] + mobile[0] * face_total
        diag_second = block[3] + mobile[1] * face_total
        determinant = diag_first * diag_second - block[1] * block[2]
        return (
            diag_second / determinant,
            -block[1] / determinant,
            -block[2] / determinant,
            diag_first / determinant,
        )

    def precondition(inverse, residual):
        inverse_aa, inverse_ab, inverse_ba, inverse_bb = inverse
        return jnp.stack(
            [
                inverse_aa * residual[0] + inverse_ab * residual[1],
                inverse_ba * residual[0] + inverse_bb * residual[1],
            ]
        )

    def operator(fields, mobile, block):
        count = fields.shape[0]
        scaled = (mobile * fields).reshape(count * 2, layer_count, column_count)
        picks_near = gather(scaled, near_at)
        picks_far = gather(scaled, far_at)
        from_left = shifted(jnp.concatenate([scaled[:, :, -1], picks_near], axis=1), "cells", 1)
        from_right = shifted(jnp.concatenate([scaled[:, :, 0], picks_far], axis=1), "cells", -1)
        from_above = shifted(scaled[:, -1, :], "slab", 1)
        from_below = shifted(scaled[:, 0, :], "slab", -1)
        west = jnp.concatenate([from_left[:, :layer_count, None], scaled[:, :, :-1]], axis=2)
        east = jnp.concatenate([scaled[:, :, 1:], from_right[:, :layer_count, None]], axis=2)
        above = jnp.concatenate([from_above[:, None, :], scaled[:, :-1, :]], axis=1)
        below = jnp.concatenate([scaled[:, 1:, :], from_below[:, None, :]], axis=1)
        laplace = (
            trans_east * (scaled - east)
            + trans_west * (scaled - west)
            + trans_down * (scaled - below)
            + trans_up * (scaled - above)
        )
        flux_right = weight_here * (picks_near - from_right[:, layer_count:])
        flux_left = weight_left * (from_left[:, layer_count:] - picks_far)
        fault_term = scatter(flux_right, near_at) - scatter(flux_left, far_at)
        laplace = (laplace + fault_term).reshape(count, 2, layer_count, column_count)
        pressure = fields[:, 0]
        values = gather(pressure, well_at)
        local = jnp.concatenate(
            [
                jnp.dot(well_index, well_onehot, precision=highest)[None],
                jnp.dot(well_index * values, well_onehot, precision=highest),
            ]
        )
        summed = lax.psum(local, "slab")
        back = jnp.dot(summed[1:] / summed[0], well_onehot.T, precision=highest)
        well_term = scatter(well_index * (values - back), well_at)
        first = (
            block[:, 0] * fields[:, 0]
            + block[:, 1] * fields[:, 1]
            + laplace[:, 0]
            + well_term
        )
        second = block[:, 2] * fields[:, 0] + block[:, 3] * fields[:, 1] + laplace[:, 1]
        return jnp.stack([first, second], axis=1)

    inverse_last = inverse_of(1)
    inverse_first = inverse_of(0)
    grad_last = grad[1]
    grad_first = grad[0]
    z_last = precondition(inverse_last, grad_last)
    carried = store[0] * z_last
    fields = jnp.stack(
        [z_last, precondition(inverse_first, grad_first), precondition(inverse_first, carried)]
    )
    mobile = jnp.stack([mobility[1], mobility[0], mobility[0]])
    block = jnp.stack([acc_block[1], acc_block[0], acc_block[0]])
    images = operator(fields, mobile, block)
    image_last, direct, coupled = images[0], images[1], images[2]
    (
        along_last,
        energy_last,
        norm_last,
        grad_direct,
        grad_coupled,
        carried_direct,
        carried_coupled,
        direct_direct,
        direct_coupled,
        coupled_coupled,
    ) = global_sum(
        stacked_sums(
            [
                (grad_last, image_last),
                (image_last, image_last),
                (grad_last, grad_last),
                (grad_first, direct),
                (grad_first, coupled),
                (carried, direct),
                (carried, coupled),
                (direct, direct),
                (direct, coupled),
                (coupled, coupled),
            ]
        )
    )
    alpha_last = along_last / energy_last
    along_first = grad_direct + alpha_last * (grad_coupled + carried_direct) + (
        alpha_last * alpha_last
    ) * carried_coupled
    energy_first = direct_direct + (2.0 * alpha_last) * direct_coupled + (
        alpha_last * alpha_last
    ) * coupled_coupled
    alpha_first = along_first / energy_first
    solution_last = alpha_last * z_last
    residual_last = grad_last - alpha_last * image_last
    residual_first = grad_first + store[0] * solution_last
    solution_first = alpha_first * precondition(inverse_first, residual_first)
    image_first = direct + alpha_last * coupled
    closing_first = residual_first - alpha_first * image_first
    norm_first, end_first, end_last = global_sum(
        stacked_sums(
            [
                (residual_first, residual_first),
                (closing_first, closing_first),
                (residual_last, residual_last),
            ]
        )
    )
    norms = jnp.sqrt(jnp.stack([norm_first, end_first, norm_last, end_last])).reshape(2, 2)
    return (jnp.stack([solution_first, solution_last]), norms)


def solution(mesh):
    placed = (
        P(None, None, "slab", "cells"),
        P(None, None, "slab", "cells"),
        P(None, None, "slab", "cells"),
        P(None, None, "slab", "cells"),
        P("slab", "cells"),
        P("slab", "cells"),
        P("slab", "cells"),
        P("slab", "cells"),
        P("slab", "cells"),
        P("slab", "cells"),
        P("slab", "cells"),
        P("slab", "cells"),
        P("slab", "cells"),
    )
    return jax.shard_map(
        per_device,
        mesh=mesh,
        in_specs=placed,
        out_specs=(P(None, None, "slab", "cells"), P()),
        check_vma=False,
    )
```

```python
import jax
import jax.numpy as jnp
from jax import lax
from jax.sharding import PartitionSpec as P

WELLS = 16
NSTEPS = 2


def shifted(value, axis, by):
    length = lax.axis_size(axis)
    pairs = [(i, i + by) for i in range(length) if 0 <= i + by < length]
    return lax.ppermute(value, axis, pairs)


def stacked_sums(pairs):
    partial = jnp.stack([jnp.sum(left * right, axis=-2) for left, right in pairs])
    return jnp.sum(partial.reshape(len(pairs), -1), axis=1)


def butterfly(value, axis):
    count = lax.axis_size(axis)
    if count & (count - 1):
        return lax.psum(value, axis)
    step = 1
    while step < count:
        value = value + lax.ppermute(value, axis, [(i, i ^ step) for i in range(count)])
        step *= 2
    return value


def global_sum(values):
    stacked = lax.psum(values, "slab")
    count = lax.axis_size("cells")
    if count & (count - 1):
        stacked = lax.psum(stacked, "cells")
    else:
        step = 1
        while step < count:
            stacked = stacked + lax.ppermute(
                stacked, "cells", [(i, i ^ step) for i in range(count)]
            )
            step *= 2
    return [stacked[i] for i in range(values.shape[0])]


def split3(value):
    high = value.astype(jnp.bfloat16)
    rest = value - high.astype(value.dtype)
    middle = rest.astype(jnp.bfloat16)
    low = (rest - middle.astype(value.dtype)).astype(jnp.bfloat16)
    return high, middle, low


def onehot_dot(value, onehot, dims):
    rows = value.shape[0]
    pieces = jnp.concatenate(split3(value), axis=0)
    part = lax.dot_general(
        pieces, onehot, (dims, ((), ())), preferred_element_type=jnp.float32
    )
    return (part[:rows] + part[rows : 2 * rows]) + part[2 * rows :]


def per_device(
    grad,
    acc_block,
    mobility,
    store,
    trans_h,
    trans_v,
    fault_near,
    fault_far,
    fault_trans,
    fault_count,
    compl_cell,
    compl_well,
    compl_wi,
):
    highest = lax.Precision.HIGHEST
    layer_count, column_count = trans_h.shape
    cells_size = lax.axis_size("cells")
    slab_size = lax.axis_size("slab")
    cells_place = lax.axis_index("cells")
    slab_place = lax.axis_index("slab")
    column_ids = lax.broadcasted_iota(jnp.int32, (layer_count, column_count), 1)
    layer_ids = lax.broadcasted_iota(jnp.int32, (layer_count, column_count), 0)
    zero_value = jnp.zeros((), trans_h.dtype)
    trans_east = jnp.where(
        (cells_place == cells_size - 1) & (column_ids == column_count - 1), zero_value, trans_h
    )
    trans_down = jnp.where(
        (slab_place == slab_size - 1) & (layer_ids == layer_count - 1), zero_value, trans_v
    )
    slot_count = fault_near.size
    slot_live = (jnp.arange(slot_count, dtype=jnp.int32) < fault_count.reshape(())) & (
        cells_place < cells_size - 1
    )
    weight_here = jnp.where(slot_live, fault_trans.reshape(-1), zero_value)
    from_left_setup = shifted(jnp.concatenate([trans_east[:, -1], weight_here]), "cells", 1)
    east_edge = from_left_setup[:layer_count]
    weight_left = from_left_setup[layer_count:]
    down_edge = shifted(trans_down[-1, :], "slab", 1)
    trans_west = jnp.concatenate([east_edge[:, None], trans_east[:, :-1]], axis=1)
    trans_up = jnp.concatenate([down_edge[None, :], trans_down[:-1, :]], axis=0)
    face_total = trans_east + trans_west + trans_down + trans_up

    column_iota = jnp.arange(column_count, dtype=jnp.int32)
    layer_iota = jnp.arange(layer_count, dtype=jnp.int32)

    def locate(cells):
        cells = cells.reshape(-1)
        onehot = (cells % column_count)[:, None] == column_iota[None, :]
        rows = (layer_iota[:, None] == (cells // column_count)[None, :]).astype(jnp.float32)
        return onehot.astype(jnp.bfloat16), rows

    def gather(field, where):
        onehot, rows = where
        parts = field.shape[0]
        flat = field.reshape(parts * layer_count, column_count)
        picked = onehot_dot(flat, onehot, ((1,), (1,)))
        picked = picked.reshape(parts, layer_count, -1) * rows[None]
        return jnp.sum(picked, axis=1)

    def scatter(values, where):
        onehot, rows = where
        parts = values.shape[0]
        spread = (values[:, None, :] * rows[None]).reshape(parts * layer_count, -1)
        placed = onehot_dot(spread, onehot, ((1,), (0,)))
        return placed.reshape(parts, layer_count, column_count)

    near_at = locate(fault_near)
    far_at = locate(fault_far)
    well_at = locate(compl_cell)
    well_index = compl_wi.reshape(-1)
    well_onehot = (
        compl_well.reshape(-1)[:, None] == jnp.arange(WELLS, dtype=jnp.int32)[None, :]
    ).astype(trans_h.dtype)

    def inverse_of(newton):
        block = acc_block[newton]
        mobile = mobility[newton]
        diag_first = block[0] + mobile[0] * face_total
        diag_second = block[3] + mobile[1] * face_total
        determinant = diag_first * diag_second - block[1] * block[2]
        return (
            diag_second / determinant,
            -block[1] / determinant,
            -block[2] / determinant,
            diag_first / determinant,
        )

    def precondition(inverse, residual):
        inverse_aa, inverse_ab, inverse_ba, inverse_bb = inverse
        return jnp.stack(
            [
                inverse_aa * residual[0] + inverse_ab * residual[1],
                inverse_ba * residual[0] + inverse_bb * residual[1],
            ]
        )

    def operator(fields, mobile, block):
        count = fields.shape[0]
        scaled = (mobile * fields).reshape(count * 2, layer_count, column_count)
        picks_near = gather(scaled, near_at)
        picks_far = gather(scaled, far_at)
        from_left = shifted(jnp.concatenate([scaled[:, :, -1], picks_near], axis=1), "cells", 1)
        from_right = shifted(jnp.concatenate([scaled[:, :, 0], picks_far], axis=1), "cells", -1)
        from_above = shifted(scaled[:, -1, :], "slab", 1)
        from_below = shifted(scaled[:, 0, :], "slab", -1)
        west = jnp.concatenate([from_left[:, :layer_count, None], scaled[:, :, :-1]], axis=2)
        east = jnp.concatenate([scaled[:, :, 1:], from_right[:, :layer_count, None]], axis=2)
        above = jnp.concatenate([from_above[:, None, :], scaled[:, :-1, :]], axis=1)
        below = jnp.concatenate([scaled[:, 1:, :], from_below[:, None, :]], axis=1)
        laplace = (
            trans_east * (scaled - east)
            + trans_west * (scaled - west)
            + trans_down * (scaled - below)
            + trans_up * (scaled - above)
        )
        flux_right = weight_here * (picks_near - from_right[:, layer_count:])
        flux_left = weight_left * (from_left[:, layer_count:] - picks_far)
        fault_term = scatter(flux_right, near_at) - scatter(flux_left, far_at)
        laplace = (laplace + fault_term).reshape(count, 2, layer_count, column_count)
        pressure = fields[:, 0]
        values = gather(pressure, well_at)
        local = jnp.concatenate(
            [
                jnp.dot(well_index, well_onehot, precision=highest)[None],
                jnp.dot(well_index * values, well_onehot, precision=highest),
            ]
        )
        summed = butterfly(local, "slab")
        back = jnp.dot(summed[1:] / summed[0], well_onehot.T, precision=highest)
        well_term = scatter(well_index * (values - back), well_at)
        first = (
            block[:, 0] * fields[:, 0]
            + block[:, 1] * fields[:, 1]
            + laplace[:, 0]
            + well_term
        )
        second = block[:, 2] * fields[:, 0] + block[:, 3] * fields[:, 1] + laplace[:, 1]
        return jnp.stack([first, second], axis=1)

    inverse_last = inverse_of(1)
    inverse_first = inverse_of(0)
    grad_last = grad[1]
    grad_first = grad[0]
    z_last = precondition(inverse_last, grad_last)
    carried = store[0] * z_last
    fields = jnp.stack(
        [z_last, precondition(inverse_first, grad_first), precondition(inverse_first, carried)]
    )
    mobile = jnp.stack([mobility[1], mobility[0], mobility[0]])
    block = jnp.stack([acc_block[1], acc_block[0], acc_block[0]])
    images = operator(fields, mobile, block)
    image_last, direct, coupled = images[0], images[1], images[2]
    (
        along_last,
        energy_last,
        norm_last,
        grad_direct,
        grad_coupled,
        carried_direct,
        carried_coupled,
        direct_direct,
        direct_coupled,
        coupled_coupled,
    ) = global_sum(
        stacked_sums(
            [
                (grad_last, image_last),
                (image_last, image_last),
                (grad_last, grad_last),
                (grad_first, direct),
                (grad_first, coupled),
                (carried, direct),
                (carried, coupled),
                (direct, direct),
                (direct, coupled),
                (coupled, coupled),
            ]
        )
    )
    alpha_last = along_last / energy_last
    along_first = grad_direct + alpha_last * (grad_coupled + carried_direct) + (
        alpha_last * alpha_last
    ) * carried_coupled
    energy_first = direct_direct + (2.0 * alpha_last) * direct_coupled + (
        alpha_last * alpha_last
    ) * coupled_coupled
    alpha_first = along_first / energy_first
    solution_last = alpha_last * z_last
    residual_last = grad_last - alpha_last * image_last
    residual_first = grad_first + store[0] * solution_last
    solution_first = alpha_first * precondition(inverse_first, residual_first)
    image_first = direct + alpha_last * coupled
    closing_first = residual_first - alpha_first * image_first
    norm_first, end_first, end_last = global_sum(
        stacked_sums(
            [
                (residual_first, residual_first),
                (closing_first, closing_first),
                (residual_last, residual_last),
            ]
        )
    )
    norms = jnp.sqrt(jnp.stack([norm_first, end_first, norm_last, end_last])).reshape(2, 2)
    return (jnp.stack([solution_first, solution_last]), norms)


def solution(mesh):
    placed = (
        P(None, None, "slab", "cells"),
        P(None, None, "slab", "cells"),
        P(None, None, "slab", "cells"),
        P(None, None, "slab", "cells"),
        P("slab", "cells"),
        P("slab", "cells"),
        P("slab", "cells"),
        P("slab", "cells"),
        P("slab", "cells"),
        P("slab", "cells"),
        P("slab", "cells"),
        P("slab", "cells"),
        P("slab", "cells"),
    )
    return jax.shard_map(
        per_device,
        mesh=mesh,
        in_specs=placed,
        out_specs=(P(None, None, "slab", "cells"), P()),
        check_vma=False,
    )
```

```python
import jax
import jax.numpy as jnp
from jax import lax
from jax.sharding import PartitionSpec as P

WELLS = 16
NSTEPS = 2


def shifted(value, axis, by):
    length = lax.axis_size(axis)
    pairs = [(i, i + by) for i in range(length) if 0 <= i + by < length]
    return lax.ppermute(value, axis, pairs)


def stacked_sums(pairs):
    partial = jnp.stack([jnp.sum(left * right, axis=-2) for left, right in pairs])
    return jnp.sum(partial.reshape(len(pairs), -1), axis=1)


def butterfly(value, axis):
    count = lax.axis_size(axis)
    if count & (count - 1):
        return lax.psum(value, axis)
    step = 1
    while step < count:
        value = value + lax.ppermute(value, axis, [(i, i ^ step) for i in range(count)])
        step *= 2
    return value


def global_sum(values):
    axes = ("cells", "slab")
    count = lax.axis_size("cells") * lax.axis_size("slab")
    copies = jnp.broadcast_to(values[None], (count,) + values.shape)
    gathered = lax.all_to_all(copies, axes, 0, 0, tiled=True)
    stacked = jnp.sum(gathered, axis=0)
    return [stacked[i] for i in range(values.shape[0])]


def split3(value):
    high = value.astype(jnp.bfloat16)
    rest = value - high.astype(value.dtype)
    middle = rest.astype(jnp.bfloat16)
    low = (rest - middle.astype(value.dtype)).astype(jnp.bfloat16)
    return high, middle, low


def onehot_dot(value, onehot, dims):
    rows = value.shape[0]
    pieces = jnp.concatenate(split3(value), axis=0)
    part = lax.dot_general(
        pieces, onehot, (dims, ((), ())), preferred_element_type=jnp.float32
    )
    return (part[:rows] + part[rows : 2 * rows]) + part[2 * rows :]


def per_device(
    grad,
    acc_block,
    mobility,
    store,
    trans_h,
    trans_v,
    fault_near,
    fault_far,
    fault_trans,
    fault_count,
    compl_cell,
    compl_well,
    compl_wi,
):
    highest = lax.Precision.HIGHEST
    layer_count, column_count = trans_h.shape
    cells_size = lax.axis_size("cells")
    slab_size = lax.axis_size("slab")
    cells_place = lax.axis_index("cells")
    slab_place = lax.axis_index("slab")
    column_ids = lax.broadcasted_iota(jnp.int32, (layer_count, column_count), 1)
    layer_ids = lax.broadcasted_iota(jnp.int32, (layer_count, column_count), 0)
    zero_value = jnp.zeros((), trans_h.dtype)
    trans_east = jnp.where(
        (cells_place == cells_size - 1) & (column_ids == column_count - 1), zero_value, trans_h
    )
    trans_down = jnp.where(
        (slab_place == slab_size - 1) & (layer_ids == layer_count - 1), zero_value, trans_v
    )
    slot_count = fault_near.size
    slot_live = (jnp.arange(slot_count, dtype=jnp.int32) < fault_count.reshape(())) & (
        cells_place < cells_size - 1
    )
    weight_here = jnp.where(slot_live, fault_trans.reshape(-1), zero_value)
    from_left_setup = shifted(jnp.concatenate([trans_east[:, -1], weight_here]), "cells", 1)
    east_edge = from_left_setup[:layer_count]
    weight_left = from_left_setup[layer_count:]
    down_edge = shifted(trans_down[-1, :], "slab", 1)
    trans_west = jnp.concatenate([east_edge[:, None], trans_east[:, :-1]], axis=1)
    trans_up = jnp.concatenate([down_edge[None, :], trans_down[:-1, :]], axis=0)
    face_total = trans_east + trans_west + trans_down + trans_up

    column_iota = jnp.arange(column_count, dtype=jnp.int32)
    layer_iota = jnp.arange(layer_count, dtype=jnp.int32)

    def locate(cells):
        cells = cells.reshape(-1)
        onehot = (cells % column_count)[:, None] == column_iota[None, :]
        rows = (layer_iota[:, None] == (cells // column_count)[None, :]).astype(jnp.float32)
        return onehot.astype(jnp.bfloat16), rows

    def gather(field, where):
        onehot, rows = where
        parts = field.shape[0]
        flat = field.reshape(parts * layer_count, column_count)
        picked = onehot_dot(flat, onehot, ((1,), (1,)))
        picked = picked.reshape(parts, layer_count, -1) * rows[None]
        return jnp.sum(picked, axis=1)

    def scatter(values, where):
        onehot, rows = where
        parts = values.shape[0]
        spread = (values[:, None, :] * rows[None]).reshape(parts * layer_count, -1)
        placed = onehot_dot(spread, onehot, ((1,), (0,)))
        return placed.reshape(parts, layer_count, column_count)

    near_at = locate(fault_near)
    far_at = locate(fault_far)
    well_at = locate(compl_cell)
    well_index = compl_wi.reshape(-1)
    well_onehot = (
        compl_well.reshape(-1)[:, None] == jnp.arange(WELLS, dtype=jnp.int32)[None, :]
    ).astype(trans_h.dtype)

    def inverse_of(newton):
        block = acc_block[newton]
        mobile = mobility[newton]
        diag_first = block[0] + mobile[0] * face_total
        diag_second = block[3] + mobile[1] * face_total
        determinant = diag_first * diag_second - block[1] * block[2]
        return (
            diag_second / determinant,
            -block[1] / determinant,
            -block[2] / determinant,
            diag_first / determinant,
        )

    def precondition(inverse, residual):
        inverse_aa, inverse_ab, inverse_ba, inverse_bb = inverse
        return jnp.stack(
            [
                inverse_aa * residual[0] + inverse_ab * residual[1],
                inverse_ba * residual[0] + inverse_bb * residual[1],
            ]
        )

    def operator(fields, mobile, block):
        count = fields.shape[0]
        scaled = (mobile * fields).reshape(count * 2, layer_count, column_count)
        picks_near = gather(scaled, near_at)
        picks_far = gather(scaled, far_at)
        from_left = shifted(jnp.concatenate([scaled[:, :, -1], picks_near], axis=1), "cells", 1)
        from_right = shifted(jnp.concatenate([scaled[:, :, 0], picks_far], axis=1), "cells", -1)
        from_above = shifted(scaled[:, -1, :], "slab", 1)
        from_below = shifted(scaled[:, 0, :], "slab", -1)
        west = jnp.concatenate([from_left[:, :layer_count, None], scaled[:, :, :-1]], axis=2)
        east = jnp.concatenate([scaled[:, :, 1:], from_right[:, :layer_count, None]], axis=2)
        above = jnp.concatenate([from_above[:, None, :], scaled[:, :-1, :]], axis=1)
        below = jnp.concatenate([scaled[:, 1:, :], from_below[:, None, :]], axis=1)
        laplace = (
            trans_east * (scaled - east)
            + trans_west * (scaled - west)
            + trans_down * (scaled - below)
            + trans_up * (scaled - above)
        )
        flux_right = weight_here * (picks_near - from_right[:, layer_count:])
        flux_left = weight_left * (from_left[:, layer_count:] - picks_far)
        fault_term = scatter(flux_right, near_at) - scatter(flux_left, far_at)
        laplace = (laplace + fault_term).reshape(count, 2, layer_count, column_count)
        pressure = fields[:, 0]
        values = gather(pressure, well_at)
        local = jnp.concatenate(
            [
                jnp.dot(well_index, well_onehot, precision=highest)[None],
                jnp.dot(well_index * values, well_onehot, precision=highest),
            ]
        )
        summed = butterfly(local, "slab")
        back = jnp.dot(summed[1:] / summed[0], well_onehot.T, precision=highest)
        well_term = scatter(well_index * (values - back), well_at)
        first = (
            block[:, 0] * fields[:, 0]
            + block[:, 1] * fields[:, 1]
            + laplace[:, 0]
            + well_term
        )
        second = block[:, 2] * fields[:, 0] + block[:, 3] * fields[:, 1] + laplace[:, 1]
        return jnp.stack([first, second], axis=1)

    inverse_last = inverse_of(1)
    inverse_first = inverse_of(0)
    grad_last = grad[1]
    grad_first = grad[0]
    z_last = precondition(inverse_last, grad_last)
    carried = store[0] * z_last
    fields = jnp.stack(
        [z_last, precondition(inverse_first, grad_first), precondition(inverse_first, carried)]
    )
    mobile = jnp.stack([mobility[1], mobility[0], mobility[0]])
    block = jnp.stack([acc_block[1], acc_block[0], acc_block[0]])
    images = operator(fields, mobile, block)
    image_last, direct, coupled = images[0], images[1], images[2]
    (
        along_last,
        energy_last,
        norm_last,
        grad_direct,
        grad_coupled,
        carried_direct,
        carried_coupled,
        direct_direct,
        direct_coupled,
        coupled_coupled,
    ) = global_sum(
        stacked_sums(
            [
                (grad_last, image_last),
                (image_last, image_last),
                (grad_last, grad_last),
                (grad_first, direct),
                (grad_first, coupled),
                (carried, direct),
                (carried, coupled),
                (direct, direct),
                (direct, coupled),
                (coupled, coupled),
            ]
        )
    )
    alpha_last = along_last / energy_last
    along_first = grad_direct + alpha_last * (grad_coupled + carried_direct) + (
        alpha_last * alpha_last
    ) * carried_coupled
    energy_first = direct_direct + (2.0 * alpha_last) * direct_coupled + (
        alpha_last * alpha_last
    ) * coupled_coupled
    alpha_first = along_first / energy_first
    solution_last = alpha_last * z_last
    residual_last = grad_last - alpha_last * image_last
    residual_first = grad_first + store[0] * solution_last
    solution_first = alpha_first * precondition(inverse_first, residual_first)
    image_first = direct + alpha_last * coupled
    closing_first = residual_first - alpha_first * image_first
    norm_first, end_first, end_last = global_sum(
        stacked_sums(
            [
                (residual_first, residual_first),
                (closing_first, closing_first),
                (residual_last, residual_last),
            ]
        )
    )
    norms = jnp.sqrt(jnp.stack([norm_first, end_first, norm_last, end_last])).reshape(2, 2)
    return (jnp.stack([solution_first, solution_last]), norms)


def solution(mesh):
    placed = (
        P(None, None, "slab", "cells"),
        P(None, None, "slab", "cells"),
        P(None, None, "slab", "cells"),
        P(None, None, "slab", "cells"),
        P("slab", "cells"),
        P("slab", "cells"),
        P("slab", "cells"),
        P("slab", "cells"),
        P("slab", "cells"),
        P("slab", "cells"),
        P("slab", "cells"),
        P("slab", "cells"),
        P("slab", "cells"),
    )
    return jax.shard_map(
        per_device,
        mesh=mesh,
        in_specs=placed,
        out_specs=(P(None, None, "slab", "cells"), P()),
        check_vma=False,
    )
```

```python
import jax
import jax.numpy as jnp
from jax import lax
from jax.sharding import PartitionSpec as P

WELLS = 16
NSTEPS = 2


def shifted(value, axis, by):
    length = lax.axis_size(axis)
    pairs = [(i, i + by) for i in range(length) if 0 <= i + by < length]
    return lax.ppermute(value, axis, pairs)


def stacked_sums(pairs):
    partial = jnp.stack([jnp.sum(left * right, axis=-2) for left, right in pairs])
    return jnp.sum(partial.reshape(len(pairs), -1), axis=1)


def butterfly(value, axis):
    count = lax.axis_size(axis)
    if count & (count - 1):
        return lax.psum(value, axis)
    step = 1
    while step < count:
        value = value + lax.ppermute(value, axis, [(i, i ^ step) for i in range(count)])
        step *= 2
    return value


def global_sum(values):
    axes = ("cells", "slab")
    count = lax.axis_size("cells") * lax.axis_size("slab")
    copies = jnp.broadcast_to(values[None], (count,) + values.shape)
    gathered = lax.all_to_all(copies, axes, 0, 0, tiled=True)
    return jnp.sum(gathered, axis=0)


def split3(value):
    high = value.astype(jnp.bfloat16)
    rest = value - high.astype(value.dtype)
    middle = rest.astype(jnp.bfloat16)
    low = (rest - middle.astype(value.dtype)).astype(jnp.bfloat16)
    return high, middle, low


def onehot_dot(value, onehot, dims):
    rows = value.shape[0]
    pieces = jnp.concatenate(split3(value), axis=0)
    part = lax.dot_general(
        pieces, onehot, (dims, ((), ())), preferred_element_type=jnp.float32
    )
    return (part[:rows] + part[rows : 2 * rows]) + part[2 * rows :]


def per_device(
    grad,
    acc_block,
    mobility,
    store,
    trans_h,
    trans_v,
    fault_near,
    fault_far,
    fault_trans,
    fault_count,
    compl_cell,
    compl_well,
    compl_wi,
):
    highest = lax.Precision.HIGHEST
    layer_count, column_count = trans_h.shape
    cells_size = lax.axis_size("cells")
    slab_size = lax.axis_size("slab")
    cells_place = lax.axis_index("cells")
    slab_place = lax.axis_index("slab")
    column_ids = lax.broadcasted_iota(jnp.int32, (layer_count, column_count), 1)
    layer_ids = lax.broadcasted_iota(jnp.int32, (layer_count, column_count), 0)
    zero_value = jnp.zeros((), trans_h.dtype)
    trans_east = jnp.where(
        (cells_place == cells_size - 1) & (column_ids == column_count - 1), zero_value, trans_h
    )
    trans_down = jnp.where(
        (slab_place == slab_size - 1) & (layer_ids == layer_count - 1), zero_value, trans_v
    )
    slot_count = fault_near.size
    slot_live = (jnp.arange(slot_count, dtype=jnp.int32) < fault_count.reshape(())) & (
        cells_place < cells_size - 1
    )
    weight_here = jnp.where(slot_live, fault_trans.reshape(-1), zero_value)
    from_left_setup = shifted(jnp.concatenate([trans_east[:, -1], weight_here]), "cells", 1)
    east_edge = from_left_setup[:layer_count]
    weight_left = from_left_setup[layer_count:]
    down_edge = shifted(trans_down[-1, :], "slab", 1)
    trans_west = jnp.concatenate([east_edge[:, None], trans_east[:, :-1]], axis=1)
    trans_up = jnp.concatenate([down_edge[None, :], trans_down[:-1, :]], axis=0)
    face_total = trans_east + trans_west + trans_down + trans_up

    column_iota = jnp.arange(column_count, dtype=jnp.int32)
    layer_iota = jnp.arange(layer_count, dtype=jnp.int32)

    def locate(cells):
        cells = cells.reshape(-1)
        onehot = (cells % column_count)[:, None] == column_iota[None, :]
        rows = (layer_iota[:, None] == (cells // column_count)[None, :]).astype(jnp.float32)
        return onehot.astype(jnp.bfloat16), rows

    def gather(field, where):
        onehot, rows = where
        parts = field.shape[0]
        flat = field.reshape(parts * layer_count, column_count)
        picked = onehot_dot(flat, onehot, ((1,), (1,)))
        picked = picked.reshape(parts, layer_count, -1) * rows[None]
        return jnp.sum(picked, axis=1)

    def scatter(values, where):
        onehot, rows = where
        parts = values.shape[0]
        spread = (values[:, None, :] * rows[None]).reshape(parts * layer_count, -1)
        placed = onehot_dot(spread, onehot, ((1,), (0,)))
        return placed.reshape(parts, layer_count, column_count)

    near_at = locate(fault_near)
    far_at = locate(fault_far)
    well_at = locate(compl_cell)
    well_index = compl_wi.reshape(-1)
    well_onehot = (
        compl_well.reshape(-1)[:, None] == jnp.arange(WELLS, dtype=jnp.int32)[None, :]
    ).astype(trans_h.dtype)

    def inverse_of(newton):
        block = acc_block[newton]
        mobile = mobility[newton]
        diag_first = block[0] + mobile[0] * face_total
        diag_second = block[3] + mobile[1] * face_total
        determinant = diag_first * diag_second - block[1] * block[2]
        return (
            diag_second / determinant,
            -block[1] / determinant,
            -block[2] / determinant,
            diag_first / determinant,
        )

    def precondition(inverse, residual):
        inverse_aa, inverse_ab, inverse_ba, inverse_bb = inverse
        return jnp.stack(
            [
                inverse_aa * residual[0] + inverse_ab * residual[1],
                inverse_ba * residual[0] + inverse_bb * residual[1],
            ]
        )

    def operator(fields, mobile, block):
        count = fields.shape[0]
        scaled = (mobile * fields).reshape(count * 2, layer_count, column_count)
        picks_near = gather(scaled, near_at)
        picks_far = gather(scaled, far_at)
        from_left = shifted(jnp.concatenate([scaled[:, :, -1], picks_near], axis=1), "cells", 1)
        from_right = shifted(jnp.concatenate([scaled[:, :, 0], picks_far], axis=1), "cells", -1)
        from_above = shifted(scaled[:, -1, :], "slab", 1)
        from_below = shifted(scaled[:, 0, :], "slab", -1)
        west = jnp.concatenate([from_left[:, :layer_count, None], scaled[:, :, :-1]], axis=2)
        east = jnp.concatenate([scaled[:, :, 1:], from_right[:, :layer_count, None]], axis=2)
        above = jnp.concatenate([from_above[:, None, :], scaled[:, :-1, :]], axis=1)
        below = jnp.concatenate([scaled[:, 1:, :], from_below[:, None, :]], axis=1)
        laplace = (
            trans_east * (scaled - east)
            + trans_west * (scaled - west)
            + trans_down * (scaled - below)
            + trans_up * (scaled - above)
        )
        flux_right = weight_here * (picks_near - from_right[:, layer_count:])
        flux_left = weight_left * (from_left[:, layer_count:] - picks_far)
        fault_term = scatter(flux_right, near_at) - scatter(flux_left, far_at)
        laplace = (laplace + fault_term).reshape(count, 2, layer_count, column_count)
        pressure = fields[:, 0]
        values = gather(pressure, well_at)
        local = jnp.concatenate(
            [
                jnp.dot(well_index, well_onehot, precision=highest)[None],
                jnp.dot(well_index * values, well_onehot, precision=highest),
            ]
        )
        summed = butterfly(local, "slab")
        back = jnp.dot(summed[1:] / summed[0], well_onehot.T, precision=highest)
        well_term = scatter(well_index * (values - back), well_at)
        first = (
            block[:, 0] * fields[:, 0]
            + block[:, 1] * fields[:, 1]
            + laplace[:, 0]
            + well_term
        )
        second = block[:, 2] * fields[:, 0] + block[:, 3] * fields[:, 1] + laplace[:, 1]
        return jnp.stack([first, second], axis=1)

    inverse_last = inverse_of(1)
    inverse_first = inverse_of(0)
    grad_last = grad[1]
    grad_first = grad[0]
    z_last = precondition(inverse_last, grad_last)
    carried = store[0] * z_last
    fields = jnp.stack(
        [z_last, precondition(inverse_first, grad_first), precondition(inverse_first, carried)]
    )
    mobile = jnp.stack([mobility[1], mobility[0], mobility[0]])
    block = jnp.stack([acc_block[1], acc_block[0], acc_block[0]])
    images = operator(fields, mobile, block)
    image_last, direct, coupled = images[0], images[1], images[2]
    first_sums = global_sum(
        stacked_sums(
            [
                (grad_last, image_last),
                (image_last, image_last),
                (grad_last, grad_last),
                (grad_first, direct),
                (grad_first, coupled),
                (carried, direct),
                (carried, coupled),
                (direct, direct),
                (direct, coupled),
                (coupled, coupled),
            ]
        )
    )
    lanes = lax.optimization_barrier(
        jnp.broadcast_to(first_sums[:, None], (first_sums.shape[0], column_count))
    )
    (
        along_last,
        energy_last,
        norm_last,
        grad_direct,
        grad_coupled,
        carried_direct,
        carried_coupled,
        direct_direct,
        direct_coupled,
        coupled_coupled,
    ) = [lanes[i] for i in range(first_sums.shape[0])]
    alpha_last = along_last / energy_last
    along_first = grad_direct + alpha_last * (grad_coupled + carried_direct) + (
        alpha_last * alpha_last
    ) * carried_coupled
    energy_first = direct_direct + (2.0 * alpha_last) * direct_coupled + (
        alpha_last * alpha_last
    ) * coupled_coupled
    alpha_first = along_first / energy_first
    solution_last = alpha_last * z_last
    residual_last = grad_last - alpha_last * image_last
    residual_first = grad_first + store[0] * solution_last
    solution_first = alpha_first * precondition(inverse_first, residual_first)
    image_first = direct + alpha_last * coupled
    closing_first = residual_first - alpha_first * image_first
    second_sums = global_sum(
        stacked_sums(
            [
                (residual_first, residual_first),
                (closing_first, closing_first),
                (residual_last, residual_last),
            ]
        )
    )
    norms = jnp.sqrt(
        jnp.concatenate([second_sums[0:2], first_sums[2:3], second_sums[2:3]])
    ).reshape(2, 2)
    return (jnp.stack([solution_first, solution_last]), norms)


def solution(mesh):
    placed = (
        P(None, None, "slab", "cells"),
        P(None, None, "slab", "cells"),
        P(None, None, "slab", "cells"),
        P(None, None, "slab", "cells"),
        P("slab", "cells"),
        P("slab", "cells"),
        P("slab", "cells"),
        P("slab", "cells"),
        P("slab", "cells"),
        P("slab", "cells"),
        P("slab", "cells"),
        P("slab", "cells"),
        P("slab", "cells"),
    )
    return jax.shard_map(
        per_device,
        mesh=mesh,
        in_specs=placed,
        out_specs=(P(None, None, "slab", "cells"), P()),
        check_vma=False,
    )
```

```python
import jax
import jax.numpy as jnp
from jax import lax
from jax.sharding import PartitionSpec as P

WELLS = 16
NSTEPS = 2


def shifted(value, axis, by):
    length = lax.axis_size(axis)
    pairs = [(i, i + by) for i in range(length) if 0 <= i + by < length]
    return lax.ppermute(value, axis, pairs)


def stacked_sums(pairs):
    partial = jnp.stack([jnp.sum(left * right, axis=-2) for left, right in pairs])
    return jnp.sum(partial.reshape(len(pairs), -1), axis=1)


def butterfly(value, axis):
    count = lax.axis_size(axis)
    if count & (count - 1):
        return lax.psum(value, axis)
    step = 1
    while step < count:
        value = value + lax.ppermute(value, axis, [(i, i ^ step) for i in range(count)])
        step *= 2
    return value


def global_sum(values):
    axes = ("cells", "slab")
    count = lax.axis_size("cells") * lax.axis_size("slab")
    copies = jnp.broadcast_to(values[None], (count,) + values.shape)
    gathered = lax.all_to_all(copies, axes, 0, 0, tiled=True)
    return jnp.sum(gathered, axis=0)


def split3(value):
    high = value.astype(jnp.bfloat16)
    rest = value - high.astype(value.dtype)
    middle = rest.astype(jnp.bfloat16)
    low = (rest - middle.astype(value.dtype)).astype(jnp.bfloat16)
    return high, middle, low


def onehot_dot(value, onehot, dims):
    rows = value.shape[0]
    pieces = jnp.concatenate(split3(value), axis=0)
    part = lax.dot_general(
        pieces, onehot, (dims, ((), ())), preferred_element_type=jnp.float32
    )
    return (part[:rows] + part[rows : 2 * rows]) + part[2 * rows :]


def per_device(
    grad,
    acc_block,
    mobility,
    store,
    trans_h,
    trans_v,
    fault_near,
    fault_far,
    fault_trans,
    fault_count,
    compl_cell,
    compl_well,
    compl_wi,
):
    highest = lax.Precision.HIGHEST
    layer_count, column_count = trans_h.shape
    cells_size = lax.axis_size("cells")
    slab_size = lax.axis_size("slab")
    cells_place = lax.axis_index("cells")
    slab_place = lax.axis_index("slab")
    column_ids = lax.broadcasted_iota(jnp.int32, (layer_count, column_count), 1)
    layer_ids = lax.broadcasted_iota(jnp.int32, (layer_count, column_count), 0)
    zero_value = jnp.zeros((), trans_h.dtype)
    trans_east = jnp.where(
        (cells_place == cells_size - 1) & (column_ids == column_count - 1), zero_value, trans_h
    )
    trans_down = jnp.where(
        (slab_place == slab_size - 1) & (layer_ids == layer_count - 1), zero_value, trans_v
    )
    slot_count = fault_near.size
    slot_live = (jnp.arange(slot_count, dtype=jnp.int32) < fault_count.reshape(())) & (
        cells_place < cells_size - 1
    )
    weight_here = jnp.where(slot_live, fault_trans.reshape(-1), zero_value)
    from_left_setup = shifted(jnp.concatenate([trans_east[:, -1], weight_here]), "cells", 1)
    east_edge = from_left_setup[:layer_count]
    weight_left = from_left_setup[layer_count:]
    down_edge = shifted(trans_down[-1, :], "slab", 1)
    trans_west = jnp.concatenate([east_edge[:, None], trans_east[:, :-1]], axis=1)
    trans_up = jnp.concatenate([down_edge[None, :], trans_down[:-1, :]], axis=0)
    face_total = trans_east + trans_west + trans_down + trans_up

    column_iota = jnp.arange(column_count, dtype=jnp.int32)
    layer_iota = jnp.arange(layer_count, dtype=jnp.int32)

    def locate(cells):
        cells = cells.reshape(-1)
        onehot = (cells % column_count)[:, None] == column_iota[None, :]
        rows = (layer_iota[:, None] == (cells // column_count)[None, :]).astype(jnp.float32)
        return onehot.astype(jnp.bfloat16), rows

    def gather(field, where):
        onehot, rows = where
        parts = field.shape[0]
        flat = field.reshape(parts * layer_count, column_count)
        picked = onehot_dot(flat, onehot, ((1,), (1,)))
        picked = picked.reshape(parts, layer_count, -1) * rows[None]
        return jnp.sum(picked, axis=1)

    def scatter(values, where):
        onehot, rows = where
        parts = values.shape[0]
        spread = (values[:, None, :] * rows[None]).reshape(parts * layer_count, -1)
        placed = onehot_dot(spread, onehot, ((1,), (0,)))
        return placed.reshape(parts, layer_count, column_count)

    fault_at = locate(jnp.concatenate([fault_near.reshape(-1), fault_far.reshape(-1)]))
    well_at = locate(compl_cell)
    well_index = compl_wi.reshape(-1)
    well_onehot = (
        compl_well.reshape(-1)[:, None] == jnp.arange(WELLS, dtype=jnp.int32)[None, :]
    ).astype(trans_h.dtype)

    def inverse_of(newton):
        block = acc_block[newton]
        mobile = mobility[newton]
        diag_first = block[0] + mobile[0] * face_total
        diag_second = block[3] + mobile[1] * face_total
        determinant = diag_first * diag_second - block[1] * block[2]
        return (
            diag_second / determinant,
            -block[1] / determinant,
            -block[2] / determinant,
            diag_first / determinant,
        )

    def precondition(inverse, residual):
        inverse_aa, inverse_ab, inverse_ba, inverse_bb = inverse
        return jnp.stack(
            [
                inverse_aa * residual[0] + inverse_ab * residual[1],
                inverse_ba * residual[0] + inverse_bb * residual[1],
            ]
        )

    def slab_shift(value, by):
        count = lax.axis_size("slab")
        return lax.ppermute(value, "slab", [(i, (i + by) % count) for i in range(count)])

    def operator(fields, mobile, block):
        count = fields.shape[0]
        scaled = (mobile * fields).reshape(count * 2, layer_count, column_count)
        picks = gather(scaled, fault_at)
        picks_near = picks[:, :slot_count]
        picks_far = picks[:, slot_count:]
        from_left = shifted(jnp.concatenate([scaled[:, :, -1], picks_near], axis=1), "cells", 1)
        from_right = shifted(jnp.concatenate([scaled[:, :, 0], picks_far], axis=1), "cells", -1)
        pressure = fields[:, 0]
        values = gather(pressure, well_at)
        local = jnp.concatenate(
            [
                jnp.dot(well_index, well_onehot, precision=highest)[None],
                jnp.dot(well_index * values, well_onehot, precision=highest),
            ]
        )
        halo_size = count * 2 * column_count
        from_above = slab_shift(
            jnp.concatenate([scaled[:, -1, :].reshape(-1), local.reshape(-1)]), 1
        )
        from_below = slab_shift(
            jnp.concatenate([scaled[:, 0, :].reshape(-1), local.reshape(-1)]), -1
        )
        summed = local
        if slab_size > 1:
            summed = summed + from_above[halo_size:].reshape(local.shape)
        if slab_size > 2:
            summed = summed + from_below[halo_size:].reshape(local.shape)
        for by in range(2, slab_size - 1):
            summed = summed + slab_shift(local, by)
        from_above = from_above[:halo_size].reshape(count * 2, column_count)
        from_below = from_below[:halo_size].reshape(count * 2, column_count)
        west = jnp.concatenate([from_left[:, :layer_count, None], scaled[:, :, :-1]], axis=2)
        east = jnp.concatenate([scaled[:, :, 1:], from_right[:, :layer_count, None]], axis=2)
        above = jnp.concatenate([from_above[:, None, :], scaled[:, :-1, :]], axis=1)
        below = jnp.concatenate([scaled[:, 1:, :], from_below[:, None, :]], axis=1)
        laplace = (
            trans_east * (scaled - east)
            + trans_west * (scaled - west)
            + trans_down * (scaled - below)
            + trans_up * (scaled - above)
        )
        flux_right = weight_here * (picks_near - from_right[:, layer_count:])
        flux_left = weight_left * (from_left[:, layer_count:] - picks_far)
        fault_term = scatter(jnp.concatenate([flux_right, -flux_left], axis=1), fault_at)
        laplace = (laplace + fault_term).reshape(count, 2, layer_count, column_count)
        back = jnp.dot(summed[1:] / summed[0], well_onehot.T, precision=highest)
        well_term = scatter(well_index * (values - back), well_at)
        first = (
            block[:, 0] * fields[:, 0]
            + block[:, 1] * fields[:, 1]
            + laplace[:, 0]
            + well_term
        )
        second = block[:, 2] * fields[:, 0] + block[:, 3] * fields[:, 1] + laplace[:, 1]
        return jnp.stack([first, second], axis=1)

    inverse_last = inverse_of(1)
    inverse_first = inverse_of(0)
    grad_last = grad[1]
    grad_first = grad[0]
    z_last = precondition(inverse_last, grad_last)
    carried = store[0] * z_last
    fields = jnp.stack(
        [z_last, precondition(inverse_first, grad_first), precondition(inverse_first, carried)]
    )
    mobile = jnp.stack([mobility[1], mobility[0], mobility[0]])
    block = jnp.stack([acc_block[1], acc_block[0], acc_block[0]])
    images = operator(fields, mobile, block)
    image_last, direct, coupled = images[0], images[1], images[2]
    first_sums = global_sum(
        stacked_sums(
            [
                (grad_last, image_last),
                (image_last, image_last),
                (grad_last, grad_last),
                (grad_first, direct),
                (grad_first, coupled),
                (carried, direct),
                (carried, coupled),
                (direct, direct),
                (direct, coupled),
                (coupled, coupled),
            ]
        )
    )
    lanes = lax.optimization_barrier(
        jnp.broadcast_to(first_sums[:, None], (first_sums.shape[0], column_count))
    )
    (
        along_last,
        energy_last,
        norm_last,
        grad_direct,
        grad_coupled,
        carried_direct,
        carried_coupled,
        direct_direct,
        direct_coupled,
        coupled_coupled,
    ) = [lanes[i] for i in range(first_sums.shape[0])]
    alpha_last = along_last / energy_last
    along_first = grad_direct + alpha_last * (grad_coupled + carried_direct) + (
        alpha_last * alpha_last
    ) * carried_coupled
    energy_first = direct_direct + (2.0 * alpha_last) * direct_coupled + (
        alpha_last * alpha_last
    ) * coupled_coupled
    alpha_first = along_first / energy_first
    solution_last = alpha_last * z_last
    residual_last = grad_last - alpha_last * image_last
    residual_first = grad_first + store[0] * solution_last
    solution_first = alpha_first * precondition(inverse_first, residual_first)
    image_first = direct + alpha_last * coupled
    closing_first = residual_first - alpha_first * image_first
    second_sums = global_sum(
        stacked_sums(
            [
                (residual_first, residual_first),
                (closing_first, closing_first),
                (residual_last, residual_last),
            ]
        )
    )
    norms = jnp.sqrt(
        jnp.concatenate([second_sums[0:2], first_sums[2:3], second_sums[2:3]])
    ).reshape(2, 2)
    return (jnp.stack([solution_first, solution_last]), norms)


def solution(mesh):
    placed = (
        P(None, None, "slab", "cells"),
        P(None, None, "slab", "cells"),
        P(None, None, "slab", "cells"),
        P(None, None, "slab", "cells"),
        P("slab", "cells"),
        P("slab", "cells"),
        P("slab", "cells"),
        P("slab", "cells"),
        P("slab", "cells"),
        P("slab", "cells"),
        P("slab", "cells"),
        P("slab", "cells"),
        P("slab", "cells"),
    )
    return jax.shard_map(
        per_device,
        mesh=mesh,
        in_specs=placed,
        out_specs=(P(None, None, "slab", "cells"), P()),
        check_vma=False,
    )
```

```python
import jax
import jax.numpy as jnp
from jax import lax
from jax.sharding import PartitionSpec as P

WELLS = 16
NSTEPS = 2


def shifted(value, axis, by):
    length = lax.axis_size(axis)
    pairs = [(i, i + by) for i in range(length) if 0 <= i + by < length]
    return lax.ppermute(value, axis, pairs)


def stacked_sums(pairs):
    partial = jnp.stack([jnp.sum(left * right, axis=-2) for left, right in pairs])
    return jnp.sum(partial.reshape(len(pairs), -1), axis=1)


def butterfly(value, axis):
    count = lax.axis_size(axis)
    if count & (count - 1):
        return lax.psum(value, axis)
    step = 1
    while step < count:
        value = value + lax.ppermute(value, axis, [(i, i ^ step) for i in range(count)])
        step *= 2
    return value


def global_sum(values):
    axes = ("cells", "slab")
    count = lax.axis_size("cells") * lax.axis_size("slab")
    copies = jnp.broadcast_to(values[None], (count,) + values.shape)
    gathered = lax.all_to_all(copies, axes, 0, 0, tiled=True)
    return jnp.sum(gathered, axis=0)


def split3(value):
    high = value.astype(jnp.bfloat16)
    rest = value - high.astype(value.dtype)
    middle = rest.astype(jnp.bfloat16)
    low = (rest - middle.astype(value.dtype)).astype(jnp.bfloat16)
    return high, middle, low


def onehot_dot(value, onehot, dims):
    rows = value.shape[0]
    pieces = jnp.concatenate(split3(value), axis=0)
    part = lax.dot_general(
        pieces, onehot, (dims, ((), ())), preferred_element_type=jnp.float32
    )
    return (part[:rows] + part[rows : 2 * rows]) + part[2 * rows :]


def per_device(
    grad,
    acc_block,
    mobility,
    store,
    trans_h,
    trans_v,
    fault_near,
    fault_far,
    fault_trans,
    fault_count,
    compl_cell,
    compl_well,
    compl_wi,
):
    highest = lax.Precision.HIGHEST
    layer_count, column_count = trans_h.shape
    cells_size = lax.axis_size("cells")
    slab_size = lax.axis_size("slab")
    cells_place = lax.axis_index("cells")
    slab_place = lax.axis_index("slab")
    column_ids = lax.broadcasted_iota(jnp.int32, (layer_count, column_count), 1)
    layer_ids = lax.broadcasted_iota(jnp.int32, (layer_count, column_count), 0)
    zero_value = jnp.zeros((), trans_h.dtype)
    trans_east = jnp.where(
        (cells_place == cells_size - 1) & (column_ids == column_count - 1), zero_value, trans_h
    )
    trans_down = jnp.where(
        (slab_place == slab_size - 1) & (layer_ids == layer_count - 1), zero_value, trans_v
    )
    slot_count = fault_near.size
    slot_live = (jnp.arange(slot_count, dtype=jnp.int32) < fault_count.reshape(())) & (
        cells_place < cells_size - 1
    )
    weight_here = jnp.where(slot_live, fault_trans.reshape(-1), zero_value)
    from_left_setup = shifted(jnp.concatenate([trans_east[:, -1], weight_here]), "cells", 1)
    east_edge = from_left_setup[:layer_count]
    weight_left = from_left_setup[layer_count:]
    down_edge = shifted(trans_down[-1, :], "slab", 1)
    trans_west = jnp.concatenate([east_edge[:, None], trans_east[:, :-1]], axis=1)
    trans_up = jnp.concatenate([down_edge[None, :], trans_down[:-1, :]], axis=0)
    face_total = trans_east + trans_west + trans_down + trans_up

    column_iota = jnp.arange(column_count, dtype=jnp.int32)
    layer_iota = jnp.arange(layer_count, dtype=jnp.int32)

    def locate(cells):
        cells = cells.reshape(-1)
        onehot = (cells % column_count)[:, None] == column_iota[None, :]
        rows = (layer_iota[:, None] == (cells // column_count)[None, :]).astype(jnp.float32)
        return onehot.astype(jnp.bfloat16), rows

    def gather(field, where):
        onehot, rows = where
        parts = field.shape[0]
        flat = field.reshape(parts * layer_count, column_count)
        picked = onehot_dot(flat, onehot, ((1,), (1,)))
        picked = picked.reshape(parts, layer_count, -1) * rows[None]
        return jnp.sum(picked, axis=1)

    def scatter(values, where):
        onehot, rows = where
        parts = values.shape[0]
        spread = (values[:, None, :] * rows[None]).reshape(parts * layer_count, -1)
        placed = onehot_dot(spread, onehot, ((1,), (0,)))
        return placed.reshape(parts, layer_count, column_count)

    fault_at = locate(jnp.concatenate([fault_near.reshape(-1), fault_far.reshape(-1)]))
    well_at = locate(compl_cell)
    well_index = compl_wi.reshape(-1)
    well_onehot = (
        compl_well.reshape(-1)[:, None] == jnp.arange(WELLS, dtype=jnp.int32)[None, :]
    ).astype(trans_h.dtype)

    def inverse_of(newton):
        block = acc_block[newton]
        mobile = mobility[newton]
        diag_first = block[0] + mobile[0] * face_total
        diag_second = block[3] + mobile[1] * face_total
        determinant = diag_first * diag_second - block[1] * block[2]
        return (
            diag_second / determinant,
            -block[1] / determinant,
            -block[2] / determinant,
            diag_first / determinant,
        )

    def precondition(inverse, residual):
        inverse_aa, inverse_ab, inverse_ba, inverse_bb = inverse
        return jnp.stack(
            [
                inverse_aa * residual[0] + inverse_ab * residual[1],
                inverse_ba * residual[0] + inverse_bb * residual[1],
            ]
        )

    def slab_shift(value, by):
        count = lax.axis_size("slab")
        return lax.ppermute(value, "slab", [(i, (i + by) % count) for i in range(count)])

    def operator(fields, mobile, block):
        count = fields.shape[0]
        scaled = (mobile * fields).reshape(count * 2, layer_count, column_count)
        picks = gather(scaled, fault_at)
        picks_near = picks[:, :slot_count]
        picks_far = picks[:, slot_count:]
        from_left = shifted(jnp.concatenate([picks_near, scaled[:, :, -1]], axis=1), "cells", 1)
        from_right = shifted(jnp.concatenate([picks_far, scaled[:, :, 0]], axis=1), "cells", -1)
        pressure = fields[:, 0]
        values = gather(pressure, well_at)
        local = jnp.concatenate(
            [
                jnp.dot(well_index, well_onehot, precision=highest)[None],
                jnp.dot(well_index * values, well_onehot, precision=highest),
            ]
        )
        halo_rows = count * 2
        well_rows = -(-local.size // column_count)
        well_block = jnp.pad(
            local.reshape(-1), (0, well_rows * column_count - local.size)
        ).reshape(well_rows, column_count)
        from_above = slab_shift(jnp.concatenate([scaled[:, -1, :], well_block]), 1)
        from_below = slab_shift(jnp.concatenate([scaled[:, 0, :], well_block]), -1)

        def wells_of(message):
            return message[halo_rows:].reshape(-1)[: local.size].reshape(local.shape)

        summed = local
        if slab_size > 1:
            summed = summed + wells_of(from_above)
        if slab_size > 2:
            summed = summed + wells_of(from_below)
        for by in range(2, slab_size - 1):
            summed = summed + slab_shift(local, by)
        from_above = from_above[:halo_rows]
        from_below = from_below[:halo_rows]
        west = jnp.concatenate([from_left[:, slot_count:, None], scaled[:, :, :-1]], axis=2)
        east = jnp.concatenate([scaled[:, :, 1:], from_right[:, slot_count:, None]], axis=2)
        above = jnp.concatenate([from_above[:, None, :], scaled[:, :-1, :]], axis=1)
        below = jnp.concatenate([scaled[:, 1:, :], from_below[:, None, :]], axis=1)
        laplace = (
            trans_east * (scaled - east)
            + trans_west * (scaled - west)
            + trans_down * (scaled - below)
            + trans_up * (scaled - above)
        )
        flux_right = weight_here * (picks_near - from_right[:, :slot_count])
        flux_left = weight_left * (from_left[:, :slot_count] - picks_far)
        fault_term = scatter(jnp.concatenate([flux_right, -flux_left], axis=1), fault_at)
        laplace = (laplace + fault_term).reshape(count, 2, layer_count, column_count)
        back = jnp.dot(summed[1:] / summed[0], well_onehot.T, precision=highest)
        well_term = scatter(well_index * (values - back), well_at)
        first = (
            block[:, 0] * fields[:, 0]
            + block[:, 1] * fields[:, 1]
            + laplace[:, 0]
            + well_term
        )
        second = block[:, 2] * fields[:, 0] + block[:, 3] * fields[:, 1] + laplace[:, 1]
        return jnp.stack([first, second], axis=1)

    inverse_last = inverse_of(1)
    inverse_first = inverse_of(0)
    grad_last = grad[1]
    grad_first = grad[0]
    z_last = precondition(inverse_last, grad_last)
    carried = store[0] * z_last
    fields = jnp.stack(
        [z_last, precondition(inverse_first, grad_first), precondition(inverse_first, carried)]
    )
    mobile = jnp.stack([mobility[1], mobility[0], mobility[0]])
    block = jnp.stack([acc_block[1], acc_block[0], acc_block[0]])
    images = operator(fields, mobile, block)
    image_last, direct, coupled = images[0], images[1], images[2]
    first_sums = global_sum(
        stacked_sums(
            [
                (grad_last, image_last),
                (image_last, image_last),
                (grad_last, grad_last),
                (grad_first, direct),
                (grad_first, coupled),
                (carried, direct),
                (carried, coupled),
                (direct, direct),
                (direct, coupled),
                (coupled, coupled),
            ]
        )
    )
    lanes = lax.optimization_barrier(
        jnp.broadcast_to(first_sums[:, None], (first_sums.shape[0], column_count))
    )
    (
        along_last,
        energy_last,
        norm_last,
        grad_direct,
        grad_coupled,
        carried_direct,
        carried_coupled,
        direct_direct,
        direct_coupled,
        coupled_coupled,
    ) = [lanes[i] for i in range(first_sums.shape[0])]
    alpha_last = along_last / energy_last
    along_first = grad_direct + alpha_last * (grad_coupled + carried_direct) + (
        alpha_last * alpha_last
    ) * carried_coupled
    energy_first = direct_direct + (2.0 * alpha_last) * direct_coupled + (
        alpha_last * alpha_last
    ) * coupled_coupled
    alpha_first = along_first / energy_first
    solution_last = alpha_last * z_last
    residual_last = grad_last - alpha_last * image_last
    residual_first = grad_first + store[0] * solution_last
    solution_first = alpha_first * precondition(inverse_first, residual_first)
    image_first = direct + alpha_last * coupled
    closing_first = residual_first - alpha_first * image_first
    second_sums = global_sum(
        stacked_sums(
            [
                (residual_first, residual_first),
                (closing_first, closing_first),
                (residual_last, residual_last),
            ]
        )
    )
    norms = jnp.sqrt(
        jnp.concatenate([second_sums[0:2], first_sums[2:3], second_sums[2:3]])
    ).reshape(2, 2)
    return (jnp.stack([solution_first, solution_last]), norms)


def solution(mesh):
    placed = (
        P(None, None, "slab", "cells"),
        P(None, None, "slab", "cells"),
        P(None, None, "slab", "cells"),
        P(None, None, "slab", "cells"),
        P("slab", "cells"),
        P("slab", "cells"),
        P("slab", "cells"),
        P("slab", "cells"),
        P("slab", "cells"),
        P("slab", "cells"),
        P("slab", "cells"),
        P("slab", "cells"),
        P("slab", "cells"),
    )
    return jax.shard_map(
        per_device,
        mesh=mesh,
        in_specs=placed,
        out_specs=(P(None, None, "slab", "cells"), P()),
        check_vma=False,
    )
```

```python
import jax
import jax.numpy as jnp
from jax import lax
from jax.sharding import PartitionSpec as P

WELLS = 16
NSTEPS = 2


def shifted(value, axis, by):
    length = lax.axis_size(axis)
    pairs = [(i, i + by) for i in range(length) if 0 <= i + by < length]
    return lax.ppermute(value, axis, pairs)


def stacked_sums(pairs):
    partial = jnp.stack([jnp.sum(left * right, axis=-2) for left, right in pairs])
    return jnp.sum(partial.reshape(len(pairs), -1), axis=1)


def butterfly(value, axis):
    count = lax.axis_size(axis)
    if count & (count - 1):
        return lax.psum(value, axis)
    step = 1
    while step < count:
        value = value + lax.ppermute(value, axis, [(i, i ^ step) for i in range(count)])
        step *= 2
    return value


def global_sum(values):
    axes = ("cells", "slab")
    count = lax.axis_size("cells") * lax.axis_size("slab")
    copies = jnp.broadcast_to(values[None], (count,) + values.shape)
    gathered = lax.all_to_all(copies, axes, 0, 0, tiled=True)
    return jnp.sum(gathered, axis=0)


def split3(value):
    high = value.astype(jnp.bfloat16)
    rest = value - high.astype(value.dtype)
    middle = rest.astype(jnp.bfloat16)
    low = (rest - middle.astype(value.dtype)).astype(jnp.bfloat16)
    return high, middle, low


def split2(value):
    high = value.astype(jnp.bfloat16)
    low = (value - high.astype(value.dtype)).astype(jnp.bfloat16)
    return high, low


def onehot_dot(value, onehot, dims, split=split3):
    rows = value.shape[0]
    parts = split(value)
    pieces = jnp.concatenate(parts, axis=0)
    part = lax.dot_general(
        pieces, onehot, (dims, ((), ())), preferred_element_type=jnp.float32
    )
    total = part[:rows]
    for index in range(1, len(parts)):
        total = total + part[index * rows : (index + 1) * rows]
    return total


def per_device(
    grad,
    acc_block,
    mobility,
    store,
    trans_h,
    trans_v,
    fault_near,
    fault_far,
    fault_trans,
    fault_count,
    compl_cell,
    compl_well,
    compl_wi,
):
    highest = lax.Precision.HIGHEST
    layer_count, column_count = trans_h.shape
    cells_size = lax.axis_size("cells")
    slab_size = lax.axis_size("slab")
    cells_place = lax.axis_index("cells")
    slab_place = lax.axis_index("slab")
    column_ids = lax.broadcasted_iota(jnp.int32, (layer_count, column_count), 1)
    layer_ids = lax.broadcasted_iota(jnp.int32, (layer_count, column_count), 0)
    zero_value = jnp.zeros((), trans_h.dtype)
    trans_east = jnp.where(
        (cells_place == cells_size - 1) & (column_ids == column_count - 1), zero_value, trans_h
    )
    trans_down = jnp.where(
        (slab_place == slab_size - 1) & (layer_ids == layer_count - 1), zero_value, trans_v
    )
    slot_count = fault_near.size
    slot_live = (jnp.arange(slot_count, dtype=jnp.int32) < fault_count.reshape(())) & (
        cells_place < cells_size - 1
    )
    weight_here = jnp.where(slot_live, fault_trans.reshape(-1), zero_value)
    from_left_setup = shifted(jnp.concatenate([trans_east[:, -1], weight_here]), "cells", 1)
    east_edge = from_left_setup[:layer_count]
    weight_left = from_left_setup[layer_count:]
    down_edge = shifted(trans_down[-1, :], "slab", 1)
    trans_west = jnp.concatenate([east_edge[:, None], trans_east[:, :-1]], axis=1)
    trans_up = jnp.concatenate([down_edge[None, :], trans_down[:-1, :]], axis=0)
    face_total = trans_east + trans_west + trans_down + trans_up

    column_iota = jnp.arange(column_count, dtype=jnp.int32)
    layer_iota = jnp.arange(layer_count, dtype=jnp.int32)

    def locate(cells):
        cells = cells.reshape(-1)
        onehot = (cells % column_count)[:, None] == column_iota[None, :]
        rows = (layer_iota[:, None] == (cells // column_count)[None, :]).astype(jnp.float32)
        return onehot.astype(jnp.bfloat16), rows

    def gather(field, where, split=split3):
        onehot, rows = where
        parts = field.shape[0]
        flat = field.reshape(parts * layer_count, column_count)
        picked = onehot_dot(flat, onehot, ((1,), (1,)), split)
        picked = picked.reshape(parts, layer_count, -1) * rows[None]
        return jnp.sum(picked, axis=1)

    def scatter(values, where, split=split3):
        onehot, rows = where
        parts = values.shape[0]
        spread = (values[:, None, :] * rows[None]).reshape(parts * layer_count, -1)
        placed = onehot_dot(spread, onehot, ((1,), (0,)), split)
        return placed.reshape(parts, layer_count, column_count)

    fault_at = locate(jnp.concatenate([fault_near.reshape(-1), fault_far.reshape(-1)]))
    well_at = locate(compl_cell)
    well_index = compl_wi.reshape(-1)
    well_onehot = (
        compl_well.reshape(-1)[:, None] == jnp.arange(WELLS, dtype=jnp.int32)[None, :]
    ).astype(trans_h.dtype)

    def inverse_of(newton):
        block = acc_block[newton]
        mobile = mobility[newton]
        diag_first = block[0] + mobile[0] * face_total
        diag_second = block[3] + mobile[1] * face_total
        determinant = diag_first * diag_second - block[1] * block[2]
        return (
            diag_second / determinant,
            -block[1] / determinant,
            -block[2] / determinant,
            diag_first / determinant,
        )

    def precondition(inverse, residual):
        inverse_aa, inverse_ab, inverse_ba, inverse_bb = inverse
        return jnp.stack(
            [
                inverse_aa * residual[0] + inverse_ab * residual[1],
                inverse_ba * residual[0] + inverse_bb * residual[1],
            ]
        )

    def slab_shift(value, by):
        count = lax.axis_size("slab")
        return lax.ppermute(value, "slab", [(i, (i + by) % count) for i in range(count)])

    def operator(fields, mobile, block):
        count = fields.shape[0]
        scaled = (mobile * fields).reshape(count * 2, layer_count, column_count)
        picks = gather(scaled, fault_at, split2)
        picks_near = picks[:, :slot_count]
        picks_far = picks[:, slot_count:]
        from_left = shifted(jnp.concatenate([scaled[:, :, -1], picks_near], axis=1), "cells", 1)
        from_right = shifted(jnp.concatenate([scaled[:, :, 0], picks_far], axis=1), "cells", -1)
        pressure = fields[:, 0]
        values = gather(pressure, well_at)
        local = jnp.concatenate(
            [
                jnp.dot(well_index, well_onehot, precision=highest)[None],
                jnp.dot(well_index * values, well_onehot, precision=highest),
            ]
        )
        halo_size = count * 2 * column_count
        from_above = slab_shift(
            jnp.concatenate([scaled[:, -1, :].reshape(-1), local.reshape(-1)]), 1
        )
        from_below = slab_shift(
            jnp.concatenate([scaled[:, 0, :].reshape(-1), local.reshape(-1)]), -1
        )
        summed = local
        if slab_size > 1:
            summed = summed + from_above[halo_size:].reshape(local.shape)
        if slab_size > 2:
            summed = summed + from_below[halo_size:].reshape(local.shape)
        for by in range(2, slab_size - 1):
            summed = summed + slab_shift(local, by)
        from_above = from_above[:halo_size].reshape(count * 2, column_count)
        from_below = from_below[:halo_size].reshape(count * 2, column_count)
        west = jnp.concatenate([from_left[:, :layer_count, None], scaled[:, :, :-1]], axis=2)
        east = jnp.concatenate([scaled[:, :, 1:], from_right[:, :layer_count, None]], axis=2)
        above = jnp.concatenate([from_above[:, None, :], scaled[:, :-1, :]], axis=1)
        below = jnp.concatenate([scaled[:, 1:, :], from_below[:, None, :]], axis=1)
        laplace = (
            trans_east * (scaled - east)
            + trans_west * (scaled - west)
            + trans_down * (scaled - below)
            + trans_up * (scaled - above)
        )
        flux_right = weight_here * (picks_near - from_right[:, layer_count:])
        flux_left = weight_left * (from_left[:, layer_count:] - picks_far)
        fault_term = scatter(
            jnp.concatenate([flux_right, -flux_left], axis=1), fault_at, split2
        )
        laplace = (laplace + fault_term).reshape(count, 2, layer_count, column_count)
        back = jnp.dot(summed[1:] / summed[0], well_onehot.T, precision=highest)
        well_term = scatter(well_index * (values - back), well_at)
        first = (
            block[:, 0] * fields[:, 0]
            + block[:, 1] * fields[:, 1]
            + laplace[:, 0]
            + well_term
        )
        second = block[:, 2] * fields[:, 0] + block[:, 3] * fields[:, 1] + laplace[:, 1]
        return jnp.stack([first, second], axis=1)

    inverse_last = inverse_of(1)
    inverse_first = inverse_of(0)
    grad_last = grad[1]
    grad_first = grad[0]
    z_last = precondition(inverse_last, grad_last)
    carried = store[0] * z_last
    fields = jnp.stack(
        [z_last, precondition(inverse_first, grad_first), precondition(inverse_first, carried)]
    )
    mobile = jnp.stack([mobility[1], mobility[0], mobility[0]])
    block = jnp.stack([acc_block[1], acc_block[0], acc_block[0]])
    images = operator(fields, mobile, block)
    image_last, direct, coupled = images[0], images[1], images[2]
    first_sums = global_sum(
        stacked_sums(
            [
                (grad_last, image_last),
                (image_last, image_last),
                (grad_last, grad_last),
                (grad_first, direct),
                (grad_first, coupled),
                (carried, direct),
                (carried, coupled),
                (direct, direct),
                (direct, coupled),
                (coupled, coupled),
            ]
        )
    )
    lanes = lax.optimization_barrier(
        jnp.broadcast_to(first_sums[:, None], (first_sums.shape[0], column_count))
    )
    (
        along_last,
        energy_last,
        norm_last,
        grad_direct,
        grad_coupled,
        carried_direct,
        carried_coupled,
        direct_direct,
        direct_coupled,
        coupled_coupled,
    ) = [lanes[i] for i in range(first_sums.shape[0])]
    alpha_last = along_last / energy_last
    along_first = grad_direct + alpha_last * (grad_coupled + carried_direct) + (
        alpha_last * alpha_last
    ) * carried_coupled
    energy_first = direct_direct + (2.0 * alpha_last) * direct_coupled + (
        alpha_last * alpha_last
    ) * coupled_coupled
    alpha_first = along_first / energy_first
    solution_last = alpha_last * z_last
    residual_last = grad_last - alpha_last * image_last
    residual_first = grad_first + store[0] * solution_last
    solution_first = alpha_first * precondition(inverse_first, residual_first)
    image_first = direct + alpha_last * coupled
    closing_first = residual_first - alpha_first * image_first
    second_sums = global_sum(
        stacked_sums(
            [
                (residual_first, residual_first),
                (closing_first, closing_first),
                (residual_last, residual_last),
            ]
        )
    )
    norms = jnp.sqrt(
        jnp.concatenate([second_sums[0:2], first_sums[2:3], second_sums[2:3]])
    ).reshape(2, 2)
    return (jnp.stack([solution_first, solution_last]), norms)


def solution(mesh):
    placed = (
        P(None, None, "slab", "cells"),
        P(None, None, "slab", "cells"),
        P(None, None, "slab", "cells"),
        P(None, None, "slab", "cells"),
        P("slab", "cells"),
        P("slab", "cells"),
        P("slab", "cells"),
        P("slab", "cells"),
        P("slab", "cells"),
        P("slab", "cells"),
        P("slab", "cells"),
        P("slab", "cells"),
        P("slab", "cells"),
    )
    return jax.shard_map(
        per_device,
        mesh=mesh,
        in_specs=placed,
        out_specs=(P(None, None, "slab", "cells"), P()),
        check_vma=False,
    )
```

```python
import jax
import jax.numpy as jnp
from jax import lax
from jax.sharding import PartitionSpec as P

WELLS = 16
NSTEPS = 2


def shifted(value, axis, by):
    length = lax.axis_size(axis)
    pairs = [(i, i + by) for i in range(length) if 0 <= i + by < length]
    return lax.ppermute(value, axis, pairs)


def stacked_sums(pairs):
    partial = jnp.stack([jnp.sum(left * right, axis=-2) for left, right in pairs])
    return jnp.sum(partial.reshape(len(pairs), -1), axis=1)


def butterfly(value, axis):
    count = lax.axis_size(axis)
    if count & (count - 1):
        return lax.psum(value, axis)
    step = 1
    while step < count:
        value = value + lax.ppermute(value, axis, [(i, i ^ step) for i in range(count)])
        step *= 2
    return value


def global_sum(values):
    axes = ("cells", "slab")
    count = lax.axis_size("cells") * lax.axis_size("slab")
    copies = jnp.broadcast_to(values[None], (count,) + values.shape)
    gathered = lax.all_to_all(copies, axes, 0, 0, tiled=True)
    return jnp.sum(gathered, axis=0)


def split3(value):
    high = value.astype(jnp.bfloat16)
    rest = value - high.astype(value.dtype)
    middle = rest.astype(jnp.bfloat16)
    low = (rest - middle.astype(value.dtype)).astype(jnp.bfloat16)
    return high, middle, low


def split2(value):
    high = value.astype(jnp.bfloat16)
    low = (value - high.astype(value.dtype)).astype(jnp.bfloat16)
    return high, low


def onehot_dot(value, onehot, dims, split=split3):
    rows = value.shape[0]
    parts = split(value)
    pieces = jnp.concatenate(parts, axis=0)
    part = lax.dot_general(
        pieces, onehot, (dims, ((), ())), preferred_element_type=jnp.float32
    )
    total = part[:rows]
    for index in range(1, len(parts)):
        total = total + part[index * rows : (index + 1) * rows]
    return total


def per_device(
    grad,
    acc_block,
    mobility,
    store,
    trans_h,
    trans_v,
    fault_near,
    fault_far,
    fault_trans,
    fault_count,
    compl_cell,
    compl_well,
    compl_wi,
):
    highest = lax.Precision.HIGHEST
    layer_count, column_count = trans_h.shape
    cells_size = lax.axis_size("cells")
    slab_size = lax.axis_size("slab")
    cells_place = lax.axis_index("cells")
    slab_place = lax.axis_index("slab")
    column_ids = lax.broadcasted_iota(jnp.int32, (layer_count, column_count), 1)
    layer_ids = lax.broadcasted_iota(jnp.int32, (layer_count, column_count), 0)
    zero_value = jnp.zeros((), trans_h.dtype)
    trans_east = jnp.where(
        (cells_place == cells_size - 1) & (column_ids == column_count - 1), zero_value, trans_h
    )
    trans_down = jnp.where(
        (slab_place == slab_size - 1) & (layer_ids == layer_count - 1), zero_value, trans_v
    )
    slot_count = fault_near.size
    slot_live = (jnp.arange(slot_count, dtype=jnp.int32) < fault_count.reshape(())) & (
        cells_place < cells_size - 1
    )
    weight_here = jnp.where(slot_live, fault_trans.reshape(-1), zero_value)
    from_left_setup = shifted(jnp.concatenate([trans_east[:, -1], weight_here]), "cells", 1)
    east_edge = from_left_setup[:layer_count]
    weight_left = from_left_setup[layer_count:]
    down_edge = shifted(trans_down[-1, :], "slab", 1)
    trans_west = jnp.concatenate([east_edge[:, None], trans_east[:, :-1]], axis=1)
    trans_up = jnp.concatenate([down_edge[None, :], trans_down[:-1, :]], axis=0)
    face_total = trans_east + trans_west + trans_down + trans_up

    column_iota = jnp.arange(column_count, dtype=jnp.int32)
    layer_iota = jnp.arange(layer_count, dtype=jnp.int32)

    def locate(cells):
        cells = cells.reshape(-1)
        onehot = (cells % column_count)[:, None] == column_iota[None, :]
        rows = (layer_iota[:, None] == (cells // column_count)[None, :]).astype(jnp.float32)
        return onehot.astype(jnp.float8_e4m3fn), rows

    def gather(field, where, split=split3):
        onehot, rows = where
        parts = field.shape[0]
        flat = field.reshape(parts * layer_count, column_count)
        picked = onehot_dot(flat, onehot, ((1,), (1,)), split)
        picked = picked.reshape(parts, layer_count, -1) * rows[None]
        return jnp.sum(picked, axis=1)

    def scatter(values, where, split=split3):
        onehot, rows = where
        parts = values.shape[0]
        spread = (values[:, None, :] * rows[None]).reshape(parts * layer_count, -1)
        placed = onehot_dot(spread, onehot, ((1,), (0,)), split)
        return placed.reshape(parts, layer_count, column_count)

    fault_at = locate(jnp.concatenate([fault_near.reshape(-1), fault_far.reshape(-1)]))
    well_at = locate(compl_cell)
    well_index = compl_wi.reshape(-1)
    well_onehot = (
        compl_well.reshape(-1)[:, None] == jnp.arange(WELLS, dtype=jnp.int32)[None, :]
    ).astype(trans_h.dtype)

    def inverse_of(newton):
        block = acc_block[newton]
        mobile = mobility[newton]
        diag_first = block[0] + mobile[0] * face_total
        diag_second = block[3] + mobile[1] * face_total
        determinant = diag_first * diag_second - block[1] * block[2]
        return (
            diag_second / determinant,
            -block[1] / determinant,
            -block[2] / determinant,
            diag_first / determinant,
        )

    def precondition(inverse, residual):
        inverse_aa, inverse_ab, inverse_ba, inverse_bb = inverse
        return jnp.stack(
            [
                inverse_aa * residual[0] + inverse_ab * residual[1],
                inverse_ba * residual[0] + inverse_bb * residual[1],
            ]
        )

    def slab_shift(value, by):
        count = lax.axis_size("slab")
        return lax.ppermute(value, "slab", [(i, (i + by) % count) for i in range(count)])

    def operator(fields, mobile, block):
        count = fields.shape[0]
        scaled = (mobile * fields).reshape(count * 2, layer_count, column_count)
        picks = gather(scaled, fault_at, split2)
        picks_near = picks[:, :slot_count]
        picks_far = picks[:, slot_count:]
        from_left = shifted(jnp.concatenate([scaled[:, :, -1], picks_near], axis=1), "cells", 1)
        from_right = shifted(jnp.concatenate([scaled[:, :, 0], picks_far], axis=1), "cells", -1)
        pressure = fields[:, 0]
        values = gather(pressure, well_at)
        local = jnp.concatenate(
            [
                jnp.dot(well_index, well_onehot, precision=highest)[None],
                jnp.dot(well_index * values, well_onehot, precision=highest),
            ]
        )
        halo_size = count * 2 * column_count
        from_above = slab_shift(
            jnp.concatenate([scaled[:, -1, :].reshape(-1), local.reshape(-1)]), 1
        )
        from_below = slab_shift(
            jnp.concatenate([scaled[:, 0, :].reshape(-1), local.reshape(-1)]), -1
        )
        summed = local
        if slab_size > 1:
            summed = summed + from_above[halo_size:].reshape(local.shape)
        if slab_size > 2:
            summed = summed + from_below[halo_size:].reshape(local.shape)
        for by in range(2, slab_size - 1):
            summed = summed + slab_shift(local, by)
        from_above = from_above[:halo_size].reshape(count * 2, column_count)
        from_below = from_below[:halo_size].reshape(count * 2, column_count)
        west = jnp.concatenate([from_left[:, :layer_count, None], scaled[:, :, :-1]], axis=2)
        east = jnp.concatenate([scaled[:, :, 1:], from_right[:, :layer_count, None]], axis=2)
        above = jnp.concatenate([from_above[:, None, :], scaled[:, :-1, :]], axis=1)
        below = jnp.concatenate([scaled[:, 1:, :], from_below[:, None, :]], axis=1)
        laplace = (
            trans_east * (scaled - east)
            + trans_west * (scaled - west)
            + trans_down * (scaled - below)
            + trans_up * (scaled - above)
        )
        flux_right = weight_here * (picks_near - from_right[:, layer_count:])
        flux_left = weight_left * (from_left[:, layer_count:] - picks_far)
        fault_term = scatter(
            jnp.concatenate([flux_right, -flux_left], axis=1), fault_at, split2
        )
        laplace = (laplace + fault_term).reshape(count, 2, layer_count, column_count)
        back = jnp.dot(summed[1:] / summed[0], well_onehot.T, precision=highest)
        well_term = scatter(well_index * (values - back), well_at)
        first = (
            block[:, 0] * fields[:, 0]
            + block[:, 1] * fields[:, 1]
            + laplace[:, 0]
            + well_term
        )
        second = block[:, 2] * fields[:, 0] + block[:, 3] * fields[:, 1] + laplace[:, 1]
        return jnp.stack([first, second], axis=1)

    inverse_last = inverse_of(1)
    inverse_first = inverse_of(0)
    grad_last = grad[1]
    grad_first = grad[0]
    z_last = precondition(inverse_last, grad_last)
    carried = store[0] * z_last
    fields = jnp.stack(
        [z_last, precondition(inverse_first, grad_first), precondition(inverse_first, carried)]
    )
    mobile = jnp.stack([mobility[1], mobility[0], mobility[0]])
    block = jnp.stack([acc_block[1], acc_block[0], acc_block[0]])
    images = operator(fields, mobile, block)
    image_last, direct, coupled = images[0], images[1], images[2]
    first_sums = global_sum(
        stacked_sums(
            [
                (grad_last, image_last),
                (image_last, image_last),
                (grad_last, grad_last),
                (grad_first, direct),
                (grad_first, coupled),
                (carried, direct),
                (carried, coupled),
                (direct, direct),
                (direct, coupled),
                (coupled, coupled),
            ]
        )
    )
    lanes = lax.optimization_barrier(
        jnp.broadcast_to(first_sums[:, None], (first_sums.shape[0], column_count))
    )
    (
        along_last,
        energy_last,
        norm_last,
        grad_direct,
        grad_coupled,
        carried_direct,
        carried_coupled,
        direct_direct,
        direct_coupled,
        coupled_coupled,
    ) = [lanes[i] for i in range(first_sums.shape[0])]
    alpha_last = along_last / energy_last
    along_first = grad_direct + alpha_last * (grad_coupled + carried_direct) + (
        alpha_last * alpha_last
    ) * carried_coupled
    energy_first = direct_direct + (2.0 * alpha_last) * direct_coupled + (
        alpha_last * alpha_last
    ) * coupled_coupled
    alpha_first = along_first / energy_first
    solution_last = alpha_last * z_last
    residual_last = grad_last - alpha_last * image_last
    residual_first = grad_first + store[0] * solution_last
    solution_first = alpha_first * precondition(inverse_first, residual_first)
    image_first = direct + alpha_last * coupled
    closing_first = residual_first - alpha_first * image_first
    second_sums = global_sum(
        stacked_sums(
            [
                (residual_first, residual_first),
                (closing_first, closing_first),
                (residual_last, residual_last),
            ]
        )
    )
    norms = jnp.sqrt(
        jnp.concatenate([second_sums[0:2], first_sums[2:3], second_sums[2:3]])
    ).reshape(2, 2)
    return (jnp.stack([solution_first, solution_last]), norms)


def solution(mesh):
    placed = (
        P(None, None, "slab", "cells"),
        P(None, None, "slab", "cells"),
        P(None, None, "slab", "cells"),
        P(None, None, "slab", "cells"),
        P("slab", "cells"),
        P("slab", "cells"),
        P("slab", "cells"),
        P("slab", "cells"),
        P("slab", "cells"),
        P("slab", "cells"),
        P("slab", "cells"),
        P("slab", "cells"),
        P("slab", "cells"),
    )
    return jax.shard_map(
        per_device,
        mesh=mesh,
        in_specs=placed,
        out_specs=(P(None, None, "slab", "cells"), P()),
        check_vma=False,
    )
```

```python
import jax
import jax.numpy as jnp
from jax import lax
from jax.sharding import PartitionSpec as P

WELLS = 16
NSTEPS = 2


def shifted(value, axis, by):
    length = lax.axis_size(axis)
    pairs = [(i, i + by) for i in range(length) if 0 <= i + by < length]
    return lax.ppermute(value, axis, pairs)


def stacked_sums(pairs):
    partial = jnp.stack([jnp.sum(left * right, axis=-2) for left, right in pairs])
    return jnp.sum(partial.reshape(len(pairs), -1), axis=1)


def butterfly(value, axis):
    count = lax.axis_size(axis)
    if count & (count - 1):
        return lax.psum(value, axis)
    step = 1
    while step < count:
        value = value + lax.ppermute(value, axis, [(i, i ^ step) for i in range(count)])
        step *= 2
    return value


def global_sum(values):
    axes = ("cells", "slab")
    count = lax.axis_size("cells") * lax.axis_size("slab")
    copies = jnp.broadcast_to(values[None], (count,) + values.shape)
    gathered = lax.all_to_all(copies, axes, 0, 0, tiled=True)
    return jnp.sum(gathered, axis=0)


def split3(value):
    high = value.astype(jnp.bfloat16)
    rest = value - high.astype(value.dtype)
    middle = rest.astype(jnp.bfloat16)
    low = (rest - middle.astype(value.dtype)).astype(jnp.bfloat16)
    return high, middle, low


def split2(value):
    high = value.astype(jnp.bfloat16)
    low = (value - high.astype(value.dtype)).astype(jnp.bfloat16)
    return high, low


def onehot_dot(value, onehot, dims, split=split3):
    rows = value.shape[0]
    parts = split(value)
    pieces = jnp.concatenate(parts, axis=0)
    part = lax.dot_general(
        pieces, onehot, (dims, ((), ())), preferred_element_type=jnp.float32
    )
    total = part[:rows]
    for index in range(1, len(parts)):
        total = total + part[index * rows : (index + 1) * rows]
    return total


def per_device(
    grad,
    acc_block,
    mobility,
    store,
    trans_h,
    trans_v,
    fault_near,
    fault_far,
    fault_trans,
    fault_count,
    compl_cell,
    compl_well,
    compl_wi,
):
    highest = lax.Precision.HIGHEST
    layer_count, column_count = trans_h.shape
    cells_size = lax.axis_size("cells")
    slab_size = lax.axis_size("slab")
    cells_place = lax.axis_index("cells")
    slab_place = lax.axis_index("slab")
    column_ids = lax.broadcasted_iota(jnp.int32, (layer_count, column_count), 1)
    layer_ids = lax.broadcasted_iota(jnp.int32, (layer_count, column_count), 0)
    zero_value = jnp.zeros((), trans_h.dtype)
    trans_east = jnp.where(
        (cells_place == cells_size - 1) & (column_ids == column_count - 1), zero_value, trans_h
    )
    trans_down = jnp.where(
        (slab_place == slab_size - 1) & (layer_ids == layer_count - 1), zero_value, trans_v
    )
    slot_count = fault_near.size
    slot_live = (jnp.arange(slot_count, dtype=jnp.int32) < fault_count.reshape(())) & (
        cells_place < cells_size - 1
    )
    weight_here = jnp.where(slot_live, fault_trans.reshape(-1), zero_value)
    from_left_setup = shifted(jnp.concatenate([trans_east[:, -1], weight_here]), "cells", 1)
    east_edge = from_left_setup[:layer_count]
    weight_left = from_left_setup[layer_count:]
    down_edge = shifted(trans_down[-1, :], "slab", 1)
    trans_west = jnp.concatenate([east_edge[:, None], trans_east[:, :-1]], axis=1)
    trans_up = jnp.concatenate([down_edge[None, :], trans_down[:-1, :]], axis=0)
    face_total = trans_east + trans_west + trans_down + trans_up

    column_iota = jnp.arange(column_count, dtype=jnp.int32)
    layer_iota = jnp.arange(layer_count, dtype=jnp.int32)

    def locate(cells):
        cells = cells.reshape(-1)
        onehot = (cells % column_count)[:, None] == column_iota[None, :]
        rows = (layer_iota[:, None] == (cells // column_count)[None, :]).astype(jnp.float32)
        return onehot.astype(jnp.float8_e4m3fn), rows

    def gather(field, where, split=split3):
        onehot, rows = where
        parts = field.shape[0]
        flat = field.reshape(parts * layer_count, column_count)
        picked = onehot_dot(flat, onehot, ((1,), (1,)), split)
        picked = picked.reshape(parts, layer_count, -1) * rows[None]
        return jnp.sum(picked, axis=1)

    def scatter(values, where, split=split3):
        onehot, rows = where
        parts = values.shape[0]
        spread = (values[:, None, :] * rows[None]).reshape(parts * layer_count, -1)
        placed = onehot_dot(spread, onehot, ((1,), (0,)), split)
        return placed.reshape(parts, layer_count, column_count)

    fault_at = locate(jnp.concatenate([fault_near.reshape(-1), fault_far.reshape(-1)]))
    well_at = locate(compl_cell)
    well_index = compl_wi.reshape(-1)
    well_onehot = (
        compl_well.reshape(-1)[:, None] == jnp.arange(WELLS, dtype=jnp.int32)[None, :]
    ).astype(trans_h.dtype)

    def inverse_of(newton):
        block = acc_block[newton]
        mobile = mobility[newton]
        diag_first = block[0] + mobile[0] * face_total
        diag_second = block[3] + mobile[1] * face_total
        determinant = diag_first * diag_second - block[1] * block[2]
        return (
            diag_second / determinant,
            -block[1] / determinant,
            -block[2] / determinant,
            diag_first / determinant,
        )

    def precondition(inverse, residual):
        inverse_aa, inverse_ab, inverse_ba, inverse_bb = inverse
        return jnp.stack(
            [
                inverse_aa * residual[0] + inverse_ab * residual[1],
                inverse_ba * residual[0] + inverse_bb * residual[1],
            ]
        )

    def slab_shift(value, by):
        count = lax.axis_size("slab")
        return lax.ppermute(value, "slab", [(i, (i + by) % count) for i in range(count)])

    def operator(fields, mobile, block):
        count = fields.shape[0]
        scaled = (mobile * fields).reshape(count * 2, layer_count, column_count)
        picks = gather(scaled, fault_at, split2)
        picks_near = picks[:, :slot_count]
        picks_far = picks[:, slot_count:]
        from_left = shifted(jnp.concatenate([scaled[:, :, -1], picks_near], axis=1), "cells", 1)
        from_right = shifted(jnp.concatenate([scaled[:, :, 0], picks_far], axis=1), "cells", -1)
        pressure = fields[:, 0]
        values = gather(pressure, well_at)
        local = jnp.concatenate(
            [
                jnp.dot(well_index, well_onehot, precision=highest)[None],
                jnp.dot(well_index * values, well_onehot, precision=highest),
            ]
        )
        halo_size = count * 2 * column_count
        from_above = slab_shift(
            jnp.concatenate([scaled[:, -1, :].reshape(-1), local.reshape(-1)]), 1
        )
        from_below = slab_shift(
            jnp.concatenate([scaled[:, 0, :].reshape(-1), local.reshape(-1)]), -1
        )
        summed = local
        if slab_size > 1:
            summed = summed + from_above[halo_size:].reshape(local.shape)
        if slab_size > 2:
            summed = summed + from_below[halo_size:].reshape(local.shape)
        for by in range(2, slab_size - 1):
            summed = summed + slab_shift(local, by)
        from_above = from_above[:halo_size].reshape(count * 2, column_count)
        from_below = from_below[:halo_size].reshape(count * 2, column_count)
        west = jnp.concatenate([from_left[:, :layer_count, None], scaled[:, :, :-1]], axis=2)
        east = jnp.concatenate([scaled[:, :, 1:], from_right[:, :layer_count, None]], axis=2)
        above = jnp.concatenate([from_above[:, None, :], scaled[:, :-1, :]], axis=1)
        below = jnp.concatenate([scaled[:, 1:, :], from_below[:, None, :]], axis=1)
        laplace = (
            trans_east * (scaled - east)
            + trans_west * (scaled - west)
            + trans_down * (scaled - below)
            + trans_up * (scaled - above)
        )
        flux_right = weight_here * (picks_near - from_right[:, layer_count:])
        flux_left = weight_left * (from_left[:, layer_count:] - picks_far)
        fault_term = scatter(
            jnp.concatenate([flux_right, -flux_left], axis=1), fault_at, split2
        )
        laplace = (laplace + fault_term).reshape(count, 2, layer_count, column_count)
        back = jnp.dot(summed[1:] / summed[0], well_onehot.T, precision=highest)
        well_term = scatter(well_index * (values - back), well_at)
        first = (
            block[:, 0] * fields[:, 0]
            + block[:, 1] * fields[:, 1]
            + laplace[:, 0]
            + well_term
        )
        second = block[:, 2] * fields[:, 0] + block[:, 3] * fields[:, 1] + laplace[:, 1]
        return jnp.stack([first, second], axis=1)

    inverse_last = inverse_of(1)
    inverse_first = inverse_of(0)
    grad_last = grad[1]
    grad_first = grad[0]
    z_last = precondition(inverse_last, grad_last)
    carried = store[0] * z_last
    fields = jnp.stack(
        [z_last, precondition(inverse_first, grad_first), precondition(inverse_first, carried)]
    )
    mobile = jnp.stack([mobility[1], mobility[0], mobility[0]])
    block = jnp.stack([acc_block[1], acc_block[0], acc_block[0]])
    images = operator(fields, mobile, block)
    image_last, direct, coupled = images[0], images[1], images[2]
    first_sums = global_sum(
        stacked_sums(
            [
                (grad_last, image_last),
                (image_last, image_last),
                (grad_last, grad_last),
                (grad_first, direct),
                (grad_first, coupled),
                (carried, direct),
                (carried, coupled),
                (direct, direct),
                (direct, coupled),
                (coupled, coupled),
            ]
        )
    )
    lanes = lax.optimization_barrier(
        jnp.broadcast_to(first_sums[:, None], (first_sums.shape[0], column_count))
    )
    (
        along_last,
        energy_last,
        norm_last,
        grad_direct,
        grad_coupled,
        carried_direct,
        carried_coupled,
        direct_direct,
        direct_coupled,
        coupled_coupled,
    ) = [lanes[i] for i in range(first_sums.shape[0])]
    alpha_last = along_last / energy_last
    along_first = grad_direct + alpha_last * (grad_coupled + carried_direct) + (
        alpha_last * alpha_last
    ) * carried_coupled
    energy_first = direct_direct + (2.0 * alpha_last) * direct_coupled + (
        alpha_last * alpha_last
    ) * coupled_coupled
    alpha_first = along_first / energy_first
    solution_last = alpha_last * z_last
    residual_last = grad_last - alpha_last * image_last
    residual_first = grad_first + store[0] * solution_last
    solution_first = alpha_first * precondition(inverse_first, residual_first)
    image_first = direct + alpha_last * coupled
    closing_first = residual_first - alpha_first * image_first
    second_sums = global_sum(
        stacked_sums(
            [
                (residual_first, residual_first),
                (closing_first, closing_first),
                (grad_last, grad_last),
                (residual_last, residual_last),
            ]
        )
    )
    norms = jnp.sqrt(second_sums).reshape(2, 2)
    return (jnp.stack([solution_first, solution_last]), norms)


def solution(mesh):
    placed = (
        P(None, None, "slab", "cells"),
        P(None, None, "slab", "cells"),
        P(None, None, "slab", "cells"),
        P(None, None, "slab", "cells"),
        P("slab", "cells"),
        P("slab", "cells"),
        P("slab", "cells"),
        P("slab", "cells"),
        P("slab", "cells"),
        P("slab", "cells"),
        P("slab", "cells"),
        P("slab", "cells"),
        P("slab", "cells"),
    )
    return jax.shard_map(
        per_device,
        mesh=mesh,
        in_specs=placed,
        out_specs=(P(None, None, "slab", "cells"), P()),
        check_vma=False,
    )
```

```python
import jax
import jax.numpy as jnp
from jax import lax
from jax.sharding import PartitionSpec as P

WELLS = 16
NSTEPS = 2


def shifted(value, axis, by):
    length = lax.axis_size(axis)
    pairs = [(i, i + by) for i in range(length) if 0 <= i + by < length]
    return lax.ppermute(value, axis, pairs)


def stacked_sums(pairs):
    partial = jnp.stack([jnp.sum(left * right, axis=-2) for left, right in pairs])
    return jnp.sum(partial.reshape(len(pairs), -1), axis=1)


def butterfly(value, axis):
    count = lax.axis_size(axis)
    if count & (count - 1):
        return lax.psum(value, axis)
    step = 1
    while step < count:
        value = value + lax.ppermute(value, axis, [(i, i ^ step) for i in range(count)])
        step *= 2
    return value


def global_sum(values):
    axes = ("cells", "slab")
    count = lax.axis_size("cells") * lax.axis_size("slab")
    copies = jnp.broadcast_to(values[None], (count,) + values.shape)
    gathered = lax.all_to_all(copies, axes, 0, 0, tiled=True)
    return jnp.sum(gathered, axis=0)


def split3(value):
    high = value.astype(jnp.bfloat16)
    rest = value - high.astype(value.dtype)
    middle = rest.astype(jnp.bfloat16)
    low = (rest - middle.astype(value.dtype)).astype(jnp.bfloat16)
    return high, middle, low


def split2(value):
    high = value.astype(jnp.bfloat16)
    low = (value - high.astype(value.dtype)).astype(jnp.bfloat16)
    return high, low


def onehot_dot(value, onehot, dims, split=split3):
    rows = value.shape[0]
    parts = split(value)
    pieces = jnp.concatenate(parts, axis=0)
    part = lax.dot_general(
        pieces, onehot, (dims, ((), ())), preferred_element_type=jnp.float32
    )
    total = part[:rows]
    for index in range(1, len(parts)):
        total = total + part[index * rows : (index + 1) * rows]
    return total


def per_device(
    grad,
    acc_block,
    mobility,
    store,
    trans_h,
    trans_v,
    fault_near,
    fault_far,
    fault_trans,
    fault_count,
    compl_cell,
    compl_well,
    compl_wi,
):
    highest = lax.Precision.HIGHEST
    layer_count, column_count = trans_h.shape
    cells_size = lax.axis_size("cells")
    slab_size = lax.axis_size("slab")
    cells_place = lax.axis_index("cells")
    slab_place = lax.axis_index("slab")
    column_ids = lax.broadcasted_iota(jnp.int32, (layer_count, column_count), 1)
    layer_ids = lax.broadcasted_iota(jnp.int32, (layer_count, column_count), 0)
    zero_value = jnp.zeros((), trans_h.dtype)
    trans_east = jnp.where(
        (cells_place == cells_size - 1) & (column_ids == column_count - 1), zero_value, trans_h
    )
    trans_down = jnp.where(
        (slab_place == slab_size - 1) & (layer_ids == layer_count - 1), zero_value, trans_v
    )
    slot_count = fault_near.size
    slot_live = (jnp.arange(slot_count, dtype=jnp.int32) < fault_count.reshape(())) & (
        cells_place < cells_size - 1
    )
    weight_here = jnp.where(slot_live, fault_trans.reshape(-1), zero_value)
    from_left_setup = shifted(jnp.concatenate([trans_east[:, -1], weight_here]), "cells", 1)
    east_edge = from_left_setup[:layer_count]
    weight_left = from_left_setup[layer_count:]
    down_edge = shifted(trans_down[-1, :], "slab", 1)
    trans_west = jnp.concatenate([east_edge[:, None], trans_east[:, :-1]], axis=1)
    trans_up = jnp.concatenate([down_edge[None, :], trans_down[:-1, :]], axis=0)
    face_total = trans_east + trans_west + trans_down + trans_up

    column_iota = jnp.arange(column_count, dtype=jnp.int32)
    layer_iota = jnp.arange(layer_count, dtype=jnp.int32)

    def locate(cells):
        cells = cells.reshape(-1)
        onehot = (cells % column_count)[:, None] == column_iota[None, :]
        rows = (layer_iota[:, None] == (cells // column_count)[None, :]).astype(jnp.float32)
        return onehot.astype(jnp.float8_e4m3fn), rows

    def gather(field, where, split=split3):
        onehot, rows = where
        parts = field.shape[0]
        flat = field.reshape(parts * layer_count, column_count)
        picked = onehot_dot(flat, onehot, ((1,), (1,)), split)
        picked = picked.reshape(parts, layer_count, -1) * rows[None]
        return jnp.sum(picked, axis=1)

    def scatter(values, where, split=split3):
        onehot, rows = where
        parts = values.shape[0]
        spread = (values[:, None, :] * rows[None]).reshape(parts * layer_count, -1)
        placed = onehot_dot(spread, onehot, ((1,), (0,)), split)
        return placed.reshape(parts, layer_count, column_count)

    fault_at = locate(jnp.concatenate([fault_near.reshape(-1), fault_far.reshape(-1)]))
    well_at = locate(compl_cell)
    well_index = compl_wi.reshape(-1)
    well_onehot = (
        compl_well.reshape(-1)[:, None] == jnp.arange(WELLS, dtype=jnp.int32)[None, :]
    ).astype(trans_h.dtype)

    def inverse_of(newton):
        block = acc_block[newton]
        mobile = mobility[newton]
        diag_first = block[0] + mobile[0] * face_total
        diag_second = block[3] + mobile[1] * face_total
        determinant = diag_first * diag_second - block[1] * block[2]
        return (
            diag_second / determinant,
            -block[1] / determinant,
            -block[2] / determinant,
            diag_first / determinant,
        )

    def precondition(inverse, residual):
        inverse_aa, inverse_ab, inverse_ba, inverse_bb = inverse
        return jnp.stack(
            [
                inverse_aa * residual[0] + inverse_ab * residual[1],
                inverse_ba * residual[0] + inverse_bb * residual[1],
            ]
        )

    def slab_shift(value, by):
        count = lax.axis_size("slab")
        return lax.ppermute(value, "slab", [(i, (i + by) % count) for i in range(count)])

    def operator(fields, mobile, block):
        count = fields.shape[0]
        scaled = (mobile * fields).reshape(count * 2, layer_count, column_count)
        picks = gather(scaled, fault_at, split2)
        picks_near = picks[:, :slot_count]
        picks_far = picks[:, slot_count:]
        from_left = shifted(jnp.concatenate([scaled[:, :, -1], picks_near], axis=1), "cells", 1)
        from_right = shifted(jnp.concatenate([scaled[:, :, 0], picks_far], axis=1), "cells", -1)
        pressure = fields[:, 0]
        values = gather(pressure, well_at)
        local = jnp.concatenate(
            [
                jnp.dot(well_index, well_onehot, precision=highest)[None],
                jnp.dot(well_index * values, well_onehot, precision=highest),
            ]
        )
        halo_rows = count * 2
        wells = local.shape[1]
        lanes = -(-wells // column_count) * column_count
        well_block = jnp.pad(local, ((0, 0), (0, lanes - wells))).reshape(-1, column_count)
        from_above = slab_shift(jnp.concatenate([scaled[:, -1, :], well_block]), 1)
        from_below = slab_shift(jnp.concatenate([scaled[:, 0, :], well_block]), -1)

        def wells_of(message):
            return message[halo_rows:].reshape(local.shape[0], lanes)[:, :wells]

        summed = local
        if slab_size > 1:
            summed = summed + wells_of(from_above)
        if slab_size > 2:
            summed = summed + wells_of(from_below)
        for by in range(2, slab_size - 1):
            summed = summed + slab_shift(local, by)
        from_above = from_above[:halo_rows]
        from_below = from_below[:halo_rows]
        west = jnp.concatenate([from_left[:, :layer_count, None], scaled[:, :, :-1]], axis=2)
        east = jnp.concatenate([scaled[:, :, 1:], from_right[:, :layer_count, None]], axis=2)
        above = jnp.concatenate([from_above[:, None, :], scaled[:, :-1, :]], axis=1)
        below = jnp.concatenate([scaled[:, 1:, :], from_below[:, None, :]], axis=1)
        laplace = (
            trans_east * (scaled - east)
            + trans_west * (scaled - west)
            + trans_down * (scaled - below)
            + trans_up * (scaled - above)
        )
        flux_right = weight_here * (picks_near - from_right[:, layer_count:])
        flux_left = weight_left * (from_left[:, layer_count:] - picks_far)
        fault_term = scatter(
            jnp.concatenate([flux_right, -flux_left], axis=1), fault_at, split2
        )
        laplace = (laplace + fault_term).reshape(count, 2, layer_count, column_count)
        back = jnp.dot(summed[1:] / summed[0], well_onehot.T, precision=highest)
        well_term = scatter(well_index * (values - back), well_at)
        first = (
            block[:, 0] * fields[:, 0]
            + block[:, 1] * fields[:, 1]
            + laplace[:, 0]
            + well_term
        )
        second = block[:, 2] * fields[:, 0] + block[:, 3] * fields[:, 1] + laplace[:, 1]
        return jnp.stack([first, second], axis=1)

    inverse_last = inverse_of(1)
    inverse_first = inverse_of(0)
    grad_last = grad[1]
    grad_first = grad[0]
    z_last = precondition(inverse_last, grad_last)
    carried = store[0] * z_last
    fields = jnp.stack(
        [z_last, precondition(inverse_first, grad_first), precondition(inverse_first, carried)]
    )
    mobile = jnp.stack([mobility[1], mobility[0], mobility[0]])
    block = jnp.stack([acc_block[1], acc_block[0], acc_block[0]])
    images = operator(fields, mobile, block)
    image_last, direct, coupled = images[0], images[1], images[2]
    first_sums = global_sum(
        stacked_sums(
            [
                (grad_last, image_last),
                (image_last, image_last),
                (grad_last, grad_last),
                (grad_first, direct),
                (grad_first, coupled),
                (carried, direct),
                (carried, coupled),
                (direct, direct),
                (direct, coupled),
                (coupled, coupled),
            ]
        )
    )
    lanes = lax.optimization_barrier(
        jnp.broadcast_to(first_sums[:, None], (first_sums.shape[0], column_count))
    )
    (
        along_last,
        energy_last,
        norm_last,
        grad_direct,
        grad_coupled,
        carried_direct,
        carried_coupled,
        direct_direct,
        direct_coupled,
        coupled_coupled,
    ) = [lanes[i] for i in range(first_sums.shape[0])]
    alpha_last = along_last / energy_last
    along_first = grad_direct + alpha_last * (grad_coupled + carried_direct) + (
        alpha_last * alpha_last
    ) * carried_coupled
    energy_first = direct_direct + (2.0 * alpha_last) * direct_coupled + (
        alpha_last * alpha_last
    ) * coupled_coupled
    alpha_first = along_first / energy_first
    solution_last = alpha_last * z_last
    residual_last = grad_last - alpha_last * image_last
    residual_first = grad_first + store[0] * solution_last
    solution_first = alpha_first * precondition(inverse_first, residual_first)
    image_first = direct + alpha_last * coupled
    closing_first = residual_first - alpha_first * image_first
    second_sums = global_sum(
        stacked_sums(
            [
                (residual_first, residual_first),
                (closing_first, closing_first),
                (grad_last, grad_last),
                (residual_last, residual_last),
            ]
        )
    )
    norms = jnp.sqrt(second_sums).reshape(2, 2)
    return (jnp.stack([solution_first, solution_last]), norms)


def solution(mesh):
    placed = (
        P(None, None, "slab", "cells"),
        P(None, None, "slab", "cells"),
        P(None, None, "slab", "cells"),
        P(None, None, "slab", "cells"),
        P("slab", "cells"),
        P("slab", "cells"),
        P("slab", "cells"),
        P("slab", "cells"),
        P("slab", "cells"),
        P("slab", "cells"),
        P("slab", "cells"),
        P("slab", "cells"),
        P("slab", "cells"),
    )
    return jax.shard_map(
        per_device,
        mesh=mesh,
        in_specs=placed,
        out_specs=(P(None, None, "slab", "cells"), P()),
        check_vma=False,
    )
```

```python
import jax
import jax.numpy as jnp
from jax import lax
from jax.sharding import PartitionSpec as P

WELLS = 16
NSTEPS = 2


def shifted(value, axis, by):
    length = lax.axis_size(axis)
    pairs = [(i, i + by) for i in range(length) if 0 <= i + by < length]
    return lax.ppermute(value, axis, pairs)


def stacked_sums(pairs):
    partial = jnp.stack([jnp.sum(left * right, axis=-2) for left, right in pairs])
    return jnp.sum(partial.reshape(len(pairs), -1), axis=1)


def butterfly(value, axis):
    count = lax.axis_size(axis)
    if count & (count - 1):
        return lax.psum(value, axis)
    step = 1
    while step < count:
        value = value + lax.ppermute(value, axis, [(i, i ^ step) for i in range(count)])
        step *= 2
    return value


def global_sum(values):
    axes = ("cells", "slab")
    count = lax.axis_size("cells") * lax.axis_size("slab")
    copies = jnp.broadcast_to(values[None], (count,) + values.shape)
    gathered = lax.all_to_all(copies, axes, 0, 0, tiled=True)
    return jnp.sum(gathered, axis=0)


def split3(value):
    high = value.astype(jnp.bfloat16)
    rest = value - high.astype(value.dtype)
    middle = rest.astype(jnp.bfloat16)
    low = (rest - middle.astype(value.dtype)).astype(jnp.bfloat16)
    return high, middle, low


def split2(value):
    high = value.astype(jnp.bfloat16)
    low = (value - high.astype(value.dtype)).astype(jnp.bfloat16)
    return high, low


def onehot_dot(value, onehot, dims, split=split3):
    rows = value.shape[0]
    parts = split(value)
    pieces = jnp.concatenate(parts, axis=0)
    part = lax.dot_general(
        pieces, onehot, (dims, ((), ())), preferred_element_type=jnp.float32
    )
    total = part[:rows]
    for index in range(1, len(parts)):
        total = total + part[index * rows : (index + 1) * rows]
    return total


def per_device(
    grad,
    acc_block,
    mobility,
    store,
    trans_h,
    trans_v,
    fault_near,
    fault_far,
    fault_trans,
    fault_count,
    compl_cell,
    compl_well,
    compl_wi,
):
    highest = lax.Precision.HIGHEST
    layer_count, column_count = trans_h.shape
    cells_size = lax.axis_size("cells")
    slab_size = lax.axis_size("slab")
    cells_place = lax.axis_index("cells")
    slab_place = lax.axis_index("slab")
    column_ids = lax.broadcasted_iota(jnp.int32, (layer_count, column_count), 1)
    layer_ids = lax.broadcasted_iota(jnp.int32, (layer_count, column_count), 0)
    zero_value = jnp.zeros((), trans_h.dtype)
    trans_east = jnp.where(
        (cells_place == cells_size - 1) & (column_ids == column_count - 1), zero_value, trans_h
    )
    trans_down = jnp.where(
        (slab_place == slab_size - 1) & (layer_ids == layer_count - 1), zero_value, trans_v
    )
    slot_count = fault_near.size
    slot_live = (jnp.arange(slot_count, dtype=jnp.int32) < fault_count.reshape(())) & (
        cells_place < cells_size - 1
    )
    weight_here = jnp.where(slot_live, fault_trans.reshape(-1), zero_value)
    from_left_setup = shifted(jnp.concatenate([trans_east[:, -1], weight_here]), "cells", 1)
    east_edge = from_left_setup[:layer_count]
    weight_left = from_left_setup[layer_count:]
    down_edge = shifted(trans_down[-1, :], "slab", 1)
    trans_west = jnp.concatenate([east_edge[:, None], trans_east[:, :-1]], axis=1)
    trans_up = jnp.concatenate([down_edge[None, :], trans_down[:-1, :]], axis=0)
    face_total = trans_east + trans_west + trans_down + trans_up

    column_iota = jnp.arange(column_count, dtype=jnp.int32)
    layer_iota = jnp.arange(layer_count, dtype=jnp.int32)

    def locate(cells):
        cells = cells.reshape(-1)
        onehot = (cells % column_count)[:, None] == column_iota[None, :]
        rows = (layer_iota[:, None] == (cells // column_count)[None, :]).astype(jnp.float32)
        return onehot.astype(jnp.float8_e4m3fn), rows

    def gather(field, where, split=split3):
        onehot, rows = where
        parts = field.shape[0]
        flat = field.reshape(parts * layer_count, column_count)
        picked = onehot_dot(flat, onehot, ((1,), (1,)), split)
        picked = picked.reshape(parts, layer_count, -1) * rows[None]
        return jnp.sum(picked, axis=1)

    def scatter(values, where, split=split3):
        onehot, rows = where
        parts = values.shape[0]
        spread = (values[:, None, :] * rows[None]).reshape(parts * layer_count, -1)
        placed = onehot_dot(spread, onehot, ((1,), (0,)), split)
        return placed.reshape(parts, layer_count, column_count)

    edge_cells = jnp.concatenate(
        [layer_iota * column_count, layer_iota * column_count + (column_count - 1)]
    )
    fault_at = locate(
        jnp.concatenate([fault_near.reshape(-1), fault_far.reshape(-1), edge_cells])
    )
    west_face = east_edge
    east_face = trans_east[:, -1]
    well_at = locate(compl_cell)
    well_index = compl_wi.reshape(-1)
    well_onehot = (
        compl_well.reshape(-1)[:, None] == jnp.arange(WELLS, dtype=jnp.int32)[None, :]
    ).astype(trans_h.dtype)

    def inverse_of(newton):
        block = acc_block[newton]
        mobile = mobility[newton]
        diag_first = block[0] + mobile[0] * face_total
        diag_second = block[3] + mobile[1] * face_total
        determinant = diag_first * diag_second - block[1] * block[2]
        return (
            diag_second / determinant,
            -block[1] / determinant,
            -block[2] / determinant,
            diag_first / determinant,
        )

    def precondition(inverse, residual):
        inverse_aa, inverse_ab, inverse_ba, inverse_bb = inverse
        return jnp.stack(
            [
                inverse_aa * residual[0] + inverse_ab * residual[1],
                inverse_ba * residual[0] + inverse_bb * residual[1],
            ]
        )

    def slab_shift(value, by):
        count = lax.axis_size("slab")
        return lax.ppermute(value, "slab", [(i, (i + by) % count) for i in range(count)])

    def operator(fields, mobile, block):
        count = fields.shape[0]
        scaled = (mobile * fields).reshape(count * 2, layer_count, column_count)
        picks = gather(scaled, fault_at, split2)
        picks_near = picks[:, :slot_count]
        picks_far = picks[:, slot_count : 2 * slot_count]
        from_left = shifted(jnp.concatenate([scaled[:, :, -1], picks_near], axis=1), "cells", 1)
        from_right = shifted(jnp.concatenate([scaled[:, :, 0], picks_far], axis=1), "cells", -1)
        pressure = fields[:, 0]
        values = gather(pressure, well_at)
        local = jnp.concatenate(
            [
                jnp.dot(well_index, well_onehot, precision=highest)[None],
                jnp.dot(well_index * values, well_onehot, precision=highest),
            ]
        )
        halo_rows = count * 2
        wells = local.shape[1]
        lanes = -(-wells // column_count) * column_count
        well_block = jnp.pad(local, ((0, 0), (0, lanes - wells))).reshape(-1, column_count)
        from_above = slab_shift(jnp.concatenate([scaled[:, -1, :], well_block]), 1)
        from_below = slab_shift(jnp.concatenate([scaled[:, 0, :], well_block]), -1)

        def wells_of(message):
            return message[halo_rows:].reshape(local.shape[0], lanes)[:, :wells]

        summed = local
        if slab_size > 1:
            summed = summed + wells_of(from_above)
        if slab_size > 2:
            summed = summed + wells_of(from_below)
        for by in range(2, slab_size - 1):
            summed = summed + slab_shift(local, by)
        from_above = from_above[:halo_rows]
        from_below = from_below[:halo_rows]
        zero_column = jnp.zeros_like(scaled[:, :, :1])
        west = jnp.concatenate([zero_column, scaled[:, :, :-1]], axis=2)
        east = jnp.concatenate([scaled[:, :, 1:], zero_column], axis=2)
        above = jnp.where(
            layer_ids == 0,
            from_above[:, None, :],
            jnp.pad(scaled[:, :-1, :], ((0, 0), (1, 0), (0, 0))),
        )
        below = jnp.where(
            layer_ids == layer_count - 1,
            from_below[:, None, :],
            jnp.pad(scaled[:, 1:, :], ((0, 0), (0, 1), (0, 0))),
        )
        laplace = (
            trans_east * (scaled - east)
            + trans_west * (scaled - west)
            + trans_down * (scaled - below)
            + trans_up * (scaled - above)
        )
        flux_right = weight_here * (picks_near - from_right[:, layer_count:])
        flux_left = weight_left * (from_left[:, layer_count:] - picks_far)
        fault_term = scatter(
            jnp.concatenate(
                [
                    flux_right,
                    -flux_left,
                    -west_face * from_left[:, :layer_count],
                    -east_face * from_right[:, :layer_count],
                ],
                axis=1,
            ),
            fault_at,
            split2,
        )
        laplace = (laplace + fault_term).reshape(count, 2, layer_count, column_count)
        back = jnp.dot(summed[1:] / summed[0], well_onehot.T, precision=highest)
        well_term = scatter(well_index * (values - back), well_at)
        first = (
            block[:, 0] * fields[:, 0]
            + block[:, 1] * fields[:, 1]
            + laplace[:, 0]
            + well_term
        )
        second = block[:, 2] * fields[:, 0] + block[:, 3] * fields[:, 1] + laplace[:, 1]
        return jnp.stack([first, second], axis=1)

    inverse_last = inverse_of(1)
    inverse_first = inverse_of(0)
    grad_last = grad[1]
    grad_first = grad[0]
    z_last = precondition(inverse_last, grad_last)
    carried = store[0] * z_last
    fields = jnp.stack(
        [z_last, precondition(inverse_first, grad_first), precondition(inverse_first, carried)]
    )
    mobile = jnp.stack([mobility[1], mobility[0], mobility[0]])
    block = jnp.stack([acc_block[1], acc_block[0], acc_block[0]])
    images = operator(fields, mobile, block)
    image_last, direct, coupled = images[0], images[1], images[2]
    first_sums = global_sum(
        stacked_sums(
            [
                (grad_last, image_last),
                (image_last, image_last),
                (grad_last, grad_last),
                (grad_first, direct),
                (grad_first, coupled),
                (carried, direct),
                (carried, coupled),
                (direct, direct),
                (direct, coupled),
                (coupled, coupled),
            ]
        )
    )
    lanes = lax.optimization_barrier(
        jnp.broadcast_to(first_sums[:, None], (first_sums.shape[0], column_count))
    )
    (
        along_last,
        energy_last,
        norm_last,
        grad_direct,
        grad_coupled,
        carried_direct,
        carried_coupled,
        direct_direct,
        direct_coupled,
        coupled_coupled,
    ) = [lanes[i] for i in range(first_sums.shape[0])]
    alpha_last = along_last / energy_last
    along_first = grad_direct + alpha_last * (grad_coupled + carried_direct) + (
        alpha_last * alpha_last
    ) * carried_coupled
    energy_first = direct_direct + (2.0 * alpha_last) * direct_coupled + (
        alpha_last * alpha_last
    ) * coupled_coupled
    alpha_first = along_first / energy_first
    solution_last = alpha_last * z_last
    residual_last = grad_last - alpha_last * image_last
    residual_first = grad_first + store[0] * solution_last
    solution_first = alpha_first * precondition(inverse_first, residual_first)
    image_first = direct + alpha_last * coupled
    closing_first = residual_first - alpha_first * image_first
    second_sums = global_sum(
        stacked_sums(
            [
                (residual_first, residual_first),
                (closing_first, closing_first),
                (grad_last, grad_last),
                (residual_last, residual_last),
            ]
        )
    )
    norms = jnp.sqrt(second_sums).reshape(2, 2)
    return (jnp.stack([solution_first, solution_last]), norms)


def solution(mesh):
    placed = (
        P(None, None, "slab", "cells"),
        P(None, None, "slab", "cells"),
        P(None, None, "slab", "cells"),
        P(None, None, "slab", "cells"),
        P("slab", "cells"),
        P("slab", "cells"),
        P("slab", "cells"),
        P("slab", "cells"),
        P("slab", "cells"),
        P("slab", "cells"),
        P("slab", "cells"),
        P("slab", "cells"),
        P("slab", "cells"),
    )
    return jax.shard_map(
        per_device,
        mesh=mesh,
        in_specs=placed,
        out_specs=(P(None, None, "slab", "cells"), P()),
        check_vma=False,
    )
```

```python
import jax
import jax.numpy as jnp
from jax import lax
from jax.sharding import PartitionSpec as P

WELLS = 16
NSTEPS = 2


def shifted(value, axis, by):
    length = lax.axis_size(axis)
    pairs = [(i, i + by) for i in range(length) if 0 <= i + by < length]
    return lax.ppermute(value, axis, pairs)


def stacked_sums(pairs):
    partial = jnp.stack([jnp.sum(left * right, axis=-2) for left, right in pairs])
    return jnp.sum(partial.reshape(len(pairs), -1), axis=1)


def butterfly(value, axis):
    count = lax.axis_size(axis)
    if count & (count - 1):
        return lax.psum(value, axis)
    step = 1
    while step < count:
        value = value + lax.ppermute(value, axis, [(i, i ^ step) for i in range(count)])
        step *= 2
    return value


def global_sum(values):
    axes = ("cells", "slab")
    count = lax.axis_size("cells") * lax.axis_size("slab")
    copies = jnp.broadcast_to(values[None], (count,) + values.shape)
    gathered = lax.all_to_all(copies, axes, 0, 0, tiled=True)
    return jnp.sum(gathered, axis=0)


def split3(value):
    high = value.astype(jnp.bfloat16)
    rest = value - high.astype(value.dtype)
    middle = rest.astype(jnp.bfloat16)
    low = (rest - middle.astype(value.dtype)).astype(jnp.bfloat16)
    return high, middle, low


def split2(value):
    high = value.astype(jnp.bfloat16)
    low = (value - high.astype(value.dtype)).astype(jnp.bfloat16)
    return high, low


def onehot_dot(value, onehot, dims, split=split3):
    rows = value.shape[0]
    parts = split(value)
    pieces = jnp.concatenate(parts, axis=0)
    part = lax.dot_general(
        pieces, onehot, (dims, ((), ())), preferred_element_type=jnp.float32
    )
    total = part[:rows]
    for index in range(1, len(parts)):
        total = total + part[index * rows : (index + 1) * rows]
    return total


def per_device(
    grad,
    acc_block,
    mobility,
    store,
    trans_h,
    trans_v,
    fault_near,
    fault_far,
    fault_trans,
    fault_count,
    compl_cell,
    compl_well,
    compl_wi,
):
    highest = lax.Precision.HIGHEST
    layer_count, column_count = trans_h.shape
    cells_size = lax.axis_size("cells")
    slab_size = lax.axis_size("slab")
    cells_place = lax.axis_index("cells")
    slab_place = lax.axis_index("slab")
    column_ids = lax.broadcasted_iota(jnp.int32, (layer_count, column_count), 1)
    layer_ids = lax.broadcasted_iota(jnp.int32, (layer_count, column_count), 0)
    zero_value = jnp.zeros((), trans_h.dtype)
    trans_east = jnp.where(
        (cells_place == cells_size - 1) & (column_ids == column_count - 1), zero_value, trans_h
    )
    trans_down = jnp.where(
        (slab_place == slab_size - 1) & (layer_ids == layer_count - 1), zero_value, trans_v
    )
    slot_count = fault_near.size
    slot_live = (jnp.arange(slot_count, dtype=jnp.int32) < fault_count.reshape(())) & (
        cells_place < cells_size - 1
    )
    weight_here = jnp.where(slot_live, fault_trans.reshape(-1), zero_value)
    from_left_setup = shifted(jnp.concatenate([trans_east[:, -1], weight_here]), "cells", 1)
    east_edge = from_left_setup[:layer_count]
    weight_left = from_left_setup[layer_count:]
    down_edge = shifted(trans_down[-1, :], "slab", 1)
    trans_west = jnp.concatenate([east_edge[:, None], trans_east[:, :-1]], axis=1)
    trans_up = jnp.concatenate([down_edge[None, :], trans_down[:-1, :]], axis=0)
    face_total = trans_east + trans_west + trans_down + trans_up

    column_iota = jnp.arange(column_count, dtype=jnp.int32)
    layer_iota = jnp.arange(layer_count, dtype=jnp.int32)

    def locate(cells):
        cells = cells.reshape(-1)
        onehot = (cells % column_count)[:, None] == column_iota[None, :]
        rows = (layer_iota[:, None] == (cells // column_count)[None, :]).astype(jnp.float32)
        return onehot.astype(jnp.float8_e4m3fn), rows

    def gather(field, where, split=split3):
        onehot, rows = where
        parts = field.shape[0]
        flat = field.reshape(parts * layer_count, column_count)
        picked = onehot_dot(flat, onehot, ((1,), (1,)), split)
        picked = picked.reshape(parts, layer_count, -1) * rows[None]
        return jnp.sum(picked, axis=1)

    def scatter(values, where, split=split3):
        onehot, rows = where
        parts = values.shape[0]
        spread = (values[:, None, :] * rows[None]).reshape(parts * layer_count, -1)
        placed = onehot_dot(spread, onehot, ((1,), (0,)), split)
        return placed.reshape(parts, layer_count, column_count)

    edge_pad = -(2 * layer_count) % 128
    edge_cells = jnp.concatenate(
        [
            layer_iota * column_count,
            layer_iota * column_count + (column_count - 1),
            jnp.zeros((edge_pad,), jnp.int32),
        ]
    )
    fault_at = locate(
        jnp.concatenate([fault_near.reshape(-1), fault_far.reshape(-1), edge_cells])
    )
    west_face = east_edge
    east_face = trans_east[:, -1]
    well_at = locate(compl_cell)
    well_index = compl_wi.reshape(-1)
    well_onehot = (
        compl_well.reshape(-1)[:, None] == jnp.arange(WELLS, dtype=jnp.int32)[None, :]
    ).astype(trans_h.dtype)

    def inverse_of(newton):
        block = acc_block[newton]
        mobile = mobility[newton]
        diag_first = block[0] + mobile[0] * face_total
        diag_second = block[3] + mobile[1] * face_total
        determinant = diag_first * diag_second - block[1] * block[2]
        return (
            diag_second / determinant,
            -block[1] / determinant,
            -block[2] / determinant,
            diag_first / determinant,
        )

    def precondition(inverse, residual):
        inverse_aa, inverse_ab, inverse_ba, inverse_bb = inverse
        return jnp.stack(
            [
                inverse_aa * residual[0] + inverse_ab * residual[1],
                inverse_ba * residual[0] + inverse_bb * residual[1],
            ]
        )

    def slab_shift(value, by):
        count = lax.axis_size("slab")
        return lax.ppermute(value, "slab", [(i, (i + by) % count) for i in range(count)])

    def operator(fields, mobile, block):
        count = fields.shape[0]
        scaled = (mobile * fields).reshape(count * 2, layer_count, column_count)
        picks = gather(scaled, fault_at, split2)
        picks_near = picks[:, :slot_count]
        picks_far = picks[:, slot_count : 2 * slot_count]
        from_left = shifted(jnp.concatenate([scaled[:, :, -1], picks_near], axis=1), "cells", 1)
        from_right = shifted(jnp.concatenate([scaled[:, :, 0], picks_far], axis=1), "cells", -1)
        pressure = fields[:, 0]
        values = gather(pressure, well_at)
        local = jnp.concatenate(
            [
                jnp.dot(well_index, well_onehot, precision=highest)[None],
                jnp.dot(well_index * values, well_onehot, precision=highest),
            ]
        )
        halo_rows = count * 2
        wells = local.shape[1]
        lanes = -(-wells // column_count) * column_count
        well_block = jnp.pad(local, ((0, 0), (0, lanes - wells))).reshape(-1, column_count)
        from_above = slab_shift(jnp.concatenate([scaled[:, -1, :], well_block]), 1)
        from_below = slab_shift(jnp.concatenate([scaled[:, 0, :], well_block]), -1)

        def wells_of(message):
            return message[halo_rows:].reshape(local.shape[0], lanes)[:, :wells]

        summed = local
        if slab_size > 1:
            summed = summed + wells_of(from_above)
        if slab_size > 2:
            summed = summed + wells_of(from_below)
        for by in range(2, slab_size - 1):
            summed = summed + slab_shift(local, by)
        from_above = from_above[:halo_rows]
        from_below = from_below[:halo_rows]
        zero_column = jnp.zeros_like(scaled[:, :, :1])
        west = jnp.concatenate([zero_column, scaled[:, :, :-1]], axis=2)
        east = jnp.concatenate([scaled[:, :, 1:], zero_column], axis=2)
        above = jnp.where(
            layer_ids == 0,
            from_above[:, None, :],
            jnp.pad(scaled[:, :-1, :], ((0, 0), (1, 0), (0, 0))),
        )
        below = jnp.where(
            layer_ids == layer_count - 1,
            from_below[:, None, :],
            jnp.pad(scaled[:, 1:, :], ((0, 0), (0, 1), (0, 0))),
        )
        laplace = (
            trans_east * (scaled - east)
            + trans_west * (scaled - west)
            + trans_down * (scaled - below)
            + trans_up * (scaled - above)
        )
        flux_right = weight_here * (picks_near - from_right[:, layer_count:])
        flux_left = weight_left * (from_left[:, layer_count:] - picks_far)
        fault_term = scatter(
            jnp.concatenate(
                [
                    flux_right,
                    -flux_left,
                    -west_face * from_left[:, :layer_count],
                    -east_face * from_right[:, :layer_count],
                    jnp.zeros((count * 2, edge_pad), scaled.dtype),
                ],
                axis=1,
            ),
            fault_at,
            split2,
        )
        laplace = (laplace + fault_term).reshape(count, 2, layer_count, column_count)
        back = jnp.dot(summed[1:] / summed[0], well_onehot.T, precision=highest)
        well_term = scatter(well_index * (values - back), well_at)
        first = (
            block[:, 0] * fields[:, 0]
            + block[:, 1] * fields[:, 1]
            + laplace[:, 0]
            + well_term
        )
        second = block[:, 2] * fields[:, 0] + block[:, 3] * fields[:, 1] + laplace[:, 1]
        return jnp.stack([first, second], axis=1)

    inverse_last = inverse_of(1)
    inverse_first = inverse_of(0)
    grad_last = grad[1]
    grad_first = grad[0]
    z_last = precondition(inverse_last, grad_last)
    carried = store[0] * z_last
    fields = jnp.stack(
        [z_last, precondition(inverse_first, grad_first), precondition(inverse_first, carried)]
    )
    mobile = jnp.stack([mobility[1], mobility[0], mobility[0]])
    block = jnp.stack([acc_block[1], acc_block[0], acc_block[0]])
    images = operator(fields, mobile, block)
    image_last, direct, coupled = images[0], images[1], images[2]
    first_sums = global_sum(
        stacked_sums(
            [
                (grad_last, image_last),
                (image_last, image_last),
                (grad_last, grad_last),
                (grad_first, direct),
                (grad_first, coupled),
                (carried, direct),
                (carried, coupled),
                (direct, direct),
                (direct, coupled),
                (coupled, coupled),
            ]
        )
    )
    lanes = lax.optimization_barrier(
        jnp.broadcast_to(first_sums[:, None], (first_sums.shape[0], column_count))
    )
    (
        along_last,
        energy_last,
        norm_last,
        grad_direct,
        grad_coupled,
        carried_direct,
        carried_coupled,
        direct_direct,
        direct_coupled,
        coupled_coupled,
    ) = [lanes[i] for i in range(first_sums.shape[0])]
    alpha_last = along_last / energy_last
    along_first = grad_direct + alpha_last * (grad_coupled + carried_direct) + (
        alpha_last * alpha_last
    ) * carried_coupled
    energy_first = direct_direct + (2.0 * alpha_last) * direct_coupled + (
        alpha_last * alpha_last
    ) * coupled_coupled
    alpha_first = along_first / energy_first
    solution_last = alpha_last * z_last
    residual_last = grad_last - alpha_last * image_last
    residual_first = grad_first + store[0] * solution_last
    solution_first = alpha_first * precondition(inverse_first, residual_first)
    image_first = direct + alpha_last * coupled
    closing_first = residual_first - alpha_first * image_first
    second_sums = global_sum(
        stacked_sums(
            [
                (residual_first, residual_first),
                (closing_first, closing_first),
                (grad_last, grad_last),
                (residual_last, residual_last),
            ]
        )
    )
    norms = jnp.sqrt(second_sums).reshape(2, 2)
    return (jnp.stack([solution_first, solution_last]), norms)


def solution(mesh):
    placed = (
        P(None, None, "slab", "cells"),
        P(None, None, "slab", "cells"),
        P(None, None, "slab", "cells"),
        P(None, None, "slab", "cells"),
        P("slab", "cells"),
        P("slab", "cells"),
        P("slab", "cells"),
        P("slab", "cells"),
        P("slab", "cells"),
        P("slab", "cells"),
        P("slab", "cells"),
        P("slab", "cells"),
        P("slab", "cells"),
    )
    return jax.shard_map(
        per_device,
        mesh=mesh,
        in_specs=placed,
        out_specs=(P(None, None, "slab", "cells"), P()),
        check_vma=False,
    )
```

```python
import jax
import jax.numpy as jnp
from jax import lax
from jax.sharding import PartitionSpec as P

WELLS = 16
NSTEPS = 2


def shifted(value, axis, by):
    length = lax.axis_size(axis)
    pairs = [(i, i + by) for i in range(length) if 0 <= i + by < length]
    return lax.ppermute(value, axis, pairs)


def stacked_sums(pairs):
    partial = jnp.stack([jnp.sum(left * right, axis=-2) for left, right in pairs])
    return jnp.sum(partial.reshape(len(pairs), -1), axis=1)


def butterfly(value, axis):
    count = lax.axis_size(axis)
    if count & (count - 1):
        return lax.psum(value, axis)
    step = 1
    while step < count:
        value = value + lax.ppermute(value, axis, [(i, i ^ step) for i in range(count)])
        step *= 2
    return value


def global_sum(values):
    axes = ("cells", "slab")
    count = lax.axis_size("cells") * lax.axis_size("slab")
    copies = jnp.broadcast_to(values[None], (count,) + values.shape)
    gathered = lax.all_to_all(copies, axes, 0, 0, tiled=True)
    return jnp.sum(gathered, axis=0)


def split3(value):
    high = value.astype(jnp.bfloat16)
    rest = value - high.astype(value.dtype)
    middle = rest.astype(jnp.bfloat16)
    low = (rest - middle.astype(value.dtype)).astype(jnp.bfloat16)
    return high, middle, low


def split2(value):
    high = value.astype(jnp.bfloat16)
    low = (value - high.astype(value.dtype)).astype(jnp.bfloat16)
    return high, low


def onehot_dot(value, onehot, dims, split=split3):
    rows = value.shape[0]
    parts = split(value)
    pieces = jnp.concatenate(parts, axis=0)
    part = lax.dot_general(
        pieces, onehot, (dims, ((), ())), preferred_element_type=jnp.float32
    )
    total = part[:rows]
    for index in range(1, len(parts)):
        total = total + part[index * rows : (index + 1) * rows]
    return total


def per_device(
    grad,
    acc_block,
    mobility,
    store,
    trans_h,
    trans_v,
    fault_near,
    fault_far,
    fault_trans,
    fault_count,
    compl_cell,
    compl_well,
    compl_wi,
):
    highest = lax.Precision.HIGHEST
    layer_count, column_count = trans_h.shape
    cells_size = lax.axis_size("cells")
    slab_size = lax.axis_size("slab")
    cells_place = lax.axis_index("cells")
    slab_place = lax.axis_index("slab")
    column_ids = lax.broadcasted_iota(jnp.int32, (layer_count, column_count), 1)
    layer_ids = lax.broadcasted_iota(jnp.int32, (layer_count, column_count), 0)
    zero_value = jnp.zeros((), trans_h.dtype)
    trans_east = jnp.where(
        (cells_place == cells_size - 1) & (column_ids == column_count - 1), zero_value, trans_h
    )
    trans_down = jnp.where(
        (slab_place == slab_size - 1) & (layer_ids == layer_count - 1), zero_value, trans_v
    )
    slot_count = fault_near.size
    slot_live = (jnp.arange(slot_count, dtype=jnp.int32) < fault_count.reshape(())) & (
        cells_place < cells_size - 1
    )
    weight_here = jnp.where(slot_live, fault_trans.reshape(-1), zero_value)
    from_left_setup = shifted(jnp.concatenate([trans_east[:, -1], weight_here]), "cells", 1)
    east_edge = from_left_setup[:layer_count]
    weight_left = from_left_setup[layer_count:]
    down_edge = shifted(trans_down[-1, :], "slab", 1)
    trans_west = jnp.concatenate([east_edge[:, None], trans_east[:, :-1]], axis=1)
    trans_up = jnp.concatenate([down_edge[None, :], trans_down[:-1, :]], axis=0)
    face_total = trans_east + trans_west + trans_down + trans_up

    column_iota = jnp.arange(column_count, dtype=jnp.int32)
    layer_iota = jnp.arange(layer_count, dtype=jnp.int32)

    def locate(cells):
        cells = cells.reshape(-1)
        onehot = (cells % column_count)[:, None] == column_iota[None, :]
        rows = (layer_iota[:, None] == (cells // column_count)[None, :]).astype(jnp.float32)
        return onehot.astype(jnp.float8_e4m3fn), rows

    def gather(field, where, split=split3):
        onehot, rows = where
        parts = field.shape[0]
        flat = field.reshape(parts * layer_count, column_count)
        picked = onehot_dot(flat, onehot, ((1,), (1,)), split)
        picked = picked.reshape(parts, layer_count, -1) * rows[None]
        return jnp.sum(picked, axis=1)

    def scatter(values, where, split=split3):
        onehot, rows = where
        parts = values.shape[0]
        spread = (values[:, None, :] * rows[None]).reshape(parts * layer_count, -1)
        placed = onehot_dot(spread, onehot, ((1,), (0,)), split)
        return placed.reshape(parts, layer_count, column_count)

    edge_cells = jnp.concatenate(
        [layer_iota * column_count, layer_iota * column_count + (column_count - 1)]
    )
    fault_at = locate(
        jnp.concatenate([fault_near.reshape(-1), fault_far.reshape(-1), edge_cells])
    )
    near_at = locate(fault_near)
    far_at = locate(fault_far)
    west_face = east_edge
    east_face = trans_east[:, -1]
    well_at = locate(compl_cell)
    well_index = compl_wi.reshape(-1)
    well_onehot = (
        compl_well.reshape(-1)[:, None] == jnp.arange(WELLS, dtype=jnp.int32)[None, :]
    ).astype(trans_h.dtype)

    def inverse_of(newton):
        block = acc_block[newton]
        mobile = mobility[newton]
        diag_first = block[0] + mobile[0] * face_total
        diag_second = block[3] + mobile[1] * face_total
        determinant = diag_first * diag_second - block[1] * block[2]
        return (
            diag_second / determinant,
            -block[1] / determinant,
            -block[2] / determinant,
            diag_first / determinant,
        )

    def precondition(inverse, residual):
        inverse_aa, inverse_ab, inverse_ba, inverse_bb = inverse
        return jnp.stack(
            [
                inverse_aa * residual[0] + inverse_ab * residual[1],
                inverse_ba * residual[0] + inverse_bb * residual[1],
            ]
        )

    def slab_shift(value, by):
        count = lax.axis_size("slab")
        return lax.ppermute(value, "slab", [(i, (i + by) % count) for i in range(count)])

    def operator(fields, mobile, block):
        count = fields.shape[0]
        scaled = (mobile * fields).reshape(count * 2, layer_count, column_count)
        picks_near = gather(scaled, near_at, split2)
        picks_far = gather(scaled, far_at, split2)
        from_left = shifted(jnp.concatenate([scaled[:, :, -1], picks_near], axis=1), "cells", 1)
        from_right = shifted(jnp.concatenate([scaled[:, :, 0], picks_far], axis=1), "cells", -1)
        pressure = fields[:, 0]
        values = gather(pressure, well_at)
        local = jnp.concatenate(
            [
                jnp.dot(well_index, well_onehot, precision=highest)[None],
                jnp.dot(well_index * values, well_onehot, precision=highest),
            ]
        )
        halo_rows = count * 2
        wells = local.shape[1]
        lanes = -(-wells // column_count) * column_count
        well_block = jnp.pad(local, ((0, 0), (0, lanes - wells))).reshape(-1, column_count)
        from_above = slab_shift(jnp.concatenate([scaled[:, -1, :], well_block]), 1)
        from_below = slab_shift(jnp.concatenate([scaled[:, 0, :], well_block]), -1)

        def wells_of(message):
            return message[halo_rows:].reshape(local.shape[0], lanes)[:, :wells]

        summed = local
        if slab_size > 1:
            summed = summed + wells_of(from_above)
        if slab_size > 2:
            summed = summed + wells_of(from_below)
        for by in range(2, slab_size - 1):
            summed = summed + slab_shift(local, by)
        from_above = from_above[:halo_rows]
        from_below = from_below[:halo_rows]
        zero_column = jnp.zeros_like(scaled[:, :, :1])
        west = jnp.concatenate([zero_column, scaled[:, :, :-1]], axis=2)
        east = jnp.concatenate([scaled[:, :, 1:], zero_column], axis=2)
        above = jnp.where(
            layer_ids == 0,
            from_above[:, None, :],
            jnp.pad(scaled[:, :-1, :], ((0, 0), (1, 0), (0, 0))),
        )
        below = jnp.where(
            layer_ids == layer_count - 1,
            from_below[:, None, :],
            jnp.pad(scaled[:, 1:, :], ((0, 0), (0, 1), (0, 0))),
        )
        laplace = (
            trans_east * (scaled - east)
            + trans_west * (scaled - west)
            + trans_down * (scaled - below)
            + trans_up * (scaled - above)
        )
        flux_right = weight_here * (picks_near - from_right[:, layer_count:])
        flux_left = weight_left * (from_left[:, layer_count:] - picks_far)
        fault_term = scatter(
            jnp.concatenate(
                [
                    flux_right,
                    -flux_left,
                    -west_face * from_left[:, :layer_count],
                    -east_face * from_right[:, :layer_count],
                ],
                axis=1,
            ),
            fault_at,
            split2,
        )
        laplace = (laplace + fault_term).reshape(count, 2, layer_count, column_count)
        back = jnp.dot(summed[1:] / summed[0], well_onehot.T, precision=highest)
        well_term = scatter(well_index * (values - back), well_at)
        first = (
            block[:, 0] * fields[:, 0]
            + block[:, 1] * fields[:, 1]
            + laplace[:, 0]
            + well_term
        )
        second = block[:, 2] * fields[:, 0] + block[:, 3] * fields[:, 1] + laplace[:, 1]
        return jnp.stack([first, second], axis=1)

    inverse_last = inverse_of(1)
    inverse_first = inverse_of(0)
    grad_last = grad[1]
    grad_first = grad[0]
    z_last = precondition(inverse_last, grad_last)
    carried = store[0] * z_last
    fields = jnp.stack(
        [z_last, precondition(inverse_first, grad_first), precondition(inverse_first, carried)]
    )
    mobile = jnp.stack([mobility[1], mobility[0], mobility[0]])
    block = jnp.stack([acc_block[1], acc_block[0], acc_block[0]])
    images = operator(fields, mobile, block)
    image_last, direct, coupled = images[0], images[1], images[2]
    first_sums = global_sum(
        stacked_sums(
            [
                (grad_last, image_last),
                (image_last, image_last),
                (grad_last, grad_last),
                (grad_first, direct),
                (grad_first, coupled),
                (carried, direct),
                (carried, coupled),
                (direct, direct),
                (direct, coupled),
                (coupled, coupled),
            ]
        )
    )
    lanes = lax.optimization_barrier(
        jnp.broadcast_to(first_sums[:, None], (first_sums.shape[0], column_count))
    )
    (
        along_last,
        energy_last,
        norm_last,
        grad_direct,
        grad_coupled,
        carried_direct,
        carried_coupled,
        direct_direct,
        direct_coupled,
        coupled_coupled,
    ) = [lanes[i] for i in range(first_sums.shape[0])]
    alpha_last = along_last / energy_last
    along_first = grad_direct + alpha_last * (grad_coupled + carried_direct) + (
        alpha_last * alpha_last
    ) * carried_coupled
    energy_first = direct_direct + (2.0 * alpha_last) * direct_coupled + (
        alpha_last * alpha_last
    ) * coupled_coupled
    alpha_first = along_first / energy_first
    solution_last = alpha_last * z_last
    residual_last = grad_last - alpha_last * image_last
    residual_first = grad_first + store[0] * solution_last
    solution_first = alpha_first * precondition(inverse_first, residual_first)
    image_first = direct + alpha_last * coupled
    closing_first = residual_first - alpha_first * image_first
    second_sums = global_sum(
        stacked_sums(
            [
                (residual_first, residual_first),
                (closing_first, closing_first),
                (grad_last, grad_last),
                (residual_last, residual_last),
            ]
        )
    )
    norms = jnp.sqrt(second_sums).reshape(2, 2)
    return (jnp.stack([solution_first, solution_last]), norms)


def solution(mesh):
    placed = (
        P(None, None, "slab", "cells"),
        P(None, None, "slab", "cells"),
        P(None, None, "slab", "cells"),
        P(None, None, "slab", "cells"),
        P("slab", "cells"),
        P("slab", "cells"),
        P("slab", "cells"),
        P("slab", "cells"),
        P("slab", "cells"),
        P("slab", "cells"),
        P("slab", "cells"),
        P("slab", "cells"),
        P("slab", "cells"),
    )
    return jax.shard_map(
        per_device,
        mesh=mesh,
        in_specs=placed,
        out_specs=(P(None, None, "slab", "cells"), P()),
        check_vma=False,
    )
```

```python
import jax
import jax.numpy as jnp
from jax import lax
from jax.sharding import PartitionSpec as P

WELLS = 16
NSTEPS = 2


def shifted(value, axis, by):
    length = lax.axis_size(axis)
    pairs = [(i, i + by) for i in range(length) if 0 <= i + by < length]
    return lax.ppermute(value, axis, pairs)


def stacked_sums(pairs):
    partial = jnp.stack([jnp.sum(left * right, axis=-2) for left, right in pairs])
    return jnp.sum(partial.reshape(len(pairs), -1), axis=1)


def butterfly(value, axis):
    count = lax.axis_size(axis)
    if count & (count - 1):
        return lax.psum(value, axis)
    step = 1
    while step < count:
        value = value + lax.ppermute(value, axis, [(i, i ^ step) for i in range(count)])
        step *= 2
    return value


def global_sum(values):
    axes = ("cells", "slab")
    count = lax.axis_size("cells") * lax.axis_size("slab")
    copies = jnp.broadcast_to(values[None], (count,) + values.shape)
    gathered = lax.all_to_all(copies, axes, 0, 0, tiled=True)
    return jnp.sum(gathered, axis=0)


def split3(value):
    high = value.astype(jnp.bfloat16)
    rest = value - high.astype(value.dtype)
    middle = rest.astype(jnp.bfloat16)
    low = (rest - middle.astype(value.dtype)).astype(jnp.bfloat16)
    return high, middle, low


def split2(value):
    high = value.astype(jnp.bfloat16)
    low = (value - high.astype(value.dtype)).astype(jnp.bfloat16)
    return high, low


def onehot_dot(value, onehot, dims, split=split3):
    rows = value.shape[0]
    parts = split(value)
    pieces = jnp.concatenate(parts, axis=0)
    part = lax.dot_general(
        pieces, onehot, (dims, ((), ())), preferred_element_type=jnp.float32
    )
    total = part[:rows]
    for index in range(1, len(parts)):
        total = total + part[index * rows : (index + 1) * rows]
    return total


def per_device(
    grad,
    acc_block,
    mobility,
    store,
    trans_h,
    trans_v,
    fault_near,
    fault_far,
    fault_trans,
    fault_count,
    compl_cell,
    compl_well,
    compl_wi,
):
    highest = lax.Precision.HIGHEST
    layer_count, column_count = trans_h.shape
    cells_size = lax.axis_size("cells")
    slab_size = lax.axis_size("slab")
    cells_place = lax.axis_index("cells")
    slab_place = lax.axis_index("slab")
    column_ids = lax.broadcasted_iota(jnp.int32, (layer_count, column_count), 1)
    layer_ids = lax.broadcasted_iota(jnp.int32, (layer_count, column_count), 0)
    zero_value = jnp.zeros((), trans_h.dtype)
    trans_east = jnp.where(
        (cells_place == cells_size - 1) & (column_ids == column_count - 1), zero_value, trans_h
    )
    trans_down = jnp.where(
        (slab_place == slab_size - 1) & (layer_ids == layer_count - 1), zero_value, trans_v
    )
    slot_count = fault_near.size
    slot_live = (jnp.arange(slot_count, dtype=jnp.int32) < fault_count.reshape(())) & (
        cells_place < cells_size - 1
    )
    weight_here = jnp.where(slot_live, fault_trans.reshape(-1), zero_value)
    from_left_setup = shifted(jnp.concatenate([trans_east[:, -1], weight_here]), "cells", 1)
    east_edge = from_left_setup[:layer_count]
    weight_left = from_left_setup[layer_count:]
    down_edge = shifted(trans_down[-1, :], "slab", 1)
    trans_west = jnp.concatenate([east_edge[:, None], trans_east[:, :-1]], axis=1)
    trans_up = jnp.concatenate([down_edge[None, :], trans_down[:-1, :]], axis=0)
    face_total = trans_east + trans_west + trans_down + trans_up

    column_iota = jnp.arange(column_count, dtype=jnp.int32)
    layer_iota = jnp.arange(layer_count, dtype=jnp.int32)

    def locate(cells):
        cells = cells.reshape(-1)
        onehot = (cells % column_count)[:, None] == column_iota[None, :]
        rows = (layer_iota[:, None] == (cells // column_count)[None, :]).astype(jnp.float32)
        return onehot.astype(jnp.float8_e4m3fn), rows

    def gather(field, where, split=split3):
        onehot, rows = where
        parts = field.shape[0]
        flat = field.reshape(parts * layer_count, column_count)
        picked = onehot_dot(flat, onehot, ((1,), (1,)), split)
        picked = picked.reshape(parts, layer_count, -1) * rows[None]
        return jnp.sum(picked, axis=1)

    def scatter(values, where, split=split3):
        onehot, rows = where
        parts = values.shape[0]
        spread = (values[:, None, :] * rows[None]).reshape(parts * layer_count, -1)
        placed = onehot_dot(spread, onehot, ((1,), (0,)), split)
        return placed.reshape(parts, layer_count, column_count)

    edge_cells = jnp.concatenate(
        [layer_iota * column_count, layer_iota * column_count + (column_count - 1)]
    )
    fault_at = locate(
        jnp.concatenate([fault_near.reshape(-1), fault_far.reshape(-1), edge_cells])
    )
    west_face = east_edge
    east_face = trans_east[:, -1]
    well_at = locate(compl_cell)
    well_index = compl_wi.reshape(-1)
    well_onehot = (
        compl_well.reshape(-1)[:, None] == jnp.arange(WELLS, dtype=jnp.int32)[None, :]
    ).astype(trans_h.dtype)

    def inverse_of(newton):
        block = acc_block[newton]
        mobile = mobility[newton]
        diag_first = block[0] + mobile[0] * face_total
        diag_second = block[3] + mobile[1] * face_total
        determinant = diag_first * diag_second - block[1] * block[2]
        scale = 1.0 / determinant
        return (
            diag_second * scale,
            -block[1] * scale,
            -block[2] * scale,
            diag_first * scale,
        )

    def precondition(inverse, residual):
        inverse_aa, inverse_ab, inverse_ba, inverse_bb = inverse
        return jnp.stack(
            [
                inverse_aa * residual[0] + inverse_ab * residual[1],
                inverse_ba * residual[0] + inverse_bb * residual[1],
            ]
        )

    def slab_shift(value, by):
        count = lax.axis_size("slab")
        return lax.ppermute(value, "slab", [(i, (i + by) % count) for i in range(count)])

    def operator(fields, mobile, block):
        count = fields.shape[0]
        scaled = (mobile * fields).reshape(count * 2, layer_count, column_count)
        picks = gather(scaled, fault_at, split2)
        picks_near = picks[:, :slot_count]
        picks_far = picks[:, slot_count : 2 * slot_count]
        from_left = shifted(jnp.concatenate([scaled[:, :, -1], picks_near], axis=1), "cells", 1)
        from_right = shifted(jnp.concatenate([scaled[:, :, 0], picks_far], axis=1), "cells", -1)
        pressure = fields[:, 0]
        values = gather(pressure, well_at)
        local = jnp.concatenate(
            [
                jnp.dot(well_index, well_onehot, precision=highest)[None],
                jnp.dot(well_index * values, well_onehot, precision=highest),
            ]
        )
        halo_rows = count * 2
        wells = local.shape[1]
        lanes = -(-wells // column_count) * column_count
        well_block = jnp.pad(local, ((0, 0), (0, lanes - wells))).reshape(-1, column_count)
        from_above = slab_shift(jnp.concatenate([scaled[:, -1, :], well_block]), 1)
        from_below = slab_shift(jnp.concatenate([scaled[:, 0, :], well_block]), -1)

        def wells_of(message):
            return message[halo_rows:].reshape(local.shape[0], lanes)[:, :wells]

        summed = local
        if slab_size > 1:
            summed = summed + wells_of(from_above)
        if slab_size > 2:
            summed = summed + wells_of(from_below)
        for by in range(2, slab_size - 1):
            summed = summed + slab_shift(local, by)
        from_above = from_above[:halo_rows]
        from_below = from_below[:halo_rows]
        zero_column = jnp.zeros_like(scaled[:, :, :1])
        west = jnp.concatenate([zero_column, scaled[:, :, :-1]], axis=2)
        east = jnp.concatenate([scaled[:, :, 1:], zero_column], axis=2)
        above = jnp.where(
            layer_ids == 0,
            from_above[:, None, :],
            jnp.pad(scaled[:, :-1, :], ((0, 0), (1, 0), (0, 0))),
        )
        below = jnp.where(
            layer_ids == layer_count - 1,
            from_below[:, None, :],
            jnp.pad(scaled[:, 1:, :], ((0, 0), (0, 1), (0, 0))),
        )
        laplace = (
            trans_east * (scaled - east)
            + trans_west * (scaled - west)
            + trans_down * (scaled - below)
            + trans_up * (scaled - above)
        )
        flux_right = weight_here * (picks_near - from_right[:, layer_count:])
        flux_left = weight_left * (from_left[:, layer_count:] - picks_far)
        fault_term = scatter(
            jnp.concatenate(
                [
                    flux_right,
                    -flux_left,
                    -west_face * from_left[:, :layer_count],
                    -east_face * from_right[:, :layer_count],
                ],
                axis=1,
            ),
            fault_at,
            split2,
        )
        laplace = (laplace + fault_term).reshape(count, 2, layer_count, column_count)
        back = jnp.dot(summed[1:] / summed[0], well_onehot.T, precision=highest)
        well_term = scatter(well_index * (values - back), well_at)
        first = (
            block[:, 0] * fields[:, 0]
            + block[:, 1] * fields[:, 1]
            + laplace[:, 0]
            + well_term
        )
        second = block[:, 2] * fields[:, 0] + block[:, 3] * fields[:, 1] + laplace[:, 1]
        return jnp.stack([first, second], axis=1)

    inverse_last = inverse_of(1)
    inverse_first = inverse_of(0)
    grad_last = grad[1]
    grad_first = grad[0]
    z_last = precondition(inverse_last, grad_last)
    carried = store[0] * z_last
    fields = jnp.stack(
        [z_last, precondition(inverse_first, grad_first), precondition(inverse_first, carried)]
    )
    mobile = jnp.stack([mobility[1], mobility[0], mobility[0]])
    block = jnp.stack([acc_block[1], acc_block[0], acc_block[0]])
    images = operator(fields, mobile, block)
    image_last, direct, coupled = images[0], images[1], images[2]
    first_sums = global_sum(
        stacked_sums(
            [
                (grad_last, image_last),
                (image_last, image_last),
                (grad_last, grad_last),
                (grad_first, direct),
                (grad_first, coupled),
                (carried, direct),
                (carried, coupled),
                (direct, direct),
                (direct, coupled),
                (coupled, coupled),
            ]
        )
    )
    lanes = lax.optimization_barrier(
        jnp.broadcast_to(first_sums[:, None], (first_sums.shape[0], column_count))
    )
    (
        along_last,
        energy_last,
        norm_last,
        grad_direct,
        grad_coupled,
        carried_direct,
        carried_coupled,
        direct_direct,
        direct_coupled,
        coupled_coupled,
    ) = [lanes[i] for i in range(first_sums.shape[0])]
    alpha_last = along_last / energy_last
    along_first = grad_direct + alpha_last * (grad_coupled + carried_direct) + (
        alpha_last * alpha_last
    ) * carried_coupled
    energy_first = direct_direct + (2.0 * alpha_last) * direct_coupled + (
        alpha_last * alpha_last
    ) * coupled_coupled
    alpha_first = along_first / energy_first
    solution_last = alpha_last * z_last
    residual_last = grad_last - alpha_last * image_last
    residual_first = grad_first + store[0] * solution_last
    solution_first = alpha_first * precondition(inverse_first, residual_first)
    image_first = direct + alpha_last * coupled
    closing_first = residual_first - alpha_first * image_first
    second_sums = global_sum(
        stacked_sums(
            [
                (residual_first, residual_first),
                (closing_first, closing_first),
                (grad_last, grad_last),
                (residual_last, residual_last),
            ]
        )
    )
    norms = jnp.sqrt(second_sums).reshape(2, 2)
    return (jnp.stack([solution_first, solution_last]), norms)


def solution(mesh):
    placed = (
        P(None, None, "slab", "cells"),
        P(None, None, "slab", "cells"),
        P(None, None, "slab", "cells"),
        P(None, None, "slab", "cells"),
        P("slab", "cells"),
        P("slab", "cells"),
        P("slab", "cells"),
        P("slab", "cells"),
        P("slab", "cells"),
        P("slab", "cells"),
        P("slab", "cells"),
        P("slab", "cells"),
        P("slab", "cells"),
    )
    return jax.shard_map(
        per_device,
        mesh=mesh,
        in_specs=placed,
        out_specs=(P(None, None, "slab", "cells"), P()),
        check_vma=False,
    )
```

```python
import jax
import jax.numpy as jnp
from jax import lax
from jax.sharding import PartitionSpec as P

WELLS = 16
NSTEPS = 2


def shifted(value, axis, by):
    length = lax.axis_size(axis)
    pairs = [(i, i + by) for i in range(length) if 0 <= i + by < length]
    return lax.ppermute(value, axis, pairs)


def stacked_sums(pairs):
    partial = jnp.stack([jnp.sum(left * right, axis=-2) for left, right in pairs])
    return jnp.sum(partial.reshape(len(pairs), -1), axis=1)


def butterfly(value, axis):
    count = lax.axis_size(axis)
    if count & (count - 1):
        return lax.psum(value, axis)
    step = 1
    while step < count:
        value = value + lax.ppermute(value, axis, [(i, i ^ step) for i in range(count)])
        step *= 2
    return value


def global_sum(values):
    axes = ("cells", "slab")
    count = lax.axis_size("cells") * lax.axis_size("slab")
    copies = jnp.broadcast_to(values[None], (count,) + values.shape)
    gathered = lax.all_to_all(copies, axes, 0, 0, tiled=True)
    return jnp.sum(gathered, axis=0)


def split3(value):
    high = value.astype(jnp.bfloat16)
    rest = value - high.astype(value.dtype)
    middle = rest.astype(jnp.bfloat16)
    low = (rest - middle.astype(value.dtype)).astype(jnp.bfloat16)
    return high, middle, low


def split2(value):
    high = value.astype(jnp.bfloat16)
    low = (value - high.astype(value.dtype)).astype(jnp.bfloat16)
    return high, low


def onehot_dot(value, onehot, dims, split=split3):
    rows = value.shape[0]
    parts = split(value)
    pieces = jnp.concatenate(parts, axis=0)
    part = lax.dot_general(
        pieces, onehot, (dims, ((), ())), preferred_element_type=jnp.float32
    )
    total = part[:rows]
    for index in range(1, len(parts)):
        total = total + part[index * rows : (index + 1) * rows]
    return total


def per_device(
    grad,
    acc_block,
    mobility,
    store,
    trans_h,
    trans_v,
    fault_near,
    fault_far,
    fault_trans,
    fault_count,
    compl_cell,
    compl_well,
    compl_wi,
):
    highest = lax.Precision.HIGHEST
    layer_count, column_count = trans_h.shape
    cells_size = lax.axis_size("cells")
    slab_size = lax.axis_size("slab")
    cells_place = lax.axis_index("cells")
    slab_place = lax.axis_index("slab")
    column_ids = lax.broadcasted_iota(jnp.int32, (layer_count, column_count), 1)
    layer_ids = lax.broadcasted_iota(jnp.int32, (layer_count, column_count), 0)
    zero_value = jnp.zeros((), trans_h.dtype)
    trans_east = jnp.where(
        (cells_place == cells_size - 1) & (column_ids == column_count - 1), zero_value, trans_h
    )
    trans_down = jnp.where(
        (slab_place == slab_size - 1) & (layer_ids == layer_count - 1), zero_value, trans_v
    )
    slot_count = fault_near.size
    slot_live = (jnp.arange(slot_count, dtype=jnp.int32) < fault_count.reshape(())) & (
        cells_place < cells_size - 1
    )
    weight_here = jnp.where(slot_live, fault_trans.reshape(-1), zero_value)
    from_left_setup = shifted(jnp.concatenate([trans_east[:, -1], weight_here]), "cells", 1)
    east_edge = from_left_setup[:layer_count]
    weight_left = from_left_setup[layer_count:]
    down_edge = shifted(trans_down[-1, :], "slab", 1)
    trans_west = jnp.concatenate([east_edge[:, None], trans_east[:, :-1]], axis=1)
    trans_up = jnp.concatenate([down_edge[None, :], trans_down[:-1, :]], axis=0)
    face_total = trans_east + trans_west + trans_down + trans_up

    column_iota = jnp.arange(column_count, dtype=jnp.int32)
    layer_iota = jnp.arange(layer_count, dtype=jnp.int32)

    def locate(cells):
        cells = cells.reshape(-1)
        onehot = (cells % column_count)[:, None] == column_iota[None, :]
        rows = (layer_iota[:, None] == (cells // column_count)[None, :]).astype(jnp.float32)
        return onehot.astype(jnp.float8_e4m3fn), rows

    def gather(field, where, split=split3):
        onehot, rows = where
        parts = field.shape[0]
        flat = field.reshape(parts * layer_count, column_count)
        picked = onehot_dot(flat, onehot, ((1,), (1,)), split)
        picked = picked.reshape(parts, layer_count, -1) * rows[None]
        return jnp.sum(picked, axis=1)

    def scatter(values, where, split=split3):
        onehot, rows = where
        parts = values.shape[0]
        spread = (values[:, None, :] * rows[None]).reshape(parts * layer_count, -1)
        placed = onehot_dot(spread, onehot, ((1,), (0,)), split)
        return placed.reshape(parts, layer_count, column_count)

    edge_cells = jnp.concatenate(
        [layer_iota * column_count, layer_iota * column_count + (column_count - 1)]
    )
    fault_at = locate(
        jnp.concatenate(
            [fault_near.reshape(-1), fault_far.reshape(-1), edge_cells, compl_cell.reshape(-1)]
        )
    )
    west_face = east_edge
    east_face = trans_east[:, -1]
    well_at = locate(compl_cell)
    well_index = compl_wi.reshape(-1)
    well_onehot = (
        compl_well.reshape(-1)[:, None] == jnp.arange(WELLS, dtype=jnp.int32)[None, :]
    ).astype(trans_h.dtype)

    def inverse_of(newton):
        block = acc_block[newton]
        mobile = mobility[newton]
        diag_first = block[0] + mobile[0] * face_total
        diag_second = block[3] + mobile[1] * face_total
        determinant = diag_first * diag_second - block[1] * block[2]
        scale = 1.0 / determinant
        return (
            diag_second * scale,
            -block[1] * scale,
            -block[2] * scale,
            diag_first * scale,
        )

    def precondition(inverse, residual):
        inverse_aa, inverse_ab, inverse_ba, inverse_bb = inverse
        return jnp.stack(
            [
                inverse_aa * residual[0] + inverse_ab * residual[1],
                inverse_ba * residual[0] + inverse_bb * residual[1],
            ]
        )

    def slab_shift(value, by):
        count = lax.axis_size("slab")
        return lax.ppermute(value, "slab", [(i, (i + by) % count) for i in range(count)])

    def operator(fields, mobile, block):
        count = fields.shape[0]
        scaled = (mobile * fields).reshape(count * 2, layer_count, column_count)
        picks = gather(scaled, fault_at, split2)
        picks_near = picks[:, :slot_count]
        picks_far = picks[:, slot_count : 2 * slot_count]
        from_left = shifted(jnp.concatenate([scaled[:, :, -1], picks_near], axis=1), "cells", 1)
        from_right = shifted(jnp.concatenate([scaled[:, :, 0], picks_far], axis=1), "cells", -1)
        pressure = fields[:, 0]
        values = gather(pressure, well_at)
        local = jnp.concatenate(
            [
                jnp.dot(well_index, well_onehot, precision=highest)[None],
                jnp.dot(well_index * values, well_onehot, precision=highest),
            ]
        )
        halo_rows = count * 2
        wells = local.shape[1]
        lanes = -(-wells // column_count) * column_count
        well_block = jnp.pad(local, ((0, 0), (0, lanes - wells))).reshape(-1, column_count)
        from_above = slab_shift(jnp.concatenate([scaled[:, -1, :], well_block]), 1)
        from_below = slab_shift(jnp.concatenate([scaled[:, 0, :], well_block]), -1)

        def wells_of(message):
            return message[halo_rows:].reshape(local.shape[0], lanes)[:, :wells]

        summed = local
        if slab_size > 1:
            summed = summed + wells_of(from_above)
        if slab_size > 2:
            summed = summed + wells_of(from_below)
        for by in range(2, slab_size - 1):
            summed = summed + slab_shift(local, by)
        from_above = from_above[:halo_rows]
        from_below = from_below[:halo_rows]
        zero_column = jnp.zeros_like(scaled[:, :, :1])
        west = jnp.concatenate([zero_column, scaled[:, :, :-1]], axis=2)
        east = jnp.concatenate([scaled[:, :, 1:], zero_column], axis=2)
        above = jnp.where(
            layer_ids == 0,
            from_above[:, None, :],
            jnp.pad(scaled[:, :-1, :], ((0, 0), (1, 0), (0, 0))),
        )
        below = jnp.where(
            layer_ids == layer_count - 1,
            from_below[:, None, :],
            jnp.pad(scaled[:, 1:, :], ((0, 0), (0, 1), (0, 0))),
        )
        laplace = (
            trans_east * (scaled - east)
            + trans_west * (scaled - west)
            + trans_down * (scaled - below)
            + trans_up * (scaled - above)
        )
        flux_right = weight_here * (picks_near - from_right[:, layer_count:])
        flux_left = weight_left * (from_left[:, layer_count:] - picks_far)
        back = jnp.dot(summed[1:] / summed[0], well_onehot.T, precision=highest)
        well_values = well_index * (values - back)
        well_values = jnp.stack([well_values, jnp.zeros_like(well_values)], axis=1)
        fault_term = scatter(
            jnp.concatenate(
                [
                    flux_right,
                    -flux_left,
                    -west_face * from_left[:, :layer_count],
                    -east_face * from_right[:, :layer_count],
                    well_values.reshape(count * 2, -1),
                ],
                axis=1,
            ),
            fault_at,
            split2,
        )
        laplace = (laplace + fault_term).reshape(count, 2, layer_count, column_count)
        first = block[:, 0] * fields[:, 0] + block[:, 1] * fields[:, 1] + laplace[:, 0]
        second = block[:, 2] * fields[:, 0] + block[:, 3] * fields[:, 1] + laplace[:, 1]
        return jnp.stack([first, second], axis=1)

    inverse_last = inverse_of(1)
    inverse_first = inverse_of(0)
    grad_last = grad[1]
    grad_first = grad[0]
    z_last = precondition(inverse_last, grad_last)
    carried = store[0] * z_last
    fields = jnp.stack(
        [z_last, precondition(inverse_first, grad_first), precondition(inverse_first, carried)]
    )
    mobile = jnp.stack([mobility[1], mobility[0], mobility[0]])
    block = jnp.stack([acc_block[1], acc_block[0], acc_block[0]])
    images = operator(fields, mobile, block)
    image_last, direct, coupled = images[0], images[1], images[2]
    first_sums = global_sum(
        stacked_sums(
            [
                (grad_last, image_last),
                (image_last, image_last),
                (grad_last, grad_last),
                (grad_first, direct),
                (grad_first, coupled),
                (carried, direct),
                (carried, coupled),
                (direct, direct),
                (direct, coupled),
                (coupled, coupled),
            ]
        )
    )
    lanes = lax.optimization_barrier(
        jnp.broadcast_to(first_sums[:, None], (first_sums.shape[0], column_count))
    )
    (
        along_last,
        energy_last,
        norm_last,
        grad_direct,
        grad_coupled,
        carried_direct,
        carried_coupled,
        direct_direct,
        direct_coupled,
        coupled_coupled,
    ) = [lanes[i] for i in range(first_sums.shape[0])]
    alpha_last = along_last / energy_last
    along_first = grad_direct + alpha_last * (grad_coupled + carried_direct) + (
        alpha_last * alpha_last
    ) * carried_coupled
    energy_first = direct_direct + (2.0 * alpha_last) * direct_coupled + (
        alpha_last * alpha_last
    ) * coupled_coupled
    alpha_first = along_first / energy_first
    solution_last = alpha_last * z_last
    residual_last = grad_last - alpha_last * image_last
    residual_first = grad_first + store[0] * solution_last
    solution_first = alpha_first * precondition(inverse_first, residual_first)
    image_first = direct + alpha_last * coupled
    closing_first = residual_first - alpha_first * image_first
    second_sums = global_sum(
        stacked_sums(
            [
                (residual_first, residual_first),
                (closing_first, closing_first),
                (grad_last, grad_last),
                (residual_last, residual_last),
            ]
        )
    )
    norms = jnp.sqrt(second_sums).reshape(2, 2)
    return (jnp.stack([solution_first, solution_last]), norms)


def solution(mesh):
    placed = (
        P(None, None, "slab", "cells"),
        P(None, None, "slab", "cells"),
        P(None, None, "slab", "cells"),
        P(None, None, "slab", "cells"),
        P("slab", "cells"),
        P("slab", "cells"),
        P("slab", "cells"),
        P("slab", "cells"),
        P("slab", "cells"),
        P("slab", "cells"),
        P("slab", "cells"),
        P("slab", "cells"),
        P("slab", "cells"),
    )
    return jax.shard_map(
        per_device,
        mesh=mesh,
        in_specs=placed,
        out_specs=(P(None, None, "slab", "cells"), P()),
        check_vma=False,
    )
```

```python
import jax
import jax.numpy as jnp
from jax import lax
from jax.sharding import PartitionSpec as P

WELLS = 16
NSTEPS = 2


def shifted(value, axis, by):
    length = lax.axis_size(axis)
    pairs = [(i, i + by) for i in range(length) if 0 <= i + by < length]
    return lax.ppermute(value, axis, pairs)


def stacked_sums(pairs):
    partial = jnp.stack([jnp.sum(left * right, axis=-2) for left, right in pairs])
    return jnp.sum(partial.reshape(len(pairs), -1), axis=1)


def butterfly(value, axis):
    count = lax.axis_size(axis)
    if count & (count - 1):
        return lax.psum(value, axis)
    step = 1
    while step < count:
        value = value + lax.ppermute(value, axis, [(i, i ^ step) for i in range(count)])
        step *= 2
    return value


def global_sum(values):
    axes = ("cells", "slab")
    count = lax.axis_size("cells") * lax.axis_size("slab")
    copies = jnp.broadcast_to(values[None], (count,) + values.shape)
    gathered = lax.all_to_all(copies, axes, 0, 0, tiled=True)
    return jnp.sum(gathered, axis=0)


def split3(value):
    high = value.astype(jnp.bfloat16)
    rest = value - high.astype(value.dtype)
    middle = rest.astype(jnp.bfloat16)
    low = (rest - middle.astype(value.dtype)).astype(jnp.bfloat16)
    return high, middle, low


def split2(value):
    high = value.astype(jnp.bfloat16)
    low = (value - high.astype(value.dtype)).astype(jnp.bfloat16)
    return high, low


def onehot_dot(value, onehot, dims, split=split3):
    rows = value.shape[0]
    parts = split(value)
    pieces = jnp.concatenate(parts, axis=0)
    part = lax.dot_general(
        pieces, onehot, (dims, ((), ())), preferred_element_type=jnp.float32
    )
    total = part[:rows]
    for index in range(1, len(parts)):
        total = total + part[index * rows : (index + 1) * rows]
    return total


def per_device(
    grad,
    acc_block,
    mobility,
    store,
    trans_h,
    trans_v,
    fault_near,
    fault_far,
    fault_trans,
    fault_count,
    compl_cell,
    compl_well,
    compl_wi,
):
    highest = lax.Precision.HIGHEST
    layer_count, column_count = trans_h.shape
    cells_size = lax.axis_size("cells")
    slab_size = lax.axis_size("slab")
    cells_place = lax.axis_index("cells")
    slab_place = lax.axis_index("slab")
    column_ids = lax.broadcasted_iota(jnp.int32, (layer_count, column_count), 1)
    layer_ids = lax.broadcasted_iota(jnp.int32, (layer_count, column_count), 0)
    zero_value = jnp.zeros((), trans_h.dtype)
    trans_east = jnp.where(
        (cells_place == cells_size - 1) & (column_ids == column_count - 1), zero_value, trans_h
    )
    trans_down = jnp.where(
        (slab_place == slab_size - 1) & (layer_ids == layer_count - 1), zero_value, trans_v
    )
    slot_count = fault_near.size
    slot_live = (jnp.arange(slot_count, dtype=jnp.int32) < fault_count.reshape(())) & (
        cells_place < cells_size - 1
    )
    weight_here = jnp.where(slot_live, fault_trans.reshape(-1), zero_value)
    from_left_setup = shifted(jnp.concatenate([trans_east[:, -1], weight_here]), "cells", 1)
    east_edge = from_left_setup[:layer_count]
    weight_left = from_left_setup[layer_count:]
    down_edge = shifted(trans_down[-1, :], "slab", 1)
    trans_west = jnp.concatenate([east_edge[:, None], trans_east[:, :-1]], axis=1)
    trans_up = jnp.concatenate([down_edge[None, :], trans_down[:-1, :]], axis=0)
    face_total = trans_east + trans_west + trans_down + trans_up

    column_iota = jnp.arange(column_count, dtype=jnp.int32)
    layer_iota = jnp.arange(layer_count, dtype=jnp.int32)

    def locate(cells):
        cells = cells.reshape(-1)
        onehot = (cells % column_count)[:, None] == column_iota[None, :]
        rows = (layer_iota[:, None] == (cells // column_count)[None, :]).astype(jnp.float32)
        return onehot.astype(jnp.float8_e4m3fn), rows

    def gather(field, where, split=split3):
        onehot, rows = where
        parts = field.shape[0]
        flat = field.reshape(parts * layer_count, column_count)
        picked = onehot_dot(flat, onehot, ((1,), (1,)), split)
        picked = picked.reshape(parts, layer_count, -1) * rows[None]
        return jnp.sum(picked, axis=1)

    def scatter(values, where, split=split3):
        onehot, rows = where
        parts = values.shape[0]
        spread = (values[:, None, :] * rows[None]).reshape(parts * layer_count, -1)
        placed = onehot_dot(spread, onehot, ((1,), (0,)), split)
        return placed.reshape(parts, layer_count, column_count)

    edge_cells = jnp.concatenate(
        [layer_iota * column_count, layer_iota * column_count + (column_count - 1)]
    )
    fault_at = locate(
        jnp.concatenate([fault_near.reshape(-1), fault_far.reshape(-1), edge_cells])
    )
    west_face = east_edge
    east_face = trans_east[:, -1]
    well_at = locate(compl_cell)
    well_index = compl_wi.reshape(-1)
    well_onehot = (
        compl_well.reshape(-1)[:, None] == jnp.arange(WELLS, dtype=jnp.int32)[None, :]
    ).astype(trans_h.dtype)

    def inverse_of(newton):
        block = acc_block[newton]
        mobile = mobility[newton]
        diag_first = block[0] + mobile[0] * face_total
        diag_second = block[3] + mobile[1] * face_total
        determinant = diag_first * diag_second - block[1] * block[2]
        scale = 1.0 / determinant
        return (
            diag_second * scale,
            -block[1] * scale,
            -block[2] * scale,
            diag_first * scale,
        )

    def precondition(inverse, residual):
        inverse_aa, inverse_ab, inverse_ba, inverse_bb = inverse
        return jnp.stack(
            [
                inverse_aa * residual[0] + inverse_ab * residual[1],
                inverse_ba * residual[0] + inverse_bb * residual[1],
            ]
        )

    def slab_shift(value, by):
        count = lax.axis_size("slab")
        return lax.ppermute(value, "slab", [(i, (i + by) % count) for i in range(count)])

    def operator(fields, mobile, block):
        count = fields.shape[0]
        scaled = (mobile * fields).reshape(count * 2, layer_count, column_count)
        picks = gather(scaled, fault_at, split2)
        picks_near = picks[:, :slot_count]
        picks_far = picks[:, slot_count : 2 * slot_count]
        from_left = shifted(jnp.concatenate([scaled[:, :, -1], picks_near], axis=1), "cells", 1)
        from_right = shifted(jnp.concatenate([scaled[:, :, 0], picks_far], axis=1), "cells", -1)
        pressure = fields[:, 0]
        values = gather(pressure, well_at)
        local = jnp.concatenate(
            [
                jnp.dot(well_index, well_onehot, precision=highest)[None],
                jnp.dot(well_index * values, well_onehot, precision=highest),
            ]
        )
        halo_rows = count * 2
        wells = local.shape[1]
        lanes = -(-wells // column_count) * column_count
        well_block = jnp.pad(local, ((0, 0), (0, lanes - wells))).reshape(-1, column_count)
        from_above = slab_shift(jnp.concatenate([scaled[:, -1, :], well_block]), 1)
        from_below = slab_shift(jnp.concatenate([scaled[:, 0, :], well_block]), -1)

        def wells_of(message):
            return message[halo_rows:].reshape(local.shape[0], lanes)[:, :wells]

        summed = local
        if slab_size > 1:
            summed = summed + wells_of(from_above)
        if slab_size > 2:
            summed = summed + wells_of(from_below)
        for by in range(2, slab_size - 1):
            summed = summed + slab_shift(local, by)
        from_above = from_above[:halo_rows]
        from_below = from_below[:halo_rows]
        zero_column = jnp.zeros_like(scaled[:, :, :1])
        west = jnp.concatenate([zero_column, scaled[:, :, :-1]], axis=2)
        east = jnp.concatenate([scaled[:, :, 1:], zero_column], axis=2)
        above = jnp.where(
            layer_ids == 0,
            from_above[:, None, :],
            jnp.pad(scaled[:, :-1, :], ((0, 0), (1, 0), (0, 0))),
        )
        below = jnp.where(
            layer_ids == layer_count - 1,
            from_below[:, None, :],
            jnp.pad(scaled[:, 1:, :], ((0, 0), (0, 1), (0, 0))),
        )
        laplace = (
            trans_east * (scaled - east)
            + trans_west * (scaled - west)
            + trans_down * (scaled - below)
            + trans_up * (scaled - above)
        )
        flux_right = weight_here * (picks_near - from_right[:, layer_count:])
        flux_left = weight_left * (from_left[:, layer_count:] - picks_far)
        fault_term = scatter(
            jnp.concatenate(
                [
                    flux_right,
                    -flux_left,
                    -west_face * from_left[:, :layer_count],
                    -east_face * from_right[:, :layer_count],
                ],
                axis=1,
            ),
            fault_at,
            split2,
        )
        laplace = (laplace + fault_term).reshape(count, 2, layer_count, column_count)
        back = jnp.dot(summed[1:] / summed[0], well_onehot.T, precision=highest)
        well_term = scatter(well_index * (values - back), well_at)
        first = (
            block[:, 0] * fields[:, 0]
            + block[:, 1] * fields[:, 1]
            + laplace[:, 0]
            + well_term
        )
        second = block[:, 2] * fields[:, 0] + block[:, 3] * fields[:, 1] + laplace[:, 1]
        return jnp.stack([first, second], axis=1)

    inverse_last = inverse_of(1)
    inverse_first = inverse_of(0)
    grad_last = grad[1]
    grad_first = grad[0]
    z_last = precondition(inverse_last, grad_last)
    carried = store[0] * z_last
    fields = jnp.stack(
        [z_last, precondition(inverse_first, grad_first), precondition(inverse_first, carried)]
    )
    mobile = jnp.stack([mobility[1], mobility[0], mobility[0]])
    block = jnp.stack([acc_block[1], acc_block[0], acc_block[0]])
    images = operator(fields, mobile, block)
    image_last, direct, coupled = images[0], images[1], images[2]
    first_sums = global_sum(
        stacked_sums(
            [
                (grad_last, image_last),
                (image_last, image_last),
                (grad_first, direct),
                (grad_first, coupled),
                (carried, direct),
                (carried, coupled),
                (direct, direct),
                (direct, coupled),
                (coupled, coupled),
            ]
        )
    )
    lanes = lax.optimization_barrier(
        jnp.broadcast_to(first_sums[:, None], (first_sums.shape[0], column_count))
    )
    (
        along_last,
        energy_last,
        grad_direct,
        grad_coupled,
        carried_direct,
        carried_coupled,
        direct_direct,
        direct_coupled,
        coupled_coupled,
    ) = [lanes[i] for i in range(first_sums.shape[0])]
    alpha_last = along_last / energy_last
    along_first = grad_direct + alpha_last * (grad_coupled + carried_direct) + (
        alpha_last * alpha_last
    ) * carried_coupled
    energy_first = direct_direct + (2.0 * alpha_last) * direct_coupled + (
        alpha_last * alpha_last
    ) * coupled_coupled
    alpha_first = along_first / energy_first
    solution_last = alpha_last * z_last
    residual_last = grad_last - alpha_last * image_last
    residual_first = grad_first + store[0] * solution_last
    solution_first = alpha_first * precondition(inverse_first, residual_first)
    image_first = direct + alpha_last * coupled
    closing_first = residual_first - alpha_first * image_first
    second_sums = global_sum(
        stacked_sums(
            [
                (residual_first, residual_first),
                (closing_first, closing_first),
                (grad_last, grad_last),
                (residual_last, residual_last),
            ]
        )
    )
    norms = jnp.sqrt(second_sums).reshape(2, 2)
    return (jnp.stack([solution_first, solution_last]), norms)


def solution(mesh):
    placed = (
        P(None, None, "slab", "cells"),
        P(None, None, "slab", "cells"),
        P(None, None, "slab", "cells"),
        P(None, None, "slab", "cells"),
        P("slab", "cells"),
        P("slab", "cells"),
        P("slab", "cells"),
        P("slab", "cells"),
        P("slab", "cells"),
        P("slab", "cells"),
        P("slab", "cells"),
        P("slab", "cells"),
        P("slab", "cells"),
    )
    return jax.shard_map(
        per_device,
        mesh=mesh,
        in_specs=placed,
        out_specs=(P(None, None, "slab", "cells"), P()),
        check_vma=False,
    )
```

```python
import jax
import jax.numpy as jnp
from jax import lax
from jax.sharding import PartitionSpec as P

WELLS = 16
NSTEPS = 2


def shifted(value, axis, by):
    length = lax.axis_size(axis)
    pairs = [(i, i + by) for i in range(length) if 0 <= i + by < length]
    return lax.ppermute(value, axis, pairs)


def stacked_sums(pairs):
    partial = jnp.stack([jnp.sum(left * right, axis=-2) for left, right in pairs])
    return jnp.sum(partial.reshape(len(pairs), -1), axis=1)


def butterfly(value, axis):
    count = lax.axis_size(axis)
    if count & (count - 1):
        return lax.psum(value, axis)
    step = 1
    while step < count:
        value = value + lax.ppermute(value, axis, [(i, i ^ step) for i in range(count)])
        step *= 2
    return value


def global_sum(values):
    axes = ("cells", "slab")
    count = lax.axis_size("cells") * lax.axis_size("slab")
    copies = jnp.broadcast_to(values[None], (count,) + values.shape)
    gathered = lax.all_to_all(copies, axes, 0, 0, tiled=True)
    return jnp.sum(gathered, axis=0)


def split3(value):
    high = value.astype(jnp.bfloat16)
    rest = value - high.astype(value.dtype)
    middle = rest.astype(jnp.bfloat16)
    low = (rest - middle.astype(value.dtype)).astype(jnp.bfloat16)
    return high, middle, low


def split2(value):
    high = value.astype(jnp.bfloat16)
    low = (value - high.astype(value.dtype)).astype(jnp.bfloat16)
    return high, low


def onehot_dot(value, onehot, dims, split=split3):
    rows = value.shape[0]
    parts = split(value)
    pieces = jnp.concatenate(parts, axis=0)
    part = lax.dot_general(
        pieces, onehot, (dims, ((), ())), preferred_element_type=jnp.float32
    )
    total = part[:rows]
    for index in range(1, len(parts)):
        total = total + part[index * rows : (index + 1) * rows]
    return total


def per_device(
    grad,
    acc_block,
    mobility,
    store,
    trans_h,
    trans_v,
    fault_near,
    fault_far,
    fault_trans,
    fault_count,
    compl_cell,
    compl_well,
    compl_wi,
):
    highest = lax.Precision.HIGHEST
    layer_count, column_count = trans_h.shape
    cells_size = lax.axis_size("cells")
    slab_size = lax.axis_size("slab")
    cells_place = lax.axis_index("cells")
    slab_place = lax.axis_index("slab")
    column_ids = lax.broadcasted_iota(jnp.int32, (layer_count, column_count), 1)
    layer_ids = lax.broadcasted_iota(jnp.int32, (layer_count, column_count), 0)
    zero_value = jnp.zeros((), trans_h.dtype)
    trans_east = jnp.where(
        (cells_place == cells_size - 1) & (column_ids == column_count - 1), zero_value, trans_h
    )
    trans_down = jnp.where(
        (slab_place == slab_size - 1) & (layer_ids == layer_count - 1), zero_value, trans_v
    )
    slot_count = fault_near.size
    slot_live = (jnp.arange(slot_count, dtype=jnp.int32) < fault_count.reshape(())) & (
        cells_place < cells_size - 1
    )
    weight_here = jnp.where(slot_live, fault_trans.reshape(-1), zero_value)
    from_left_setup = shifted(jnp.concatenate([trans_east[:, -1], weight_here]), "cells", 1)
    east_edge = from_left_setup[:layer_count]
    weight_left = from_left_setup[layer_count:]
    down_edge = shifted(trans_down[-1, :], "slab", 1)
    trans_west = jnp.concatenate([east_edge[:, None], trans_east[:, :-1]], axis=1)
    trans_up = jnp.concatenate([down_edge[None, :], trans_down[:-1, :]], axis=0)
    face_total = trans_east + trans_west + trans_down + trans_up

    column_iota = jnp.arange(column_count, dtype=jnp.int32)
    layer_iota = jnp.arange(layer_count, dtype=jnp.int32)

    def locate(cells):
        cells = cells.reshape(-1)
        onehot = (cells % column_count)[:, None] == column_iota[None, :]
        rows = (layer_iota[:, None] == (cells // column_count)[None, :]).astype(jnp.float32)
        return onehot.astype(jnp.float8_e4m3fn), rows

    def gather(field, where, split=split3):
        onehot, rows = where
        parts = field.shape[0]
        flat = field.reshape(parts * layer_count, column_count)
        picked = onehot_dot(flat, onehot, ((1,), (1,)), split)
        picked = picked.reshape(parts, layer_count, -1) * rows[None]
        return jnp.sum(picked, axis=1)

    def scatter(values, where, split=split3):
        onehot, rows = where
        parts = values.shape[0]
        spread = (values[:, None, :] * rows[None]).reshape(parts * layer_count, -1)
        placed = onehot_dot(spread, onehot, ((1,), (0,)), split)
        return placed.reshape(parts, layer_count, column_count)

    edge_cells = jnp.concatenate(
        [layer_iota * column_count, layer_iota * column_count + (column_count - 1)]
    )
    fault_at = locate(
        jnp.concatenate([fault_near.reshape(-1), fault_far.reshape(-1), edge_cells])
    )
    west_face = east_edge
    east_face = trans_east[:, -1]
    well_at = locate(compl_cell)
    well_index = compl_wi.reshape(-1)
    well_onehot = (
        compl_well.reshape(-1)[:, None] == jnp.arange(WELLS, dtype=jnp.int32)[None, :]
    ).astype(trans_h.dtype)

    def inverse_of(newton):
        block = acc_block[newton]
        mobile = mobility[newton]
        diag_first = block[0] + mobile[0] * face_total
        diag_second = block[3] + mobile[1] * face_total
        determinant = diag_first * diag_second - block[1] * block[2]
        scale = 1.0 / determinant
        return (
            diag_second * scale,
            -block[1] * scale,
            -block[2] * scale,
            diag_first * scale,
        )

    def precondition(inverse, residual):
        inverse_aa, inverse_ab, inverse_ba, inverse_bb = inverse
        return jnp.stack(
            [
                inverse_aa * residual[0] + inverse_ab * residual[1],
                inverse_ba * residual[0] + inverse_bb * residual[1],
            ]
        )

    def slab_shift(value, by):
        count = lax.axis_size("slab")
        return lax.ppermute(value, "slab", [(i, (i + by) % count) for i in range(count)])

    def operator(fields, mobile, block):
        count = fields.shape[0]
        scaled = (mobile * fields).reshape(count * 2, layer_count, column_count)
        picks = gather(scaled, fault_at, split2)
        picks_near = picks[:, :slot_count]
        picks_far = picks[:, slot_count : 2 * slot_count]
        from_left = shifted(jnp.concatenate([scaled[:, :, -1], picks_near], axis=1), "cells", 1)
        from_right = shifted(jnp.concatenate([scaled[:, :, 0], picks_far], axis=1), "cells", -1)
        pressure = fields[:, 0]
        values = gather(pressure, well_at, split2)
        local = jnp.concatenate(
            [
                jnp.dot(well_index, well_onehot, precision=highest)[None],
                jnp.dot(well_index * values, well_onehot, precision=highest),
            ]
        )
        halo_rows = count * 2
        wells = local.shape[1]
        lanes = -(-wells // column_count) * column_count
        well_block = jnp.pad(local, ((0, 0), (0, lanes - wells))).reshape(-1, column_count)
        from_above = slab_shift(jnp.concatenate([scaled[:, -1, :], well_block]), 1)
        from_below = slab_shift(jnp.concatenate([scaled[:, 0, :], well_block]), -1)

        def wells_of(message):
            return message[halo_rows:].reshape(local.shape[0], lanes)[:, :wells]

        summed = local
        if slab_size > 1:
            summed = summed + wells_of(from_above)
        if slab_size > 2:
            summed = summed + wells_of(from_below)
        for by in range(2, slab_size - 1):
            summed = summed + slab_shift(local, by)
        from_above = from_above[:halo_rows]
        from_below = from_below[:halo_rows]
        zero_column = jnp.zeros_like(scaled[:, :, :1])
        west = jnp.concatenate([zero_column, scaled[:, :, :-1]], axis=2)
        east = jnp.concatenate([scaled[:, :, 1:], zero_column], axis=2)
        above = jnp.where(
            layer_ids == 0,
            from_above[:, None, :],
            jnp.pad(scaled[:, :-1, :], ((0, 0), (1, 0), (0, 0))),
        )
        below = jnp.where(
            layer_ids == layer_count - 1,
            from_below[:, None, :],
            jnp.pad(scaled[:, 1:, :], ((0, 0), (0, 1), (0, 0))),
        )
        laplace = (
            trans_east * (scaled - east)
            + trans_west * (scaled - west)
            + trans_down * (scaled - below)
            + trans_up * (scaled - above)
        )
        flux_right = weight_here * (picks_near - from_right[:, layer_count:])
        flux_left = weight_left * (from_left[:, layer_count:] - picks_far)
        fault_term = scatter(
            jnp.concatenate(
                [
                    flux_right,
                    -flux_left,
                    -west_face * from_left[:, :layer_count],
                    -east_face * from_right[:, :layer_count],
                ],
                axis=1,
            ),
            fault_at,
            split2,
        )
        laplace = (laplace + fault_term).reshape(count, 2, layer_count, column_count)
        back = jnp.dot(summed[1:] / summed[0], well_onehot.T, precision=highest)
        well_term = scatter(well_index * (values - back), well_at)
        first = (
            block[:, 0] * fields[:, 0]
            + block[:, 1] * fields[:, 1]
            + laplace[:, 0]
            + well_term
        )
        second = block[:, 2] * fields[:, 0] + block[:, 3] * fields[:, 1] + laplace[:, 1]
        return jnp.stack([first, second], axis=1)

    inverse_last = inverse_of(1)
    inverse_first = inverse_of(0)
    grad_last = grad[1]
    grad_first = grad[0]
    z_last = precondition(inverse_last, grad_last)
    carried = store[0] * z_last
    fields = jnp.stack(
        [z_last, precondition(inverse_first, grad_first), precondition(inverse_first, carried)]
    )
    mobile = jnp.stack([mobility[1], mobility[0], mobility[0]])
    block = jnp.stack([acc_block[1], acc_block[0], acc_block[0]])
    images = operator(fields, mobile, block)
    image_last, direct, coupled = images[0], images[1], images[2]
    first_sums = global_sum(
        stacked_sums(
            [
                (grad_last, image_last),
                (image_last, image_last),
                (grad_last, grad_last),
                (grad_first, direct),
                (grad_first, coupled),
                (carried, direct),
                (carried, coupled),
                (direct, direct),
                (direct, coupled),
                (coupled, coupled),
            ]
        )
    )
    lanes = lax.optimization_barrier(
        jnp.broadcast_to(first_sums[:, None], (first_sums.shape[0], column_count))
    )
    (
        along_last,
        energy_last,
        norm_last,
        grad_direct,
        grad_coupled,
        carried_direct,
        carried_coupled,
        direct_direct,
        direct_coupled,
        coupled_coupled,
    ) = [lanes[i] for i in range(first_sums.shape[0])]
    alpha_last = along_last / energy_last
    along_first = grad_direct + alpha_last * (grad_coupled + carried_direct) + (
        alpha_last * alpha_last
    ) * carried_coupled
    energy_first = direct_direct + (2.0 * alpha_last) * direct_coupled + (
        alpha_last * alpha_last
    ) * coupled_coupled
    alpha_first = along_first / energy_first
    solution_last = alpha_last * z_last
    residual_last = grad_last - alpha_last * image_last
    residual_first = grad_first + store[0] * solution_last
    solution_first = alpha_first * precondition(inverse_first, residual_first)
    image_first = direct + alpha_last * coupled
    closing_first = residual_first - alpha_first * image_first
    second_sums = global_sum(
        stacked_sums(
            [
                (residual_first, residual_first),
                (closing_first, closing_first),
                (grad_last, grad_last),
                (residual_last, residual_last),
            ]
        )
    )
    norms = jnp.sqrt(second_sums).reshape(2, 2)
    return (jnp.stack([solution_first, solution_last]), norms)


def solution(mesh):
    placed = (
        P(None, None, "slab", "cells"),
        P(None, None, "slab", "cells"),
        P(None, None, "slab", "cells"),
        P(None, None, "slab", "cells"),
        P("slab", "cells"),
        P("slab", "cells"),
        P("slab", "cells"),
        P("slab", "cells"),
        P("slab", "cells"),
        P("slab", "cells"),
        P("slab", "cells"),
        P("slab", "cells"),
        P("slab", "cells"),
    )
    return jax.shard_map(
        per_device,
        mesh=mesh,
        in_specs=placed,
        out_specs=(P(None, None, "slab", "cells"), P()),
        check_vma=False,
    )
```

```python
import jax
import jax.numpy as jnp
from jax import lax
from jax.sharding import PartitionSpec as P

WELLS = 16
NSTEPS = 2


def shifted(value, axis, by):
    length = lax.axis_size(axis)
    pairs = [(i, i + by) for i in range(length) if 0 <= i + by < length]
    return lax.ppermute(value, axis, pairs)


def stacked_sums(pairs):
    partial = jnp.stack([jnp.sum(left * right, axis=-2) for left, right in pairs])
    return jnp.sum(partial.reshape(len(pairs), -1), axis=1)


def butterfly(value, axis):
    count = lax.axis_size(axis)
    if count & (count - 1):
        return lax.psum(value, axis)
    step = 1
    while step < count:
        value = value + lax.ppermute(value, axis, [(i, i ^ step) for i in range(count)])
        step *= 2
    return value


def global_sum(values):
    axes = ("cells", "slab")
    count = lax.axis_size("cells") * lax.axis_size("slab")
    copies = jnp.broadcast_to(values[None], (count,) + values.shape)
    gathered = lax.all_to_all(copies, axes, 0, 0, tiled=True)
    return jnp.sum(gathered, axis=0)


def split3(value):
    high = value.astype(jnp.bfloat16)
    rest = value - high.astype(value.dtype)
    middle = rest.astype(jnp.bfloat16)
    low = (rest - middle.astype(value.dtype)).astype(jnp.bfloat16)
    return high, middle, low


def split2(value):
    high = value.astype(jnp.bfloat16)
    low = (value - high.astype(value.dtype)).astype(jnp.bfloat16)
    return high, low


def onehot_dot(value, onehot, dims, split=split3):
    rows = value.shape[0]
    parts = split(value)
    pieces = jnp.concatenate(parts, axis=0)
    part = lax.dot_general(
        pieces, onehot, (dims, ((), ())), preferred_element_type=jnp.float32
    )
    total = part[:rows]
    for index in range(1, len(parts)):
        total = total + part[index * rows : (index + 1) * rows]
    return total


def per_device(
    grad,
    acc_block,
    mobility,
    store,
    trans_h,
    trans_v,
    fault_near,
    fault_far,
    fault_trans,
    fault_count,
    compl_cell,
    compl_well,
    compl_wi,
):
    highest = lax.Precision.HIGHEST
    layer_count, column_count = trans_h.shape
    cells_size = lax.axis_size("cells")
    slab_size = lax.axis_size("slab")
    cells_place = lax.axis_index("cells")
    slab_place = lax.axis_index("slab")
    column_ids = lax.broadcasted_iota(jnp.int32, (layer_count, column_count), 1)
    layer_ids = lax.broadcasted_iota(jnp.int32, (layer_count, column_count), 0)
    zero_value = jnp.zeros((), trans_h.dtype)
    trans_east = jnp.where(
        (cells_place == cells_size - 1) & (column_ids == column_count - 1), zero_value, trans_h
    )
    trans_down = jnp.where(
        (slab_place == slab_size - 1) & (layer_ids == layer_count - 1), zero_value, trans_v
    )
    slot_count = fault_near.size
    slot_live = (jnp.arange(slot_count, dtype=jnp.int32) < fault_count.reshape(())) & (
        cells_place < cells_size - 1
    )
    weight_here = jnp.where(slot_live, fault_trans.reshape(-1), zero_value)
    from_left_setup = shifted(jnp.concatenate([weight_here, trans_east[:, -1]]), "cells", 1)
    weight_left = from_left_setup[:slot_count]
    east_edge = from_left_setup[slot_count:]
    down_edge = shifted(trans_down[-1, :], "slab", 1)
    trans_west = jnp.concatenate([east_edge[:, None], trans_east[:, :-1]], axis=1)
    trans_up = jnp.concatenate([down_edge[None, :], trans_down[:-1, :]], axis=0)
    face_total = trans_east + trans_west + trans_down + trans_up

    column_iota = jnp.arange(column_count, dtype=jnp.int32)
    layer_iota = jnp.arange(layer_count, dtype=jnp.int32)

    def locate(cells):
        cells = cells.reshape(-1)
        onehot = (cells % column_count)[:, None] == column_iota[None, :]
        rows = (layer_iota[:, None] == (cells // column_count)[None, :]).astype(jnp.float32)
        return onehot.astype(jnp.float8_e4m3fn), rows

    def gather(field, where, split=split3):
        onehot, rows = where
        parts = field.shape[0]
        flat = field.reshape(parts * layer_count, column_count)
        picked = onehot_dot(flat, onehot, ((1,), (1,)), split)
        picked = picked.reshape(parts, layer_count, -1) * rows[None]
        return jnp.sum(picked, axis=1)

    def scatter(values, where, split=split3):
        onehot, rows = where
        parts = values.shape[0]
        spread = (values[:, None, :] * rows[None]).reshape(parts * layer_count, -1)
        placed = onehot_dot(spread, onehot, ((1,), (0,)), split)
        return placed.reshape(parts, layer_count, column_count)

    edge_cells = jnp.concatenate(
        [layer_iota * column_count, layer_iota * column_count + (column_count - 1)]
    )
    fault_at = locate(
        jnp.concatenate([fault_near.reshape(-1), fault_far.reshape(-1), edge_cells])
    )
    west_face = east_edge
    east_face = trans_east[:, -1]
    well_at = locate(compl_cell)
    well_index = compl_wi.reshape(-1)
    well_onehot = (
        compl_well.reshape(-1)[:, None] == jnp.arange(WELLS, dtype=jnp.int32)[None, :]
    ).astype(trans_h.dtype)

    def inverse_of(newton):
        block = acc_block[newton]
        mobile = mobility[newton]
        diag_first = block[0] + mobile[0] * face_total
        diag_second = block[3] + mobile[1] * face_total
        determinant = diag_first * diag_second - block[1] * block[2]
        scale = 1.0 / determinant
        return (
            diag_second * scale,
            -block[1] * scale,
            -block[2] * scale,
            diag_first * scale,
        )

    def precondition(inverse, residual):
        inverse_aa, inverse_ab, inverse_ba, inverse_bb = inverse
        return jnp.stack(
            [
                inverse_aa * residual[0] + inverse_ab * residual[1],
                inverse_ba * residual[0] + inverse_bb * residual[1],
            ]
        )

    def slab_shift(value, by):
        count = lax.axis_size("slab")
        return lax.ppermute(value, "slab", [(i, (i + by) % count) for i in range(count)])

    def operator(fields, mobile, block):
        count = fields.shape[0]
        scaled = (mobile * fields).reshape(count * 2, layer_count, column_count)
        picks = gather(scaled, fault_at, split2)
        picks_near = picks[:, :slot_count]
        picks_far = picks[:, slot_count : 2 * slot_count]
        from_left = shifted(jnp.concatenate([scaled[:, :, -1], picks_near], axis=1), "cells", 1)
        from_right = shifted(jnp.concatenate([scaled[:, :, 0], picks_far], axis=1), "cells", -1)
        pressure = fields[:, 0]
        values = gather(pressure, well_at)
        local = jnp.concatenate(
            [
                jnp.dot(well_index, well_onehot, precision=highest)[None],
                jnp.dot(well_index * values, well_onehot, precision=highest),
            ]
        )
        halo_rows = count * 2
        wells = local.shape[1]
        lanes = -(-wells // column_count) * column_count
        well_block = jnp.pad(local, ((0, 0), (0, lanes - wells))).reshape(-1, column_count)
        from_above = slab_shift(jnp.concatenate([scaled[:, -1, :], well_block]), 1)
        from_below = slab_shift(jnp.concatenate([scaled[:, 0, :], well_block]), -1)

        def wells_of(message):
            return message[halo_rows:].reshape(local.shape[0], lanes)[:, :wells]

        summed = local
        if slab_size > 1:
            summed = summed + wells_of(from_above)
        if slab_size > 2:
            summed = summed + wells_of(from_below)
        for by in range(2, slab_size - 1):
            summed = summed + slab_shift(local, by)
        from_above = from_above[:halo_rows]
        from_below = from_below[:halo_rows]
        zero_column = jnp.zeros_like(scaled[:, :, :1])
        west = jnp.concatenate([zero_column, scaled[:, :, :-1]], axis=2)
        east = jnp.concatenate([scaled[:, :, 1:], zero_column], axis=2)
        above = jnp.where(
            layer_ids == 0,
            from_above[:, None, :],
            jnp.pad(scaled[:, :-1, :], ((0, 0), (1, 0), (0, 0))),
        )
        below = jnp.where(
            layer_ids == layer_count - 1,
            from_below[:, None, :],
            jnp.pad(scaled[:, 1:, :], ((0, 0), (0, 1), (0, 0))),
        )
        laplace = (
            trans_east * (scaled - east)
            + trans_west * (scaled - west)
            + trans_down * (scaled - below)
            + trans_up * (scaled - above)
        )
        flux_right = weight_here * (picks_near - from_right[:, layer_count:])
        flux_left = weight_left * (from_left[:, layer_count:] - picks_far)
        fault_term = scatter(
            jnp.concatenate(
                [
                    flux_right,
                    -flux_left,
                    -west_face * from_left[:, :layer_count],
                    -east_face * from_right[:, :layer_count],
                ],
                axis=1,
            ),
            fault_at,
            split2,
        )
        laplace = (laplace + fault_term).reshape(count, 2, layer_count, column_count)
        back = jnp.dot(summed[1:] / summed[0], well_onehot.T, precision=highest)
        well_term = scatter(well_index * (values - back), well_at)
        first = (
            block[:, 0] * fields[:, 0]
            + block[:, 1] * fields[:, 1]
            + laplace[:, 0]
            + well_term
        )
        second = block[:, 2] * fields[:, 0] + block[:, 3] * fields[:, 1] + laplace[:, 1]
        return jnp.stack([first, second], axis=1)

    inverse_last = inverse_of(1)
    inverse_first = inverse_of(0)
    grad_last = grad[1]
    grad_first = grad[0]
    z_last = precondition(inverse_last, grad_last)
    carried = store[0] * z_last
    fields = jnp.stack(
        [z_last, precondition(inverse_first, grad_first), precondition(inverse_first, carried)]
    )
    mobile = jnp.stack([mobility[1], mobility[0], mobility[0]])
    block = jnp.stack([acc_block[1], acc_block[0], acc_block[0]])
    images = operator(fields, mobile, block)
    image_last, direct, coupled = images[0], images[1], images[2]
    first_sums = global_sum(
        stacked_sums(
            [
                (grad_last, image_last),
                (image_last, image_last),
                (grad_last, grad_last),
                (grad_first, direct),
                (grad_first, coupled),
                (carried, direct),
                (carried, coupled),
                (direct, direct),
                (direct, coupled),
                (coupled, coupled),
            ]
        )
    )
    lanes = lax.optimization_barrier(
        jnp.broadcast_to(first_sums[:, None], (first_sums.shape[0], column_count))
    )
    (
        along_last,
        energy_last,
        norm_last,
        grad_direct,
        grad_coupled,
        carried_direct,
        carried_coupled,
        direct_direct,
        direct_coupled,
        coupled_coupled,
    ) = [lanes[i] for i in range(first_sums.shape[0])]
    alpha_last = along_last / energy_last
    along_first = grad_direct + alpha_last * (grad_coupled + carried_direct) + (
        alpha_last * alpha_last
    ) * carried_coupled
    energy_first = direct_direct + (2.0 * alpha_last) * direct_coupled + (
        alpha_last * alpha_last
    ) * coupled_coupled
    alpha_first = along_first / energy_first
    solution_last = alpha_last * z_last
    residual_last = grad_last - alpha_last * image_last
    residual_first = grad_first + store[0] * solution_last
    solution_first = alpha_first * precondition(inverse_first, residual_first)
    image_first = direct + alpha_last * coupled
    closing_first = residual_first - alpha_first * image_first
    second_sums = global_sum(
        stacked_sums(
            [
                (residual_first, residual_first),
                (closing_first, closing_first),
                (grad_last, grad_last),
                (residual_last, residual_last),
            ]
        )
    )
    norms = jnp.sqrt(second_sums).reshape(2, 2)
    return (jnp.stack([solution_first, solution_last]), norms)


def solution(mesh):
    placed = (
        P(None, None, "slab", "cells"),
        P(None, None, "slab", "cells"),
        P(None, None, "slab", "cells"),
        P(None, None, "slab", "cells"),
        P("slab", "cells"),
        P("slab", "cells"),
        P("slab", "cells"),
        P("slab", "cells"),
        P("slab", "cells"),
        P("slab", "cells"),
        P("slab", "cells"),
        P("slab", "cells"),
        P("slab", "cells"),
    )
    return jax.shard_map(
        per_device,
        mesh=mesh,
        in_specs=placed,
        out_specs=(P(None, None, "slab", "cells"), P()),
        check_vma=False,
    )
```

```python
import jax
import jax.numpy as jnp
from jax import lax
from jax.sharding import PartitionSpec as P

WELLS = 16
NSTEPS = 2


def shifted(value, axis, by):
    length = lax.axis_size(axis)
    pairs = [(i, i + by) for i in range(length) if 0 <= i + by < length]
    return lax.ppermute(value, axis, pairs)


def stacked_sums(pairs):
    partial = jnp.stack([jnp.sum(left * right, axis=-2) for left, right in pairs])
    return jnp.sum(partial.reshape(len(pairs), -1), axis=1)


def butterfly(value, axis):
    count = lax.axis_size(axis)
    if count & (count - 1):
        return lax.psum(value, axis)
    step = 1
    while step < count:
        value = value + lax.ppermute(value, axis, [(i, i ^ step) for i in range(count)])
        step *= 2
    return value


def global_sum(values):
    axes = ("cells", "slab")
    count = lax.axis_size("cells") * lax.axis_size("slab")
    copies = jnp.broadcast_to(values[None], (count,) + values.shape)
    gathered = lax.all_to_all(copies, axes, 0, 0, tiled=True)
    return jnp.sum(gathered, axis=0)


def split3(value):
    high = value.astype(jnp.bfloat16)
    rest = value - high.astype(value.dtype)
    middle = rest.astype(jnp.bfloat16)
    low = (rest - middle.astype(value.dtype)).astype(jnp.bfloat16)
    return high, middle, low


def split2(value):
    high = value.astype(jnp.bfloat16)
    low = (value - high.astype(value.dtype)).astype(jnp.bfloat16)
    return high, low


def onehot_dot(value, onehot, dims, split=split3):
    rows = value.shape[0]
    parts = split(value)
    pieces = jnp.concatenate(parts, axis=0)
    part = lax.dot_general(
        pieces, onehot, (dims, ((), ())), preferred_element_type=jnp.float32
    )
    total = part[:rows]
    for index in range(1, len(parts)):
        total = total + part[index * rows : (index + 1) * rows]
    return total


def per_device(
    grad,
    acc_block,
    mobility,
    store,
    trans_h,
    trans_v,
    fault_near,
    fault_far,
    fault_trans,
    fault_count,
    compl_cell,
    compl_well,
    compl_wi,
):
    highest = lax.Precision.HIGHEST
    layer_count, column_count = trans_h.shape
    cells_size = lax.axis_size("cells")
    slab_size = lax.axis_size("slab")
    cells_place = lax.axis_index("cells")
    slab_place = lax.axis_index("slab")
    column_ids = lax.broadcasted_iota(jnp.int32, (layer_count, column_count), 1)
    layer_ids = lax.broadcasted_iota(jnp.int32, (layer_count, column_count), 0)
    zero_value = jnp.zeros((), trans_h.dtype)
    trans_east = jnp.where(
        (cells_place == cells_size - 1) & (column_ids == column_count - 1), zero_value, trans_h
    )
    trans_down = jnp.where(
        (slab_place == slab_size - 1) & (layer_ids == layer_count - 1), zero_value, trans_v
    )
    slot_count = fault_near.size
    slot_live = (jnp.arange(slot_count, dtype=jnp.int32) < fault_count.reshape(())) & (
        cells_place < cells_size - 1
    )
    weight_here = jnp.where(slot_live, fault_trans.reshape(-1), zero_value)
    from_left_setup = shifted(jnp.concatenate([weight_here, trans_east[:, -1]]), "cells", 1)
    weight_left = from_left_setup[:slot_count]
    east_edge = from_left_setup[slot_count:]
    down_edge = shifted(trans_down[-1, :], "slab", 1)
    trans_west = jnp.concatenate([east_edge[:, None], trans_east[:, :-1]], axis=1)
    trans_up = jnp.concatenate([down_edge[None, :], trans_down[:-1, :]], axis=0)
    face_total = trans_east + trans_west + trans_down + trans_up

    column_iota = jnp.arange(column_count, dtype=jnp.int32)
    layer_iota = jnp.arange(layer_count, dtype=jnp.int32)

    def locate(cells):
        cells = cells.reshape(-1)
        onehot = (cells % column_count)[:, None] == column_iota[None, :]
        rows = (layer_iota[:, None] == (cells // column_count)[None, :]).astype(jnp.float32)
        return onehot.astype(jnp.float8_e4m3fn), rows

    def gather(field, where, split=split3):
        onehot, rows = where
        parts = field.shape[0]
        flat = field.reshape(parts * layer_count, column_count)
        picked = onehot_dot(flat, onehot, ((1,), (1,)), split)
        picked = picked.reshape(parts, layer_count, -1) * rows[None]
        return jnp.sum(picked, axis=1)

    def scatter(values, where, split=split3):
        onehot, rows = where
        parts = values.shape[0]
        spread = (values[:, None, :] * rows[None]).reshape(parts * layer_count, -1)
        placed = onehot_dot(spread, onehot, ((1,), (0,)), split)
        return placed.reshape(parts, layer_count, column_count)

    edge_cells = jnp.concatenate(
        [layer_iota * column_count, layer_iota * column_count + (column_count - 1)]
    )
    fault_at = locate(
        jnp.concatenate([fault_near.reshape(-1), fault_far.reshape(-1), edge_cells])
    )
    west_face = east_edge
    east_face = trans_east[:, -1]
    well_at = locate(compl_cell)
    well_index = compl_wi.reshape(-1)
    well_onehot = (
        compl_well.reshape(-1)[:, None] == jnp.arange(WELLS, dtype=jnp.int32)[None, :]
    ).astype(trans_h.dtype)

    def inverse_of(newton):
        block = acc_block[newton]
        mobile = mobility[newton]
        diag_first = block[0] + mobile[0] * face_total
        diag_second = block[3] + mobile[1] * face_total
        determinant = diag_first * diag_second - block[1] * block[2]
        scale = 1.0 / determinant
        return (
            diag_second * scale,
            -block[1] * scale,
            -block[2] * scale,
            diag_first * scale,
        )

    def precondition(inverse, residual):
        inverse_aa, inverse_ab, inverse_ba, inverse_bb = inverse
        return jnp.stack(
            [
                inverse_aa * residual[0] + inverse_ab * residual[1],
                inverse_ba * residual[0] + inverse_bb * residual[1],
            ]
        )

    def slab_shift(value, by):
        count = lax.axis_size("slab")
        return lax.ppermute(value, "slab", [(i, (i + by) % count) for i in range(count)])

    def operator(fields, mobile, block):
        count = fields.shape[0]
        scaled = (mobile * fields).reshape(count * 2, layer_count, column_count)
        picks = gather(scaled, fault_at, split2)
        picks_near = picks[:, :slot_count]
        picks_far = picks[:, slot_count : 2 * slot_count]
        from_left = shifted(jnp.concatenate([picks_near, scaled[:, :, -1]], axis=1), "cells", 1)
        from_right = shifted(jnp.concatenate([picks_far, scaled[:, :, 0]], axis=1), "cells", -1)
        pressure = fields[:, 0]
        values = gather(pressure, well_at)
        local = jnp.concatenate(
            [
                jnp.dot(well_index, well_onehot, precision=highest)[None],
                jnp.dot(well_index * values, well_onehot, precision=highest),
            ]
        )
        halo_rows = count * 2
        wells = local.shape[1]
        lanes = -(-wells // column_count) * column_count
        well_block = jnp.pad(local, ((0, 0), (0, lanes - wells))).reshape(-1, column_count)
        from_above = slab_shift(jnp.concatenate([scaled[:, -1, :], well_block]), 1)
        from_below = slab_shift(jnp.concatenate([scaled[:, 0, :], well_block]), -1)

        def wells_of(message):
            return message[halo_rows:].reshape(local.shape[0], lanes)[:, :wells]

        summed = local
        if slab_size > 1:
            summed = summed + wells_of(from_above)
        if slab_size > 2:
            summed = summed + wells_of(from_below)
        for by in range(2, slab_size - 1):
            summed = summed + slab_shift(local, by)
        from_above = from_above[:halo_rows]
        from_below = from_below[:halo_rows]
        zero_column = jnp.zeros_like(scaled[:, :, :1])
        west = jnp.concatenate([zero_column, scaled[:, :, :-1]], axis=2)
        east = jnp.concatenate([scaled[:, :, 1:], zero_column], axis=2)
        above = jnp.where(
            layer_ids == 0,
            from_above[:, None, :],
            jnp.pad(scaled[:, :-1, :], ((0, 0), (1, 0), (0, 0))),
        )
        below = jnp.where(
            layer_ids == layer_count - 1,
            from_below[:, None, :],
            jnp.pad(scaled[:, 1:, :], ((0, 0), (0, 1), (0, 0))),
        )
        laplace = (
            trans_east * (scaled - east)
            + trans_west * (scaled - west)
            + trans_down * (scaled - below)
            + trans_up * (scaled - above)
        )
        flux_right = weight_here * (picks_near - from_right[:, :slot_count])
        flux_left = weight_left * (from_left[:, :slot_count] - picks_far)
        fault_term = scatter(
            jnp.concatenate(
                [
                    flux_right,
                    -flux_left,
                    -west_face * from_left[:, slot_count:],
                    -east_face * from_right[:, slot_count:],
                ],
                axis=1,
            ),
            fault_at,
            split2,
        )
        laplace = (laplace + fault_term).reshape(count, 2, layer_count, column_count)
        back = jnp.dot(summed[1:] / summed[0], well_onehot.T, precision=highest)
        well_term = scatter(well_index * (values - back), well_at)
        first = (
            block[:, 0] * fields[:, 0]
            + block[:, 1] * fields[:, 1]
            + laplace[:, 0]
            + well_term
        )
        second = block[:, 2] * fields[:, 0] + block[:, 3] * fields[:, 1] + laplace[:, 1]
        return jnp.stack([first, second], axis=1)

    inverse_last = inverse_of(1)
    inverse_first = inverse_of(0)
    grad_last = grad[1]
    grad_first = grad[0]
    z_last = precondition(inverse_last, grad_last)
    carried = store[0] * z_last
    fields = jnp.stack(
        [z_last, precondition(inverse_first, grad_first), precondition(inverse_first, carried)]
    )
    mobile = jnp.stack([mobility[1], mobility[0], mobility[0]])
    block = jnp.stack([acc_block[1], acc_block[0], acc_block[0]])
    images = operator(fields, mobile, block)
    image_last, direct, coupled = images[0], images[1], images[2]
    first_sums = global_sum(
        stacked_sums(
            [
                (grad_last, image_last),
                (image_last, image_last),
                (grad_last, grad_last),
                (grad_first, direct),
                (grad_first, coupled),
                (carried, direct),
                (carried, coupled),
                (direct, direct),
                (direct, coupled),
                (coupled, coupled),
            ]
        )
    )
    lanes = lax.optimization_barrier(
        jnp.broadcast_to(first_sums[:, None], (first_sums.shape[0], column_count))
    )
    (
        along_last,
        energy_last,
        norm_last,
        grad_direct,
        grad_coupled,
        carried_direct,
        carried_coupled,
        direct_direct,
        direct_coupled,
        coupled_coupled,
    ) = [lanes[i] for i in range(first_sums.shape[0])]
    alpha_last = along_last / energy_last
    along_first = grad_direct + alpha_last * (grad_coupled + carried_direct) + (
        alpha_last * alpha_last
    ) * carried_coupled
    energy_first = direct_direct + (2.0 * alpha_last) * direct_coupled + (
        alpha_last * alpha_last
    ) * coupled_coupled
    alpha_first = along_first / energy_first
    solution_last = alpha_last * z_last
    residual_last = grad_last - alpha_last * image_last
    residual_first = grad_first + store[0] * solution_last
    solution_first = alpha_first * precondition(inverse_first, residual_first)
    image_first = direct + alpha_last * coupled
    closing_first = residual_first - alpha_first * image_first
    second_sums = global_sum(
        stacked_sums(
            [
                (residual_first, residual_first),
                (closing_first, closing_first),
                (grad_last, grad_last),
                (residual_last, residual_last),
            ]
        )
    )
    norms = jnp.sqrt(second_sums).reshape(2, 2)
    return (jnp.stack([solution_first, solution_last]), norms)


def solution(mesh):
    placed = (
        P(None, None, "slab", "cells"),
        P(None, None, "slab", "cells"),
        P(None, None, "slab", "cells"),
        P(None, None, "slab", "cells"),
        P("slab", "cells"),
        P("slab", "cells"),
        P("slab", "cells"),
        P("slab", "cells"),
        P("slab", "cells"),
        P("slab", "cells"),
        P("slab", "cells"),
        P("slab", "cells"),
        P("slab", "cells"),
    )
    return jax.shard_map(
        per_device,
        mesh=mesh,
        in_specs=placed,
        out_specs=(P(None, None, "slab", "cells"), P()),
        check_vma=False,
    )
```
